32 devices in a mesh: dp: 4 (over y, x), expert: 8 (over z, core).
Axes of the slice: x: 2, y: 2, z: 4, core: 2. Of those that a mesh axis runs over, the one named last changes fastest.
Arguments:
- hidden: bfloat16 [32, 2048], P(('dp', 'expert')), may hold values from -6 to 6
- attn_gain: float32 [2048], replicated, may hold values from 0.25 to 1.75
- query_weight: bfloat16 [3072, 2048], P('expert'), may hold values from -0.125 to 0.125
- latent_down: bfloat16 [2048, 576], replicated, may hold values from -0.125 to 0.125
- latent_up: bfloat16 [512, 4096], P(None, 'expert'), may hold values from -0.25 to 0.25
- out_weight: bfloat16 [2048, 2048], P('expert'), may hold values from -0.125 to 0.125
- latent_pool: bfloat16 [128, 32, 576], P('dp'), may hold values from -1000 to 1000
- page_table: int32 [32, 16], replicated, may hold values from -1 to 127, as said below
- page_counts: int32 [32], replicated, may hold values from 1 to 16, as said below
- ffn_gain: float32 [2048], replicated, may hold values from 0.25 to 1.75
- expert_ids: int32 [32, 6], replicated, may hold values from 0 to 23, all different within a row; in each aligned block of 32 rows (0 to 31, 32 to 63, ...) at most 16 rows name the same one
- expert_gates: float32 [32, 6], replicated, may hold values from 0.05 to 0.6
- old_place: int32 [8, 4], replicated, may hold values from 0 to 23, as said below
- new_place: int32 [8, 4], replicated, may hold values from 0 to 23, as said below
- expert_gate_up: bfloat16 [32, 2, 1408, 2048], P('expert', None, None, 'dp'), as said below
- expert_down: bfloat16 [32, 1408, 2048], P('expert', None, 'dp'), as said below
- shared_gate_up: bfloat16 [2, 2816, 2048], P(None, None, 'dp'), may hold values from -0.125 to 0.125
- shared_down: bfloat16 [2816, 2048], P(None, 'dp'), may hold values from -0.109375 to 0.109375
Outputs:
- layer_out: bfloat16 [32, 2048], P(('dp', 'expert'))
- moved_gate_up: bfloat16 [32, 2, 1408, 2048], P('expert', None, None, 'dp')
- moved_down: bfloat16 [32, 1408, 2048], P('expert', None, 'dp')
The draws below stay inside these ranges and needn't reach their ends.
Inputs may be any that keep to these rules, and one draw needn't show every extreme that they name: `page_counts`: each request's count of cached pages; exactly one request has 16. `page_table`: row t names page_counts[t] pages of the pool, no page named twice in the table; its other entries are -1. Page p lies on dp index p // 32. `expert_ids`: no expert is named by more than 16 tokens in all; some expert by exactly 16. `old_place`: row i holds the experts of the slots on expert index i, slot s of row i being global slot i * 4 + s; every expert is held by one slot or more. `new_place`: equal to old_place except in exactly one slot of each row, which names another expert. `expert_gate_up`: slots that hold the same expert under old_place hold equal weights. `expert_down`: slots that hold the same expert under old_place hold equal weights.
All inputs are finite; a program needn't handle non-finite values.
Results may differ from the reference program's by a relative error of at most 0.02.
Values may be sent and summed in bfloat16 or wider, within the bound.
No kernel may reach another device: no remote copies, remote signals or barrier semaphores. Data moves between devices by JAX's collectives and lax.ppermute only.
A program may use at most 128 MiB of HBM per device.

```python
import math
import jax
import jax.numpy as jnp
import numpy as np
from jax import lax

D = 2048
HEADS = 16
NOPE = 128
ROPE = 64
VHEAD = 128
LATENT = 512
EXP_FF = 1408
SHARED_FF = 2816
TOP = 6
SLOTS_DEV = 4
PAGE = 32
MAX_PAGES = 16
EXPERTS = 24
SLOTS = 32
REQUESTS = 32
POOL_PAGES = 128
MOST = 16


def placements(key):
    base = jax.random.fold_in(key, 11)
    key_extra, key_order, key_column, key_shift = jax.random.split(base, 4)
    extra = jax.random.randint(key_extra, (SLOTS - EXPERTS,), 0, EXPERTS).astype(jnp.int32)
    listing = jnp.concatenate([jnp.arange(EXPERTS, dtype=jnp.int32), extra])
    row_count = SLOTS // SLOTS_DEV
    old_table = jax.random.permutation(key_order, listing).reshape(row_count, SLOTS_DEV)
    column = jax.random.randint(key_column, (row_count,), 0, SLOTS_DEV).astype(jnp.int32)
    shift_by = jax.random.randint(key_shift, (row_count,), 1, EXPERTS).astype(jnp.int32)
    present = jnp.take_along_axis(old_table, column[:, None], axis=1)[:, 0]
    hit_mask = jnp.arange(SLOTS_DEV, dtype=jnp.int32)[None, :] == column[:, None]
    new_table = jnp.where(hit_mask, ((present + shift_by) % EXPERTS)[:, None], old_table)
    return (old_table.astype(jnp.int32), new_table.astype(jnp.int32))


def page_layout(key):
    base = jax.random.fold_in(key, 23)
    key_rank, key_order = jax.random.split(base, 2)
    ranking = jax.random.permutation(key_rank, REQUESTS).astype(jnp.int32)
    counts = (1 + (MAX_PAGES - 1) // (1 + ranking)).astype(jnp.int32)
    order = jax.random.permutation(key_order, POOL_PAGES).astype(jnp.int32)
    offsets = jnp.cumsum(counts) - counts
    column = jnp.arange(MAX_PAGES, dtype=jnp.int32)
    place = jnp.minimum(offsets[:, None] + column[None, :], POOL_PAGES - 1)
    table = jnp.where(column[None, :] < counts[:, None], order[place], -1)
    return (table.astype(jnp.int32), counts)


def slot_weights(key, salt, shape, fan_in):
    old_table, _ = placements(key)
    slot_experts = old_table.reshape(-1)

    def one_slot(expert):
        slot_key = jax.random.fold_in(jax.random.fold_in(key, salt), expert)
        values = jax.random.normal(slot_key, shape, jnp.float32)
        return values * fan_in ** (-0.5)
    return jax.vmap(one_slot)(slot_experts)


def draw_latent_pool(key, part):
    base = jax.random.fold_in(key, 37)
    key_base, key_noise, key_pick, key_level, key_spot = jax.random.split(base, 5)
    shape = (POOL_PAGES, PAGE, LATENT + ROPE)
    values = jnp.clip(jax.random.normal(key_base, shape, jnp.float32), -4.0, 4.0)
    noise = jnp.clip(jax.random.normal(key_noise, (POOL_PAGES, ROPE), jnp.float32), -4.0, 4.0)
    planted = jax.random.randint(key_pick, (POOL_PAGES,), 0, 6) == 0
    level = jax.random.randint(key_level, (POOL_PAGES,), 0, 3)
    strength = 60.0 * jnp.where(level == 0, 1.0, jnp.where(level == 1, 2.0, 4.0))
    spot = jax.random.randint(key_spot, (POOL_PAGES,), 0, PAGE - 1)
    token = jnp.arange(PAGE)
    rope_values = values[:, :, LATENT:]
    lead_rope = jnp.take_along_axis(rope_values, spot[:, None, None], axis=1)
    strong = strength[:, None, None] * lead_rope
    first_hit = (planted[:, None] & (token[None, :] == spot[:, None]))[:, :, None]
    second_hit = (planted[:, None] & (token[None, :] == spot[:, None] + 1))[:, :, None]
    rope_part = jnp.where(first_hit, strong, jnp.where(second_hit, strong + 3.0 * noise[:, None, :], rope_values))
    return jnp.concatenate([values[:, :, :LATENT], rope_part], axis=2).astype(jnp.bfloat16)


def draw_page_table(key, part):
    return page_layout(key)[0]


def draw_page_counts(key, part):
    return page_layout(key)[1]


def draw_old_place(key, part):
    return placements(key)[0]


def draw_new_place(key, part):
    return placements(key)[1]


def draw_expert_gate_up(key, part):
    return slot_weights(key, 101, (2, EXP_FF, D), D).astype(jnp.bfloat16)


def draw_expert_down(key, part):
    return slot_weights(key, 202, (EXP_FF, D), EXP_FF).astype(jnp.bfloat16)


def block_levels(key, extent, shards, least, largest):
    def one(axis_at, shards_of):
        draws = jax.random.uniform(jax.random.fold_in(jax.random.fold_in(key, 6), axis_at), (shards_of,), jnp.float32, least / len(shards), largest / len(shards))
        return jnp.repeat(jnp.exp(draws), extent[axis_at] // shards_of).reshape((-1,) + (1,) * (len(extent) - axis_at - 1))

    loudness = one(*shards[0])
    for cut in shards[1:]:
        loudness = loudness * one(*cut)
    return loudness


def assign_block(key, own, number, rows, amount, top, bound, skew):
    sequence = jax.random.permutation(key, amount)
    packed, common = shares(amount, rows * top, bound, skew, True), shares(amount, rows * top, bound, skew, False)
    places = jnp.arange(amount)

    def named(tallies, offset_by):
        used = int((tallies > 0).sum())
        fixed = max(1, used // 4)
        passed = fixed + (places - fixed + offset_by * (used - fixed)) % max(1, amount - fixed)
        return jnp.zeros((amount,), jnp.int32).at[sequence[jnp.where(places < fixed, places, passed)]].set(jnp.asarray(tallies, jnp.int32))

    tallies = jnp.where(number % 4 == 0, named(packed, number // 4), named(common, number - number // 4 - 1))
    mixed = jax.random.permutation(jax.random.fold_in(own, 3), amount)
    giver, receiver = mixed[0:amount // 2 * 2:2], mixed[1:amount // 2 * 2:2]
    margin = jnp.minimum(tallies[giver] - 1, bound - tallies[receiver]) // 2
    margin = jnp.where((giver == sequence[0]) | (receiver == sequence[0]) | (tallies[receiver] == 0), 0, jnp.maximum(margin, 0))
    passed = jax.random.randint(jax.random.fold_in(own, 4), (amount // 2,), 0, 1 << 20) % (margin + 1)
    tallies = tallies.at[giver].add(-passed).at[receiver].add(passed)
    items = jnp.searchsorted(jnp.cumsum(tallies), jnp.arange(rows * top), side="right").astype(jnp.int32)
    grid = items.reshape(top, rows).T
    grid = grid[jax.random.permutation(jax.random.fold_in(own, 1), rows)]
    offset_by = jax.random.randint(jax.random.fold_in(own, 2), (rows, 1), 0, top)
    return jnp.take_along_axis(grid, (jnp.arange(top)[None, :] + offset_by) % top, axis=1)


def shares(amount, total, bound, lean, full):
    weights = [(1 << 20) // math.isqrt(standing ** lean) + 1 for standing in range(1, amount + 1)]
    largest = bound if full else min(bound, max(-(-total // amount), total * weights[0] // sum(weights)))
    least = 1 if total - largest >= amount - 1 else 0
    holding, spare = [largest] + [least] * (amount - 1), total - largest - least * (amount - 1)
    while spare > 0:
        candidates = [i for i in range(1, amount) if holding[i] < largest] or [i for i in range(1, amount) if holding[i] < bound]
        whole, budget = sum([weights[i] for i in candidates]), spare
        for i in candidates:
            more = min(bound - holding[i], max(1, budget * weights[i] // whole), spare)
            holding[i] = holding[i] + more
            spare = spare - more
    return np.array(holding)


def gaussian(rng, dims, spread, limit, cuts=(), kind=jnp.bfloat16):
    values = jax.random.normal(rng, dims, jnp.float32) * spread
    if len(cuts) > 0:
        values = block_levels(rng, dims, cuts, -0.22, 0.18) * values
    return jnp.clip(values, min=-limit, max=limit).astype(kind)


def setup_inputs(seed: int = 0) -> dict:
    splits = jax.random.split(jax.random.key(seed), 19)
    hidden = gaussian(splits[0], (REQUESTS, D), 1.0, 6.0, ((0, 32),))
    attn_gain = jnp.clip(1.0 + 0.15 * jax.random.normal(splits[1], (D,), jnp.float32), 0.25, 1.75)
    query_weight = gaussian(splits[2], (HEADS * (NOPE + ROPE), D), D ** -0.5, 0.125, ((0, 8),))
    latent_down = gaussian(splits[3], (D, LATENT + ROPE), D ** -0.5, 0.125)
    latent_up = gaussian(splits[4], (LATENT, HEADS * (NOPE + VHEAD)), LATENT ** -0.5, 0.25, ((1, 8),))
    out_weight = gaussian(splits[5], (HEADS * VHEAD, D), (HEADS * VHEAD) ** -0.5, 0.125, ((0, 8),))
    latent_pool = draw_latent_pool(jax.random.fold_in(splits[18], 71), 0)
    page_table = draw_page_table(jax.random.fold_in(splits[18], 71), 0)
    page_counts = draw_page_counts(jax.random.fold_in(splits[18], 71), 0)
    ffn_gain = jnp.clip(1.0 + 0.15 * jax.random.normal(splits[9], (D,), jnp.float32), 0.25, 1.75)
    expert_ids_keys = jax.random.split(jax.random.fold_in(splits[10], 1), REQUESTS // REQUESTS)
    expert_ids_turns = jax.random.permutation(jax.random.fold_in(splits[10], 3), REQUESTS // REQUESTS)
    expert_ids = jax.vmap(lambda own, number: assign_block(jax.random.fold_in(splits[10], 2), own, number, REQUESTS, EXPERTS, TOP, MOST, 2))(expert_ids_keys, expert_ids_turns).reshape((REQUESTS, TOP))
    expert_gates = jnp.clip(jax.random.uniform(splits[11], (REQUESTS, TOP), jnp.float32, 0.05, 0.6), 0.05, 0.6)
    old_place = draw_old_place(jax.random.fold_in(splits[18], 71), 0)
    new_place = draw_new_place(jax.random.fold_in(splits[18], 71), 0)
    expert_gate_up = draw_expert_gate_up(jax.random.fold_in(splits[18], 71), 0)
    expert_down = draw_expert_down(jax.random.fold_in(splits[18], 71), 0)
    shared_gate_up = gaussian(splits[16], (2, SHARED_FF, D), D ** -0.5, 0.125, ((2, 4),))
    shared_down = gaussian(splits[17], (SHARED_FF, D), SHARED_FF ** -0.5, 0.109375, ((1, 4),))
    return {"hidden": hidden, "attn_gain": attn_gain, "query_weight": query_weight, "latent_down": latent_down, "latent_up": latent_up, "out_weight": out_weight, "latent_pool": latent_pool, "page_table": page_table, "page_counts": page_counts, "ffn_gain": ffn_gain, "expert_ids": expert_ids, "expert_gates": expert_gates, "old_place": old_place, "new_place": new_place, "expert_gate_up": expert_gate_up, "expert_down": expert_down, "shared_gate_up": shared_gate_up, "shared_down": shared_down}


EPSILON = 1e-06
ROPE_BASE = 50000.0
MASKED_SCORE = -1e+30
HIGHEST = lax.Precision.HIGHEST

def rms_plain(values):
    mean_square = lax.optimization_barrier(jnp.mean(values * values, axis=-1, keepdims=True))
    return values * lax.rsqrt(mean_square + EPSILON)

def rms_norm(values, norm_gain):
    return rms_plain(values) * norm_gain

def rotary(values, position):
    half_width = values.shape[-1] // 2
    exponent = jnp.arange(half_width).astype(jnp.float32) * (2.0 / values.shape[-1])
    frequency = jnp.exp(-exponent * math.log(ROPE_BASE))
    angles = position[..., None] * frequency
    cosine = jnp.cos(angles)
    sine_part = jnp.sin(angles)
    first_half = values[..., :half_width]
    second = values[..., half_width:]
    return jnp.concatenate([first_half * cosine - second * sine_part, second * cosine + first_half * sine_part], axis=-1)

def expert_block(normed, gate_up, down_weight):
    gate_part = jnp.einsum('td,fd->tf', normed, gate_up[0], preferred_element_type=jnp.float32)
    up_part = jnp.einsum('td,fd->tf', normed, gate_up[1], preferred_element_type=jnp.float32)
    activated = (jax.nn.silu(gate_part) * up_part).astype(jnp.bfloat16)
    return jnp.dot(activated, down_weight, preferred_element_type=jnp.float32)

def reference(hidden, attn_gain, query_weight, latent_down, latent_up, out_weight, latent_pool, page_table, page_counts, ffn_gain, expert_ids, expert_gates, old_place, new_place, expert_gate_up, expert_down, shared_gate_up, shared_down):
    stream = hidden.astype(jnp.float32)
    normed = rms_norm(stream, attn_gain).astype(jnp.bfloat16)
    queries = jnp.einsum('td,qd->tq', normed, query_weight, preferred_element_type=jnp.float32).reshape(REQUESTS, HEADS, NOPE + ROPE)
    position = (page_counts * PAGE).astype(jnp.float32)
    query_rope = rotary(queries[..., NOPE:], position[:, None]).astype(jnp.bfloat16)
    up_table = latent_up.astype(jnp.float32).reshape(LATENT, HEADS, NOPE + VHEAD)
    query_latent = jnp.einsum('thn,lhn->thl', queries[..., :NOPE], up_table[..., :NOPE], precision=HIGHEST).astype(jnp.bfloat16)
    fresh_latent = jnp.dot(normed, latent_down, preferred_element_type=jnp.float32)
    new_latent = rms_plain(fresh_latent[:, :LATENT]).astype(jnp.bfloat16)
    new_rope = rotary(fresh_latent[:, LATENT:], position).astype(jnp.bfloat16)
    pages = latent_pool[jnp.maximum(page_table, 0)].astype(jnp.float32)
    valid = jnp.arange(MAX_PAGES)[None, :] < page_counts[:, None]
    score_scale = (NOPE + ROPE) ** (-0.5)
    latent_float = query_latent.astype(jnp.float32)
    rope_float = query_rope.astype(jnp.float32)
    scores = jnp.einsum('thl,tpkl->thpk', latent_float, pages[..., :LATENT], precision=HIGHEST)
    scores = scores + jnp.einsum('thr,tpkr->thpk', rope_float, pages[..., LATENT:], precision=HIGHEST)
    scores = jnp.where(valid[:, None, :, None], scores * score_scale, MASKED_SCORE)
    new_float = new_latent.astype(jnp.float32)
    own_score = jnp.einsum('thl,tl->th', latent_float, new_float, precision=HIGHEST)
    own_score = (own_score + jnp.einsum('thr,tr->th', rope_float, new_rope.astype(jnp.float32), precision=HIGHEST)) * score_scale
    highest = jnp.maximum(lax.optimization_barrier(jnp.max(scores, axis=(2, 3))), own_score)
    weights = jnp.exp(scores - highest[:, :, None, None])
    own_weight = jnp.exp(own_score - highest)
    denominator = lax.optimization_barrier(jnp.sum(weights, axis=(2, 3))) + own_weight
    rounded = lax.optimization_barrier(weights.astype(jnp.bfloat16)).astype(jnp.float32)
    numerator = jnp.einsum('thpk,tpkl->thl', rounded, pages[..., :LATENT], precision=HIGHEST)
    numerator = numerator + own_weight[..., None] * new_float[:, None, :]
    attended = (numerator / denominator[..., None]).astype(jnp.bfloat16)
    heads_out = jnp.einsum('thl,lhv->thv', attended.astype(jnp.float32), up_table[..., NOPE:], precision=HIGHEST)
    heads_out = heads_out.astype(jnp.bfloat16).reshape(REQUESTS, HEADS * VHEAD)
    residual = stream + jnp.dot(heads_out, out_weight, preferred_element_type=jnp.float32)
    normed_ffn = rms_norm(residual, ffn_gain).astype(jnp.bfloat16)
    old_flat = old_place.reshape(-1)
    holder = jnp.argmax(old_flat[None, :] == jnp.arange(EXPERTS).astype(jnp.int32)[:, None], axis=1).astype(jnp.int32)

    def one_expert(running, expert):
        routed = lax.optimization_barrier(jnp.sum(jnp.where(expert_ids == expert, expert_gates, 0.0), axis=1))
        slot_index = holder[expert]
        output = expert_block(normed_ffn, expert_gate_up[slot_index], expert_down[slot_index])
        return (running + routed[:, None] * output, None)
    combined, _ = lax.scan(one_expert, jnp.zeros((REQUESTS, D), jnp.float32), jnp.arange(EXPERTS).astype(jnp.int32))
    combined = combined + expert_block(normed_ffn, shared_gate_up, shared_down)
    layer_out = (residual + combined).astype(jnp.bfloat16)
    new_source = holder[new_place.reshape(-1)]
    return (layer_out, expert_gate_up[new_source], expert_down[new_source])
```

```python
import math

import jax
import jax.numpy as jnp
from jax import lax
from jax.sharding import PartitionSpec as P

NOPE = 128
ROPE = 64
VHEAD = 128
LATENT = 512
EXP_DEV = 3
PAGE = 32


EPSILON = 1e-06
ROPE_BASE = 50000.0
MASKED_SCORE = -1e30
HIGHEST = lax.Precision.HIGHEST


def rms_plain(values):
    mean_square = jnp.mean(values * values, axis=-1, keepdims=True)
    return values * lax.rsqrt(mean_square + EPSILON)


def rms_norm(values, norm_gain):
    return rms_plain(values) * norm_gain


def rotary(values, position):
    half_width = values.shape[-1] // 2
    exponent = jnp.arange(half_width).astype(jnp.float32) * (2.0 / values.shape[-1])
    frequency = jnp.exp(-exponent * math.log(ROPE_BASE))
    angles = position[..., None] * frequency
    cosine = jnp.cos(angles)
    sine_part = jnp.sin(angles)
    first_half = values[..., :half_width]
    second = values[..., half_width:]
    return jnp.concatenate(
        [first_half * cosine - second * sine_part, second * cosine + first_half * sine_part],
        axis=-1,
    )


def gather_rows(rows):
    by_expert = lax.all_gather(rows, "expert", axis=0, tiled=True)
    return lax.all_gather(by_expert, "dp", axis=0, tiled=True)


def spread_slots(gate_up, down, picks, ex_count):
    chosen = jnp.concatenate([gate_up[picks], down[picks][:, None]], axis=1)
    count, parts, ff_width, col_width = chosen.shape
    pieces = chosen.reshape(count, parts, ex_count, ff_width // ex_count, col_width)
    spread = lax.all_to_all(pieces, "expert", split_axis=2, concat_axis=0, tiled=True)
    return spread.reshape(ex_count * count, parts, ff_width // ex_count, col_width)


def migrate(expert_gate_up, expert_down, old_place, new_place, ex_index):
    rows, slots_local = old_place.shape
    slots = rows * slots_local
    ex_count = rows
    ff_width = expert_gate_up.shape[2]
    changed = old_place != new_place
    moved_slot = jnp.argmax(changed, axis=1)
    wanted = jnp.take_along_axis(new_place, moved_slot[:, None], axis=1)[:, 0]
    hit = old_place.reshape(-1)[None, :] == wanted[:, None]
    first = jnp.argmax(hit, axis=1).astype(jnp.int32)
    last = (slots - 1 - jnp.argmax(hit[:, ::-1], axis=1)).astype(jnp.int32)
    slot_ids = jnp.arange(slots, dtype=jnp.int32)

    def needed_of(src):
        needed = jnp.any(src[:, None] == slot_ids[None, :], axis=0).reshape(rows, slots_local)
        return needed, jnp.max(jnp.sum(needed.astype(jnp.int32), axis=1))

    need_first, load_first = needed_of(first)
    need_last, load_last = needed_of(last)
    use_last = load_last < load_first
    source = jnp.where(use_last, last, first)
    needed = jnp.where(use_last, need_last, need_first)
    load = jnp.minimum(load_first, load_last)
    rank = jnp.cumsum(needed.astype(jnp.int32), axis=1) - 1
    local_ids = jnp.arange(slots_local, dtype=jnp.int32)
    picks = jnp.stack(
        [jnp.argmax(needed & (rank == k), axis=1).astype(jnp.int32) for k in range(slots_local)],
        axis=1,
    )
    my_picks = picks[ex_index]
    src_dev = source // slots_local
    src_rank = rank.reshape(-1)[source]
    fast = min(2, slots_local)
    spread_a = spread_slots(expert_gate_up, expert_down, my_picks[:fast], ex_count)
    out_a = spread_a[src_dev * fast + jnp.minimum(src_rank, fast - 1)]
    if slots_local > fast:
        rest = slots_local - fast

        def extra():
            spread_b = spread_slots(expert_gate_up, expert_down, my_picks[fast:], ex_count)
            return spread_b[src_dev * rest + jnp.clip(src_rank - fast, 0, rest - 1)]

        out_b = lax.cond(load > fast, extra, lambda: jnp.zeros_like(out_a))
        out_a = jnp.where((src_rank < fast)[:, None, None, None], out_a, out_b)
    arrived = lax.all_to_all(out_a, "expert", split_axis=0, concat_axis=2, tiled=True)
    is_moved = local_ids == moved_slot[ex_index]
    moved_gate_up = jnp.where(is_moved[:, None, None, None], arrived[:, :2], expert_gate_up)
    moved_down = jnp.where(is_moved[:, None, None], arrived[:, 2], expert_down)
    return moved_gate_up, moved_down


def local(
    hidden,
    attn_gain,
    query_weight,
    latent_down,
    latent_up,
    out_weight,
    latent_pool,
    page_table,
    page_counts,
    ffn_gain,
    expert_ids,
    expert_gates,
    old_place,
    new_place,
    expert_gate_up,
    expert_down,
    shared_gate_up,
    shared_down,
):
    dp_count = lax.axis_size("dp")
    ex_count = lax.axis_size("expert")
    dp_index = lax.axis_index("dp")
    ex_index = lax.axis_index("expert")
    req_local = hidden.shape[0]
    group_rows = req_local * ex_count
    requests = page_counts.shape[0]
    head_local = query_weight.shape[0] // (NOPE + ROPE)
    score_scale = (NOPE + ROPE) ** (-0.5)
    group_start = dp_index * group_rows
    everyone = gather_rows(hidden)
    normed = rms_norm(everyone.astype(jnp.float32), attn_gain).astype(jnp.bfloat16)
    queries = jnp.einsum(
        "td,qd->tq", normed, query_weight, preferred_element_type=jnp.float32
    ).reshape(requests, head_local, NOPE + ROPE)
    position = (page_counts * PAGE).astype(jnp.float32)
    query_rope = rotary(queries[..., NOPE:], position[:, None]).astype(jnp.bfloat16)
    up_table = latent_up.reshape(LATENT, head_local, NOPE + VHEAD)
    query_latent = jnp.einsum(
        "thn,lhn->thl",
        queries[..., :NOPE],
        up_table[..., :NOPE].astype(jnp.float32),
        precision=HIGHEST,
    ).astype(jnp.bfloat16)
    pages_local = latent_pool.shape[0]
    pool_total = pages_local * dp_count
    flat_pages = page_table.reshape(-1)
    flat_owner = jnp.repeat(jnp.arange(requests, dtype=jnp.int32), page_table.shape[1])
    target = jnp.where(flat_pages >= 0, flat_pages, pool_total)
    owner_all = jnp.full((pool_total,), -1, jnp.int32).at[target].set(flat_owner, mode="drop")
    page_owner = lax.dynamic_slice_in_dim(owner_all, dp_index * pages_local, pages_local)
    page_used = page_owner >= 0
    owner_safe = jnp.maximum(page_owner, 0)
    page_latent = latent_pool[..., :LATENT]
    page_rope = latent_pool[..., LATENT:]
    scores = jnp.einsum(
        "phl,pkl->phk", query_latent[owner_safe], page_latent, preferred_element_type=jnp.float32
    )
    scores = (
        scores
        + jnp.einsum(
            "phr,pkr->phk", query_rope[owner_safe], page_rope, preferred_element_type=jnp.float32
        )
    ) * score_scale
    raw_max = jnp.max(scores, axis=2)
    weights = jnp.exp(scores - raw_max[..., None])
    page_total = jnp.sum(weights, axis=2)
    page_mix = jnp.einsum(
        "phk,pkl->phl",
        weights.astype(jnp.bfloat16),
        page_latent,
        preferred_element_type=jnp.float32,
    )
    page_max = jnp.where(page_used[:, None], raw_max, MASKED_SCORE)
    member = page_owner[None, :] == jnp.arange(requests, dtype=jnp.int32)[:, None]
    req_max = jnp.max(jnp.where(member[:, :, None], page_max[None], MASKED_SCORE), axis=1)
    rescale = jnp.where(page_used[:, None], jnp.exp(page_max - req_max[owner_safe]), 0.0)
    member_float = member.astype(jnp.float32)
    req_total = jnp.dot(member_float, page_total * rescale, precision=HIGHEST)
    req_mix = jnp.einsum(
        "rp,phl->rhl", member_float, page_mix * rescale[..., None], precision=HIGHEST
    )
    packed = jnp.concatenate([req_mix, req_max[..., None], req_total[..., None]], axis=-1)
    gathered = lax.all_gather(packed, "dp", axis=0, tiled=False)
    gathered = lax.dynamic_slice_in_dim(gathered, group_start, group_rows, 1)
    each_max = gathered[..., LATENT]
    part_max = jnp.max(each_max, axis=0)
    each_weight = jnp.exp(each_max - part_max[None])
    part_total = jnp.sum(gathered[..., LATENT + 1] * each_weight, axis=0)
    part_mix = jnp.sum(gathered[..., :LATENT] * each_weight[..., None], axis=0)
    own_normed = lax.dynamic_slice_in_dim(normed, group_start, group_rows, 0)
    own_position = lax.dynamic_slice_in_dim(position, group_start, group_rows, 0)
    fresh_latent = jnp.dot(own_normed, latent_down, preferred_element_type=jnp.float32)
    new_latent = rms_plain(fresh_latent[:, :LATENT]).astype(jnp.bfloat16)
    new_rope = rotary(fresh_latent[:, LATENT:], own_position).astype(jnp.bfloat16)
    own_query = lax.dynamic_slice_in_dim(query_latent, group_start, group_rows, 0)
    own_rope_query = lax.dynamic_slice_in_dim(query_rope, group_start, group_rows, 0)
    own_score = jnp.einsum("thl,tl->th", own_query, new_latent, preferred_element_type=jnp.float32)
    own_score = (
        own_score
        + jnp.einsum("thr,tr->th", own_rope_query, new_rope, preferred_element_type=jnp.float32)
    ) * score_scale
    highest = jnp.maximum(part_max, own_score)
    kept_part = jnp.exp(part_max - highest)
    own_weight = jnp.exp(own_score - highest)
    denominator = part_total * kept_part + own_weight
    numerator = (
        part_mix * kept_part[..., None]
        + own_weight[..., None] * new_latent.astype(jnp.float32)[:, None, :]
    )
    attended = (numerator / denominator[..., None]).astype(jnp.bfloat16)
    heads_out = jnp.einsum(
        "thl,lhv->thv", attended, up_table[..., NOPE:], preferred_element_type=jnp.float32
    )
    heads_out = heads_out.astype(jnp.bfloat16).reshape(group_rows, head_local * VHEAD)
    partial_value = jnp.dot(heads_out, out_weight, preferred_element_type=jnp.float32)
    attn_out = lax.psum_scatter(partial_value, "expert", scatter_dimension=0, tiled=True)
    residual = hidden.astype(jnp.float32) + attn_out
    normed_ffn = rms_norm(residual, ffn_gain).astype(jnp.bfloat16)
    slots_local = expert_gate_up.shape[0]
    ff_width = expert_gate_up.shape[2]
    col_width = expert_gate_up.shape[3]
    every_row = gather_rows(normed_ffn)
    my_columns = lax.dynamic_slice_in_dim(every_row, dp_index * col_width, col_width, 1)
    by_group = my_columns.reshape(dp_count, ex_count, req_local, col_width).transpose(1, 0, 2, 3)
    ffn_rows = by_group.reshape(requests, col_width)
    column_rows = lax.dynamic_index_in_dim(by_group, ex_index, 0, keepdims=False).reshape(
        dp_count * req_local, col_width
    )
    top_count = expert_ids.shape[1]
    experts_count = EXP_DEV * ex_count
    ids_order = (
        expert_ids.reshape(dp_count, ex_count, req_local, top_count)
        .transpose(1, 0, 2, 3)
        .reshape(requests, top_count)
    )
    gates_order = (
        expert_gates.reshape(dp_count, ex_count, req_local, top_count)
        .transpose(1, 0, 2, 3)
        .reshape(requests, top_count)
    )
    old_flat = old_place.reshape(-1)
    holds_map = old_flat[None, :] == jnp.arange(experts_count, dtype=jnp.int32)[:, None]
    holder = jnp.argmax(holds_map, axis=1)
    slot_of = holder[ids_order.reshape(-1)]
    capacity = 2 * requests * top_count // experts_count
    local_slot = slot_of - ex_index * slots_local
    slot_hot = local_slot[:, None] == jnp.arange(slots_local, dtype=jnp.int32)[None, :]
    slot_rank = jnp.cumsum(slot_hot.astype(jnp.int32), axis=0) - 1
    position_in = jnp.where(slot_hot, slot_rank, capacity)
    route_hot = (
        position_in[:, :, None] == jnp.arange(capacity, dtype=jnp.int32)[None, None, :]
    ).astype(jnp.float32)
    route_hot = route_hot.reshape(requests, top_count, slots_local, capacity)
    dispatch = jnp.sum(route_hot, axis=1).astype(jnp.bfloat16)
    combine = jnp.sum(route_hot * gates_order[:, :, None, None], axis=1)
    slot_inputs = jnp.einsum(
        "tsc,td->scd", dispatch, ffn_rows, preferred_element_type=jnp.float32
    ).astype(jnp.bfloat16)
    routed_part = jnp.einsum(
        "scd,sgfd->sgcf", slot_inputs, expert_gate_up, preferred_element_type=jnp.float32
    )
    shared_part = jnp.einsum(
        "td,gfd->gtf", column_rows, shared_gate_up, preferred_element_type=jnp.float32
    )
    routed_sum, shared_sum = lax.psum((routed_part, shared_part), "dp")
    activated = (jax.nn.silu(routed_sum[:, 0]) * routed_sum[:, 1]).astype(jnp.bfloat16)
    slot_out = jnp.einsum(
        "scf,sfd->scd", activated, expert_down, preferred_element_type=jnp.float32
    )
    routed = jnp.einsum("tsc,scd->td", combine, slot_out, precision=HIGHEST)
    shared_act = (jax.nn.silu(shared_sum[0]) * shared_sum[1]).astype(jnp.bfloat16)
    shared_term = jnp.dot(shared_act, shared_down, preferred_element_type=jnp.float32)
    moe_rows = lax.psum_scatter(routed, "expert", scatter_dimension=0, tiled=True)
    moe_part = lax.all_to_all(moe_rows + shared_term, "dp", split_axis=0, concat_axis=1, tiled=True)
    layer_out = (residual + moe_part).astype(jnp.bfloat16)
    moved_gate_up, moved_down = migrate(expert_gate_up, expert_down, old_place, new_place, ex_index)
    return (layer_out, moved_gate_up, moved_down)


def solution(mesh):
    in_specs = (
        P(("dp", "expert"), None),
        P(),
        P("expert", None),
        P(),
        P(None, "expert"),
        P("expert", None),
        P("dp", None, None),
        P(),
        P(),
        P(),
        P(),
        P(),
        P(),
        P(),
        P("expert", None, None, "dp"),
        P("expert", None, "dp"),
        P(None, None, "dp"),
        P(None, "dp"),
    )
    out_specs = (P(("dp", "expert"), None), P("expert", None, None, "dp"), P("expert", None, "dp"))
    return jax.shard_map(local, mesh=mesh, in_specs=in_specs, out_specs=out_specs, check_vma=False)
```

```python
import math

import jax
import jax.numpy as jnp
from jax import lax
from jax.sharding import PartitionSpec as P

NOPE = 128
ROPE = 64
VHEAD = 128
LATENT = 512
EXP_DEV = 3
PAGE = 32


EPSILON = 1e-06
ROPE_BASE = 50000.0
MASKED_SCORE = -1e30
HIGHEST = lax.Precision.HIGHEST


def rms_plain(values):
    mean_square = jnp.mean(values * values, axis=-1, keepdims=True)
    return values * lax.rsqrt(mean_square + EPSILON)


def rms_norm(values, norm_gain):
    return rms_plain(values) * norm_gain


def rotary(values, position):
    half_width = values.shape[-1] // 2
    exponent = jnp.arange(half_width).astype(jnp.float32) * (2.0 / values.shape[-1])
    frequency = jnp.exp(-exponent * math.log(ROPE_BASE))
    angles = position[..., None] * frequency
    cosine = jnp.cos(angles)
    sine_part = jnp.sin(angles)
    first_half = values[..., :half_width]
    second = values[..., half_width:]
    return jnp.concatenate(
        [first_half * cosine - second * sine_part, second * cosine + first_half * sine_part],
        axis=-1,
    )


def gather_rows(rows):
    by_expert = lax.all_gather(rows, "expert", axis=0, tiled=True)
    return lax.all_gather(by_expert, "dp", axis=0, tiled=True)


def pick_rows(table, rows):
    return jnp.stack([lax.dynamic_index_in_dim(table, rows[k], 0, False) for k in range(rows.shape[0])])


def pick_slots(gate_up, down, picks):
    return jnp.concatenate([pick_rows(gate_up, picks), pick_rows(down, picks)[:, None]], axis=1)


def spread_slots(chosen, ex_count):
    count, parts, ff_width, col_width = chosen.shape
    pieces = chosen.reshape(count, parts, ex_count, ff_width // ex_count, col_width)
    spread = lax.all_to_all(pieces, "expert", split_axis=2, concat_axis=0, tiled=True)
    return spread.reshape(ex_count * count, parts, ff_width // ex_count, col_width)


def scatter_sum(values, axis):
    count = lax.axis_size(axis)
    received = lax.all_to_all(values, axis, split_axis=0, concat_axis=0, tiled=True)
    return jnp.sum(received.reshape((count, -1) + values.shape[1:]), axis=0)


def sum_over(values, axis):
    return jnp.sum(lax.all_gather(values, axis, axis=0, tiled=False), axis=0)


def migrate_start(expert_gate_up, expert_down, old_place, new_place, ex_index):
    rows, slots_local = old_place.shape
    slots = rows * slots_local
    ex_count = rows
    ff_width = expert_gate_up.shape[2]
    changed = old_place != new_place
    moved_slot = jnp.argmax(changed, axis=1)
    wanted = jnp.take_along_axis(new_place, moved_slot[:, None], axis=1)[:, 0]
    hit = old_place.reshape(-1)[None, :] == wanted[:, None]
    first = jnp.argmax(hit, axis=1).astype(jnp.int32)
    last = (slots - 1 - jnp.argmax(hit[:, ::-1], axis=1)).astype(jnp.int32)
    slot_ids = jnp.arange(slots, dtype=jnp.int32)

    def needed_of(src):
        needed = jnp.any(src[:, None] == slot_ids[None, :], axis=0).reshape(rows, slots_local)
        return needed, jnp.max(jnp.sum(needed.astype(jnp.int32), axis=1))

    need_first, load_first = needed_of(first)
    need_last, load_last = needed_of(last)
    use_last = load_last < load_first
    source = jnp.where(use_last, last, first)
    needed = jnp.where(use_last, need_last, need_first)
    load = jnp.minimum(load_first, load_last)
    rank = jnp.cumsum(needed.astype(jnp.int32), axis=1) - 1
    local_ids = jnp.arange(slots_local, dtype=jnp.int32)
    picks = jnp.stack(
        [jnp.argmax(needed & (rank == k), axis=1).astype(jnp.int32) for k in range(slots_local)],
        axis=1,
    )
    my_picks = picks[ex_index]
    src_dev = source // slots_local
    src_rank = rank.reshape(-1)[source]
    fast = min(2, slots_local)
    chosen = pick_slots(expert_gate_up, expert_down, my_picks[:fast])
    return chosen, (my_picks, src_dev, src_rank, load, moved_slot[ex_index])


def migrate_finish(chosen, plan, expert_gate_up, expert_down):
    my_picks, src_dev, src_rank, load, my_moved = plan
    ex_count = src_dev.shape[0]
    slots_local = expert_gate_up.shape[0]
    fast = chosen.shape[0]
    spread_a = spread_slots(chosen, ex_count)
    out_a = pick_rows(spread_a, src_dev * fast + jnp.minimum(src_rank, fast - 1))
    if slots_local > fast:
        rest = slots_local - fast

        def extra():
            spread_b = spread_slots(pick_slots(expert_gate_up, expert_down, my_picks[fast:]), ex_count)
            out_b = pick_rows(spread_b, src_dev * rest + jnp.clip(src_rank - fast, 0, rest - 1))
            return jnp.where((src_rank < fast)[:, None, None, None], out_a, out_b)

        out_a = lax.cond(load > fast, extra, lambda: out_a)
    arrived = lax.all_to_all(out_a, "expert", split_axis=0, concat_axis=2, tiled=True)
    moved_gate_up = lax.dynamic_update_index_in_dim(expert_gate_up, arrived[0, :2], my_moved, 0)
    moved_down = lax.dynamic_update_index_in_dim(expert_down, arrived[0, 2], my_moved, 0)
    return moved_gate_up, moved_down


def local(
    hidden,
    attn_gain,
    query_weight,
    latent_down,
    latent_up,
    out_weight,
    latent_pool,
    page_table,
    page_counts,
    ffn_gain,
    expert_ids,
    expert_gates,
    old_place,
    new_place,
    expert_gate_up,
    expert_down,
    shared_gate_up,
    shared_down,
):
    dp_count = lax.axis_size("dp")
    ex_count = lax.axis_size("expert")
    dp_index = lax.axis_index("dp")
    ex_index = lax.axis_index("expert")
    req_local = hidden.shape[0]
    group_rows = req_local * ex_count
    requests = page_counts.shape[0]
    head_local = query_weight.shape[0] // (NOPE + ROPE)
    score_scale = (NOPE + ROPE) ** (-0.5)
    group_start = dp_index * group_rows
    chosen, plan = migrate_start(expert_gate_up, expert_down, old_place, new_place, ex_index)
    everyone = gather_rows(hidden)
    everyone, chosen = lax.optimization_barrier((everyone, chosen))
    normed = rms_norm(everyone.astype(jnp.float32), attn_gain).astype(jnp.bfloat16)
    queries = jnp.einsum(
        "td,qd->tq", normed, query_weight, preferred_element_type=jnp.float32
    ).reshape(requests, head_local, NOPE + ROPE)
    position = (page_counts * PAGE).astype(jnp.float32)
    query_rope = rotary(queries[..., NOPE:], position[:, None]).astype(jnp.bfloat16)
    up_table = latent_up.reshape(LATENT, head_local, NOPE + VHEAD)
    query_latent = jnp.einsum(
        "thn,lhn->thl",
        queries[..., :NOPE],
        up_table[..., :NOPE].astype(jnp.float32),
        precision=HIGHEST,
    ).astype(jnp.bfloat16)
    pages_local = latent_pool.shape[0]
    pool_total = pages_local * dp_count
    flat_pages = page_table.reshape(-1)
    flat_owner = jnp.repeat(jnp.arange(requests, dtype=jnp.int32), page_table.shape[1])
    target = jnp.where(flat_pages >= 0, flat_pages, pool_total)
    owner_all = jnp.full((pool_total,), -1, jnp.int32).at[target].set(flat_owner, mode="drop")
    page_owner = lax.dynamic_slice_in_dim(owner_all, dp_index * pages_local, pages_local)
    page_used = page_owner >= 0
    owner_safe = jnp.maximum(page_owner, 0)
    page_latent = latent_pool[..., :LATENT]
    page_rope = latent_pool[..., LATENT:]
    scores = jnp.einsum(
        "phl,pkl->phk", query_latent[owner_safe], page_latent, preferred_element_type=jnp.float32
    )
    scores = (
        scores
        + jnp.einsum(
            "phr,pkr->phk", query_rope[owner_safe], page_rope, preferred_element_type=jnp.float32
        )
    ) * score_scale
    raw_max = jnp.max(scores, axis=2)
    weights = jnp.exp(scores - raw_max[..., None])
    page_total = jnp.sum(weights, axis=2)
    page_mix = jnp.einsum(
        "phk,pkl->phl",
        weights.astype(jnp.bfloat16),
        page_latent,
        preferred_element_type=jnp.float32,
    )
    page_max = jnp.where(page_used[:, None], raw_max, MASKED_SCORE)
    member = page_owner[None, :] == jnp.arange(requests, dtype=jnp.int32)[:, None]
    req_max = jnp.max(jnp.where(member[:, :, None], page_max[None], MASKED_SCORE), axis=1)
    rescale = jnp.where(page_used[:, None], jnp.exp(page_max - req_max[owner_safe]), 0.0)
    member_float = member.astype(jnp.float32)
    req_total = jnp.dot(member_float, page_total * rescale, precision=HIGHEST)
    req_mix = jnp.einsum(
        "rp,phl->rhl", member_float, page_mix * rescale[..., None], precision=HIGHEST
    )
    packed = jnp.concatenate([req_mix, req_max[..., None], req_total[..., None]], axis=-1)
    gathered = lax.all_gather(packed, "dp", axis=0, tiled=False)
    gathered = lax.dynamic_slice_in_dim(gathered, group_start, group_rows, 1)
    each_max = gathered[..., LATENT]
    part_max = jnp.max(each_max, axis=0)
    each_weight = jnp.exp(each_max - part_max[None])
    part_total = jnp.sum(gathered[..., LATENT + 1] * each_weight, axis=0)
    part_mix = jnp.sum(gathered[..., :LATENT] * each_weight[..., None], axis=0)
    own_normed = lax.dynamic_slice_in_dim(normed, group_start, group_rows, 0)
    own_position = lax.dynamic_slice_in_dim(position, group_start, group_rows, 0)
    fresh_latent = jnp.dot(own_normed, latent_down, preferred_element_type=jnp.float32)
    new_latent = rms_plain(fresh_latent[:, :LATENT]).astype(jnp.bfloat16)
    new_rope = rotary(fresh_latent[:, LATENT:], own_position).astype(jnp.bfloat16)
    own_query = lax.dynamic_slice_in_dim(query_latent, group_start, group_rows, 0)
    own_rope_query = lax.dynamic_slice_in_dim(query_rope, group_start, group_rows, 0)
    own_score = jnp.einsum("thl,tl->th", own_query, new_latent, preferred_element_type=jnp.float32)
    own_score = (
        own_score
        + jnp.einsum("thr,tr->th", own_rope_query, new_rope, preferred_element_type=jnp.float32)
    ) * score_scale
    highest = jnp.maximum(part_max, own_score)
    kept_part = jnp.exp(part_max - highest)
    own_weight = jnp.exp(own_score - highest)
    denominator = part_total * kept_part + own_weight
    numerator = (
        part_mix * kept_part[..., None]
        + own_weight[..., None] * new_latent.astype(jnp.float32)[:, None, :]
    )
    attended = (numerator / denominator[..., None]).astype(jnp.bfloat16)
    heads_out = jnp.einsum(
        "thl,lhv->thv", attended, up_table[..., NOPE:], preferred_element_type=jnp.float32
    )
    heads_out = heads_out.astype(jnp.bfloat16).reshape(group_rows, head_local * VHEAD)
    partial_value = jnp.dot(heads_out, out_weight, preferred_element_type=jnp.float32)
    attn_out = scatter_sum(partial_value, "expert")
    residual = hidden.astype(jnp.float32) + attn_out
    normed_ffn = rms_norm(residual, ffn_gain).astype(jnp.bfloat16)
    slots_local = expert_gate_up.shape[0]
    ff_width = expert_gate_up.shape[2]
    col_width = expert_gate_up.shape[3]
    every_row = gather_rows(normed_ffn)
    my_columns = lax.dynamic_slice_in_dim(every_row, dp_index * col_width, col_width, 1)
    by_group = my_columns.reshape(dp_count, ex_count, req_local, col_width).transpose(1, 0, 2, 3)
    ffn_rows = by_group.reshape(requests, col_width)
    column_rows = lax.dynamic_index_in_dim(by_group, ex_index, 0, keepdims=False).reshape(
        dp_count * req_local, col_width
    )
    top_count = expert_ids.shape[1]
    experts_count = EXP_DEV * ex_count
    ids_order = (
        expert_ids.reshape(dp_count, ex_count, req_local, top_count)
        .transpose(1, 0, 2, 3)
        .reshape(requests, top_count)
    )
    gates_order = (
        expert_gates.reshape(dp_count, ex_count, req_local, top_count)
        .transpose(1, 0, 2, 3)
        .reshape(requests, top_count)
    )
    old_flat = old_place.reshape(-1)
    holds_map = old_flat[None, :] == jnp.arange(experts_count, dtype=jnp.int32)[:, None]
    holder = jnp.argmax(holds_map, axis=1)
    slot_of = holder[ids_order.reshape(-1)]
    capacity = 2 * requests * top_count // experts_count
    local_slot = slot_of - ex_index * slots_local
    slot_hot = local_slot[:, None] == jnp.arange(slots_local, dtype=jnp.int32)[None, :]
    slot_rank = jnp.cumsum(slot_hot.astype(jnp.int32), axis=0) - 1
    position_in = jnp.where(slot_hot, slot_rank, capacity)
    route_hot = (
        position_in[:, :, None] == jnp.arange(capacity, dtype=jnp.int32)[None, None, :]
    ).astype(jnp.float32)
    route_hot = route_hot.reshape(requests, top_count, slots_local, capacity)
    dispatch = jnp.sum(route_hot, axis=1).astype(jnp.bfloat16)
    combine = jnp.sum(route_hot * gates_order[:, :, None, None], axis=1)
    slot_inputs = jnp.einsum(
        "tsc,td->scd", dispatch, ffn_rows, preferred_element_type=jnp.float32
    ).astype(jnp.bfloat16)
    routed_part = jnp.einsum(
        "scd,sgfd->sgcf", slot_inputs, expert_gate_up, preferred_element_type=jnp.float32
    )
    shared_part = jnp.einsum(
        "td,gfd->gtf", column_rows, shared_gate_up, preferred_element_type=jnp.float32
    )
    routed_sum, shared_sum = sum_over(routed_part, "dp"), sum_over(shared_part, "dp")
    activated = (jax.nn.silu(routed_sum[:, 0]) * routed_sum[:, 1]).astype(jnp.bfloat16)
    slot_out = jnp.einsum(
        "scf,sfd->scd", activated, expert_down, preferred_element_type=jnp.float32
    )
    routed = jnp.einsum("tsc,scd->td", combine, slot_out, precision=HIGHEST)
    shared_act = (jax.nn.silu(shared_sum[0]) * shared_sum[1]).astype(jnp.bfloat16)
    shared_term = jnp.dot(shared_act, shared_down, preferred_element_type=jnp.float32)
    moe_rows = scatter_sum(routed, "expert")
    moe_part = lax.all_to_all(moe_rows + shared_term, "dp", split_axis=0, concat_axis=1, tiled=True)
    layer_out = (residual + moe_part).astype(jnp.bfloat16)
    moved_gate_up, moved_down = migrate_finish(chosen, plan, expert_gate_up, expert_down)
    return (layer_out, moved_gate_up, moved_down)


def solution(mesh):
    in_specs = (
        P(("dp", "expert"), None),
        P(),
        P("expert", None),
        P(),
        P(None, "expert"),
        P("expert", None),
        P("dp", None, None),
        P(),
        P(),
        P(),
        P(),
        P(),
        P(),
        P(),
        P("expert", None, None, "dp"),
        P("expert", None, "dp"),
        P(None, None, "dp"),
        P(None, "dp"),
    )
    out_specs = (P(("dp", "expert"), None), P("expert", None, None, "dp"), P("expert", None, "dp"))
    return jax.shard_map(local, mesh=mesh, in_specs=in_specs, out_specs=out_specs, check_vma=False)
```

```python
import math

import jax
import jax.numpy as jnp
from jax import lax
from jax.sharding import PartitionSpec as P

NOPE = 128
ROPE = 64
VHEAD = 128
LATENT = 512
EXP_DEV = 3
PAGE = 32


EPSILON = 1e-06
ROPE_BASE = 50000.0
MASKED_SCORE = -1e30
HIGHEST = lax.Precision.HIGHEST


def rms_plain(values):
    mean_square = jnp.mean(values * values, axis=-1, keepdims=True)
    return values * lax.rsqrt(mean_square + EPSILON)


def rms_norm(values, norm_gain):
    return rms_plain(values) * norm_gain


def rotary(values, position):
    half_width = values.shape[-1] // 2
    exponent = jnp.arange(half_width).astype(jnp.float32) * (2.0 / values.shape[-1])
    frequency = jnp.exp(-exponent * math.log(ROPE_BASE))
    angles = position[..., None] * frequency
    cosine = jnp.cos(angles)
    sine_part = jnp.sin(angles)
    first_half = values[..., :half_width]
    second = values[..., half_width:]
    return jnp.concatenate(
        [first_half * cosine - second * sine_part, second * cosine + first_half * sine_part],
        axis=-1,
    )


def gather_rows(rows):
    by_expert = lax.all_gather(rows, "expert", axis=0, tiled=True)
    return lax.all_gather(by_expert, "dp", axis=0, tiled=True)


def pick_rows(table, rows):
    return jnp.stack([lax.dynamic_index_in_dim(table, rows[k], 0, False) for k in range(rows.shape[0])])


def pick_slots(gate_up, down, picks):
    return jnp.concatenate([pick_rows(gate_up, picks), pick_rows(down, picks)[:, None]], axis=1)


def spread_slots(chosen, ex_count):
    count, parts, ff_width, col_width = chosen.shape
    pieces = chosen.reshape(count, parts, ex_count, ff_width // ex_count, col_width)
    spread = lax.all_to_all(pieces, "expert", split_axis=2, concat_axis=0, tiled=True)
    return spread.reshape(ex_count * count, parts, ff_width // ex_count, col_width)


def scatter_sum(values, axis):
    count = lax.axis_size(axis)
    share = values.shape[0] // count
    gathered = lax.all_gather(values, axis, axis=0, tiled=False)
    mine = lax.dynamic_slice_in_dim(gathered, lax.axis_index(axis) * share, share, 1)
    return jnp.sum(mine, axis=0)


def sum_over(values, axis):
    return jnp.sum(lax.all_gather(values, axis, axis=0, tiled=False), axis=0)


def migrate_start(expert_gate_up, expert_down, old_place, new_place, ex_index):
    rows, slots_local = old_place.shape
    slots = rows * slots_local
    ex_count = rows
    ff_width = expert_gate_up.shape[2]
    changed = old_place != new_place
    moved_slot = jnp.argmax(changed, axis=1)
    wanted = jnp.take_along_axis(new_place, moved_slot[:, None], axis=1)[:, 0]
    hit = old_place.reshape(-1)[None, :] == wanted[:, None]
    first = jnp.argmax(hit, axis=1).astype(jnp.int32)
    last = (slots - 1 - jnp.argmax(hit[:, ::-1], axis=1)).astype(jnp.int32)
    slot_ids = jnp.arange(slots, dtype=jnp.int32)

    def needed_of(src):
        needed = jnp.any(src[:, None] == slot_ids[None, :], axis=0).reshape(rows, slots_local)
        return needed, jnp.max(jnp.sum(needed.astype(jnp.int32), axis=1))

    need_first, load_first = needed_of(first)
    need_last, load_last = needed_of(last)
    use_last = load_last < load_first
    source = jnp.where(use_last, last, first)
    needed = jnp.where(use_last, need_last, need_first)
    load = jnp.minimum(load_first, load_last)
    rank = jnp.cumsum(needed.astype(jnp.int32), axis=1) - 1
    local_ids = jnp.arange(slots_local, dtype=jnp.int32)
    picks = jnp.stack(
        [jnp.argmax(needed & (rank == k), axis=1).astype(jnp.int32) for k in range(slots_local)],
        axis=1,
    )
    my_picks = picks[ex_index]
    src_dev = source // slots_local
    src_rank = rank.reshape(-1)[source]
    fast = min(2, slots_local)
    chosen = [pick_slots(expert_gate_up, expert_down, my_picks[k:k + 1]) for k in range(fast)]
    return chosen, (my_picks, src_dev, src_rank, load, moved_slot[ex_index])


def migrate_finish(spread, plan, expert_gate_up, expert_down):
    my_picks, src_dev, src_rank, load, my_moved = plan
    ex_count = src_dev.shape[0]
    slots_local = expert_gate_up.shape[0]
    fast = len(spread)
    stacked = jnp.concatenate(spread, axis=0)
    out_a = pick_rows(stacked, jnp.minimum(src_rank, fast - 1) * ex_count + src_dev)
    if slots_local > fast:
        rest = slots_local - fast

        def extra():
            spread_b = spread_slots(pick_slots(expert_gate_up, expert_down, my_picks[fast:]), ex_count)
            out_b = pick_rows(spread_b, src_dev * rest + jnp.clip(src_rank - fast, 0, rest - 1))
            return jnp.where((src_rank < fast)[:, None, None, None], out_a, out_b)

        out_a = lax.cond(load > fast, extra, lambda: out_a)
    arrived = lax.all_to_all(out_a, "expert", split_axis=0, concat_axis=2, tiled=True)
    moved_gate_up = lax.dynamic_update_index_in_dim(expert_gate_up, arrived[0, :2], my_moved, 0)
    moved_down = lax.dynamic_update_index_in_dim(expert_down, arrived[0, 2], my_moved, 0)
    return moved_gate_up, moved_down


def local(
    hidden,
    attn_gain,
    query_weight,
    latent_down,
    latent_up,
    out_weight,
    latent_pool,
    page_table,
    page_counts,
    ffn_gain,
    expert_ids,
    expert_gates,
    old_place,
    new_place,
    expert_gate_up,
    expert_down,
    shared_gate_up,
    shared_down,
):
    dp_count = lax.axis_size("dp")
    ex_count = lax.axis_size("expert")
    dp_index = lax.axis_index("dp")
    ex_index = lax.axis_index("expert")
    req_local = hidden.shape[0]
    group_rows = req_local * ex_count
    requests = page_counts.shape[0]
    head_local = query_weight.shape[0] // (NOPE + ROPE)
    score_scale = (NOPE + ROPE) ** (-0.5)
    group_start = dp_index * group_rows
    chosen, plan = migrate_start(expert_gate_up, expert_down, old_place, new_place, ex_index)
    everyone = gather_rows(hidden)
    everyone, first_chosen = lax.optimization_barrier((everyone, chosen[0]))
    first_spread = spread_slots(first_chosen, ex_count)
    normed = rms_norm(everyone.astype(jnp.float32), attn_gain).astype(jnp.bfloat16)
    queries = jnp.einsum(
        "td,qd->tq", normed, query_weight, preferred_element_type=jnp.float32
    ).reshape(requests, head_local, NOPE + ROPE)
    position = (page_counts * PAGE).astype(jnp.float32)
    query_rope = rotary(queries[..., NOPE:], position[:, None]).astype(jnp.bfloat16)
    up_table = latent_up.reshape(LATENT, head_local, NOPE + VHEAD)
    query_latent = jnp.einsum(
        "thn,lhn->thl",
        queries[..., :NOPE],
        up_table[..., :NOPE].astype(jnp.float32),
        precision=HIGHEST,
    ).astype(jnp.bfloat16)
    pages_local = latent_pool.shape[0]
    pool_total = pages_local * dp_count
    flat_pages = page_table.reshape(-1)
    flat_owner = jnp.repeat(jnp.arange(requests, dtype=jnp.int32), page_table.shape[1])
    target = jnp.where(flat_pages >= 0, flat_pages, pool_total)
    owner_all = jnp.full((pool_total,), -1, jnp.int32).at[target].set(flat_owner, mode="drop")
    page_owner = lax.dynamic_slice_in_dim(owner_all, dp_index * pages_local, pages_local)
    page_used = page_owner >= 0
    owner_safe = jnp.maximum(page_owner, 0)
    page_latent = latent_pool[..., :LATENT]
    page_rope = latent_pool[..., LATENT:]
    scores = jnp.einsum(
        "phl,pkl->phk", query_latent[owner_safe], page_latent, preferred_element_type=jnp.float32
    )
    scores = (
        scores
        + jnp.einsum(
            "phr,pkr->phk", query_rope[owner_safe], page_rope, preferred_element_type=jnp.float32
        )
    ) * score_scale
    raw_max = jnp.max(scores, axis=2)
    weights = jnp.exp(scores - raw_max[..., None])
    page_total = jnp.sum(weights, axis=2)
    page_mix = jnp.einsum(
        "phk,pkl->phl",
        weights.astype(jnp.bfloat16),
        page_latent,
        preferred_element_type=jnp.float32,
    )
    page_max = jnp.where(page_used[:, None], raw_max, MASKED_SCORE)
    member = page_owner[None, :] == jnp.arange(requests, dtype=jnp.int32)[:, None]
    req_max = jnp.max(jnp.where(member[:, :, None], page_max[None], MASKED_SCORE), axis=1)
    rescale = jnp.where(page_used[:, None], jnp.exp(page_max - req_max[owner_safe]), 0.0)
    member_float = member.astype(jnp.float32)
    req_total = jnp.dot(member_float, page_total * rescale, precision=HIGHEST)
    req_mix = jnp.einsum(
        "rp,phl->rhl", member_float, page_mix * rescale[..., None], precision=HIGHEST
    )
    packed = jnp.concatenate([req_mix, req_max[..., None], req_total[..., None]], axis=-1)
    gathered = lax.all_gather(packed, "dp", axis=0, tiled=False)
    gathered = lax.dynamic_slice_in_dim(gathered, group_start, group_rows, 1)
    each_max = gathered[..., LATENT]
    part_max = jnp.max(each_max, axis=0)
    each_weight = jnp.exp(each_max - part_max[None])
    part_total = jnp.sum(gathered[..., LATENT + 1] * each_weight, axis=0)
    part_mix = jnp.sum(gathered[..., :LATENT] * each_weight[..., None], axis=0)
    own_normed = lax.dynamic_slice_in_dim(normed, group_start, group_rows, 0)
    own_position = lax.dynamic_slice_in_dim(position, group_start, group_rows, 0)
    fresh_latent = jnp.dot(own_normed, latent_down, preferred_element_type=jnp.float32)
    new_latent = rms_plain(fresh_latent[:, :LATENT]).astype(jnp.bfloat16)
    new_rope = rotary(fresh_latent[:, LATENT:], own_position).astype(jnp.bfloat16)
    own_query = lax.dynamic_slice_in_dim(query_latent, group_start, group_rows, 0)
    own_rope_query = lax.dynamic_slice_in_dim(query_rope, group_start, group_rows, 0)
    own_score = jnp.einsum("thl,tl->th", own_query, new_latent, preferred_element_type=jnp.float32)
    own_score = (
        own_score
        + jnp.einsum("thr,tr->th", own_rope_query, new_rope, preferred_element_type=jnp.float32)
    ) * score_scale
    highest = jnp.maximum(part_max, own_score)
    kept_part = jnp.exp(part_max - highest)
    own_weight = jnp.exp(own_score - highest)
    denominator = part_total * kept_part + own_weight
    numerator = (
        part_mix * kept_part[..., None]
        + own_weight[..., None] * new_latent.astype(jnp.float32)[:, None, :]
    )
    attended = (numerator / denominator[..., None]).astype(jnp.bfloat16)
    heads_out = jnp.einsum(
        "thl,lhv->thv", attended, up_table[..., NOPE:], preferred_element_type=jnp.float32
    )
    heads_out = heads_out.astype(jnp.bfloat16).reshape(group_rows, head_local * VHEAD)
    partial_value = jnp.dot(heads_out, out_weight, preferred_element_type=jnp.float32)
    partial_value, first_spread = lax.optimization_barrier((partial_value, first_spread))
    attn_out = scatter_sum(partial_value, "expert")
    residual = hidden.astype(jnp.float32) + attn_out
    normed_ffn = rms_norm(residual, ffn_gain).astype(jnp.bfloat16)
    slots_local = expert_gate_up.shape[0]
    ff_width = expert_gate_up.shape[2]
    col_width = expert_gate_up.shape[3]
    every_row = gather_rows(normed_ffn)
    spread = [first_spread]
    if len(chosen) > 1:
        every_row, second_chosen = lax.optimization_barrier((every_row, chosen[1]))
        spread.append(spread_slots(second_chosen, ex_count))
    my_columns = lax.dynamic_slice_in_dim(every_row, dp_index * col_width, col_width, 1)
    by_group = my_columns.reshape(dp_count, ex_count, req_local, col_width).transpose(1, 0, 2, 3)
    ffn_rows = by_group.reshape(requests, col_width)
    column_rows = lax.dynamic_index_in_dim(by_group, ex_index, 0, keepdims=False).reshape(
        dp_count * req_local, col_width
    )
    top_count = expert_ids.shape[1]
    experts_count = EXP_DEV * ex_count
    ids_order = (
        expert_ids.reshape(dp_count, ex_count, req_local, top_count)
        .transpose(1, 0, 2, 3)
        .reshape(requests, top_count)
    )
    gates_order = (
        expert_gates.reshape(dp_count, ex_count, req_local, top_count)
        .transpose(1, 0, 2, 3)
        .reshape(requests, top_count)
    )
    old_flat = old_place.reshape(-1)
    holds_map = old_flat[None, :] == jnp.arange(experts_count, dtype=jnp.int32)[:, None]
    holder = jnp.argmax(holds_map, axis=1)
    slot_of = holder[ids_order.reshape(-1)]
    capacity = 2 * requests * top_count // experts_count
    local_slot = slot_of - ex_index * slots_local
    slot_hot = local_slot[:, None] == jnp.arange(slots_local, dtype=jnp.int32)[None, :]
    slot_rank = jnp.cumsum(slot_hot.astype(jnp.int32), axis=0) - 1
    position_in = jnp.where(slot_hot, slot_rank, capacity)
    route_hot = (
        position_in[:, :, None] == jnp.arange(capacity, dtype=jnp.int32)[None, None, :]
    ).astype(jnp.float32)
    route_hot = route_hot.reshape(requests, top_count, slots_local, capacity)
    dispatch = jnp.sum(route_hot, axis=1).astype(jnp.bfloat16)
    combine = jnp.sum(route_hot * gates_order[:, :, None, None], axis=1)
    slot_inputs = jnp.einsum(
        "tsc,td->scd", dispatch, ffn_rows, preferred_element_type=jnp.float32
    ).astype(jnp.bfloat16)
    routed_part = jnp.einsum(
        "scd,sgfd->sgcf", slot_inputs, expert_gate_up, preferred_element_type=jnp.float32
    )
    shared_part = jnp.einsum(
        "td,gfd->gtf", column_rows, shared_gate_up, preferred_element_type=jnp.float32
    )
    routed_sum, shared_sum = sum_over(routed_part, "dp"), sum_over(shared_part, "dp")
    activated = (jax.nn.silu(routed_sum[:, 0]) * routed_sum[:, 1]).astype(jnp.bfloat16)
    slot_out = jnp.einsum(
        "scf,sfd->scd", activated, expert_down, preferred_element_type=jnp.float32
    )
    routed = jnp.einsum("tsc,scd->td", combine, slot_out, precision=HIGHEST)
    shared_act = (jax.nn.silu(shared_sum[0]) * shared_sum[1]).astype(jnp.bfloat16)
    shared_term = jnp.dot(shared_act, shared_down, preferred_element_type=jnp.float32)
    routed, spread = lax.optimization_barrier((routed, spread))
    moe_rows = scatter_sum(routed, "expert")
    moe_part = lax.all_to_all(moe_rows + shared_term, "dp", split_axis=0, concat_axis=1, tiled=True)
    layer_out = (residual + moe_part).astype(jnp.bfloat16)
    moved_gate_up, moved_down = migrate_finish(spread, plan, expert_gate_up, expert_down)
    return (layer_out, moved_gate_up, moved_down)


def solution(mesh):
    in_specs = (
        P(("dp", "expert"), None),
        P(),
        P("expert", None),
        P(),
        P(None, "expert"),
        P("expert", None),
        P("dp", None, None),
        P(),
        P(),
        P(),
        P(),
        P(),
        P(),
        P(),
        P("expert", None, None, "dp"),
        P("expert", None, "dp"),
        P(None, None, "dp"),
        P(None, "dp"),
    )
    out_specs = (P(("dp", "expert"), None), P("expert", None, None, "dp"), P("expert", None, "dp"))
    return jax.shard_map(local, mesh=mesh, in_specs=in_specs, out_specs=out_specs, check_vma=False)
```

```python
import math

import jax
import jax.numpy as jnp
from jax import lax
from jax.sharding import PartitionSpec as P

NOPE = 128
ROPE = 64
VHEAD = 128
LATENT = 512
EXP_DEV = 3
PAGE = 32


EPSILON = 1e-06
ROPE_BASE = 50000.0
MASKED_SCORE = -1e30
HIGHEST = lax.Precision.HIGHEST


def rms_plain(values):
    mean_square = jnp.mean(values * values, axis=-1, keepdims=True)
    return values * lax.rsqrt(mean_square + EPSILON)


def rms_norm(values, norm_gain):
    return rms_plain(values) * norm_gain


def rotary(values, position):
    half_width = values.shape[-1] // 2
    exponent = jnp.arange(half_width).astype(jnp.float32) * (2.0 / values.shape[-1])
    frequency = jnp.exp(-exponent * math.log(ROPE_BASE))
    angles = position[..., None] * frequency
    cosine = jnp.cos(angles)
    sine_part = jnp.sin(angles)
    first_half = values[..., :half_width]
    second = values[..., half_width:]
    return jnp.concatenate(
        [first_half * cosine - second * sine_part, second * cosine + first_half * sine_part],
        axis=-1,
    )


def gather_rows(rows):
    by_expert = lax.all_gather(rows, "expert", axis=0, tiled=True)
    return lax.all_gather(by_expert, "dp", axis=0, tiled=True)


def pick_rows(table, rows):
    return jnp.stack([lax.dynamic_index_in_dim(table, rows[k], 0, False) for k in range(rows.shape[0])])


def pick_slots(gate_up, down, picks):
    return jnp.concatenate([pick_rows(gate_up, picks), pick_rows(down, picks)[:, None]], axis=1)


def spread_slots(chosen, ex_count):
    count, parts, ff_width, col_width = chosen.shape
    pieces = chosen.reshape(count, parts, ex_count, ff_width // ex_count, col_width)
    spread = lax.all_to_all(pieces, "expert", split_axis=2, concat_axis=0, tiled=True)
    return spread.reshape(ex_count * count, parts, ff_width // ex_count, col_width)


def scatter_sum(values, axis):
    count = lax.axis_size(axis)
    share = values.shape[0] // count
    gathered = lax.all_gather(values, axis, axis=0, tiled=False)
    mine = lax.dynamic_slice_in_dim(gathered, lax.axis_index(axis) * share, share, 1)
    return jnp.sum(mine, axis=0)


def sum_over(values, axis):
    return jnp.sum(lax.all_gather(values, axis, axis=0, tiled=False), axis=0)


def migrate_start(expert_gate_up, expert_down, old_place, new_place, ex_index):
    rows, slots_local = old_place.shape
    slots = rows * slots_local
    ex_count = rows
    ff_width = expert_gate_up.shape[2]
    changed = old_place != new_place
    moved_slot = jnp.argmax(changed, axis=1)
    wanted = jnp.take_along_axis(new_place, moved_slot[:, None], axis=1)[:, 0]
    hit = old_place.reshape(-1)[None, :] == wanted[:, None]
    first = jnp.argmax(hit, axis=1).astype(jnp.int32)
    last = (slots - 1 - jnp.argmax(hit[:, ::-1], axis=1)).astype(jnp.int32)
    slot_ids = jnp.arange(slots, dtype=jnp.int32)

    def needed_of(src):
        needed = jnp.any(src[:, None] == slot_ids[None, :], axis=0).reshape(rows, slots_local)
        return needed, jnp.max(jnp.sum(needed.astype(jnp.int32), axis=1))

    need_first, load_first = needed_of(first)
    need_last, load_last = needed_of(last)
    use_last = load_last < load_first
    source = jnp.where(use_last, last, first)
    needed = jnp.where(use_last, need_last, need_first)
    load = jnp.minimum(load_first, load_last)
    rank = jnp.cumsum(needed.astype(jnp.int32), axis=1) - 1
    local_ids = jnp.arange(slots_local, dtype=jnp.int32)
    picks = jnp.stack(
        [jnp.argmax(needed & (rank == k), axis=1).astype(jnp.int32) for k in range(slots_local)],
        axis=1,
    )
    my_picks = picks[ex_index]
    src_dev = source // slots_local
    src_rank = rank.reshape(-1)[source]
    fast = min(2, slots_local)
    chosen = [pick_slots(expert_gate_up, expert_down, my_picks[k:k + 1]) for k in range(fast)]
    return chosen, (my_picks, src_dev, src_rank, load, moved_slot[ex_index])


def migrate_route(spread, plan, expert_gate_up, expert_down):
    my_picks, src_dev, src_rank, load, my_moved = plan
    ex_count = src_dev.shape[0]
    slots_local = expert_gate_up.shape[0]
    fast = len(spread)
    stacked = jnp.concatenate(spread, axis=0)
    out_a = pick_rows(stacked, jnp.minimum(src_rank, fast - 1) * ex_count + src_dev)
    if slots_local > fast:
        rest = slots_local - fast

        def extra():
            spread_b = spread_slots(pick_slots(expert_gate_up, expert_down, my_picks[fast:]), ex_count)
            out_b = pick_rows(spread_b, src_dev * rest + jnp.clip(src_rank - fast, 0, rest - 1))
            return jnp.where((src_rank < fast)[:, None, None, None], out_a, out_b)

        out_a = lax.cond(load > fast, extra, lambda: out_a)
    return out_a


def deliver(outgoing):
    return lax.all_to_all(outgoing, "expert", split_axis=0, concat_axis=2, tiled=True)


def local(
    hidden,
    attn_gain,
    query_weight,
    latent_down,
    latent_up,
    out_weight,
    latent_pool,
    page_table,
    page_counts,
    ffn_gain,
    expert_ids,
    expert_gates,
    old_place,
    new_place,
    expert_gate_up,
    expert_down,
    shared_gate_up,
    shared_down,
):
    dp_count = lax.axis_size("dp")
    ex_count = lax.axis_size("expert")
    dp_index = lax.axis_index("dp")
    ex_index = lax.axis_index("expert")
    req_local = hidden.shape[0]
    group_rows = req_local * ex_count
    requests = page_counts.shape[0]
    head_local = query_weight.shape[0] // (NOPE + ROPE)
    score_scale = (NOPE + ROPE) ** (-0.5)
    group_start = dp_index * group_rows
    chosen, plan = migrate_start(expert_gate_up, expert_down, old_place, new_place, ex_index)
    everyone = gather_rows(hidden)
    everyone, chosen = lax.optimization_barrier((everyone, chosen))
    spread = [spread_slots(part, ex_count) for part in chosen]
    normed = rms_norm(everyone.astype(jnp.float32), attn_gain).astype(jnp.bfloat16)
    queries = jnp.einsum(
        "td,qd->tq", normed, query_weight, preferred_element_type=jnp.float32
    ).reshape(requests, head_local, NOPE + ROPE)
    position = (page_counts * PAGE).astype(jnp.float32)
    query_rope = rotary(queries[..., NOPE:], position[:, None]).astype(jnp.bfloat16)
    up_table = latent_up.reshape(LATENT, head_local, NOPE + VHEAD)
    query_latent = jnp.einsum(
        "thn,lhn->thl",
        queries[..., :NOPE],
        up_table[..., :NOPE].astype(jnp.float32),
        precision=HIGHEST,
    ).astype(jnp.bfloat16)
    pages_local = latent_pool.shape[0]
    pool_total = pages_local * dp_count
    flat_pages = page_table.reshape(-1)
    flat_owner = jnp.repeat(jnp.arange(requests, dtype=jnp.int32), page_table.shape[1])
    target = jnp.where(flat_pages >= 0, flat_pages, pool_total)
    owner_all = jnp.full((pool_total,), -1, jnp.int32).at[target].set(flat_owner, mode="drop")
    page_owner = lax.dynamic_slice_in_dim(owner_all, dp_index * pages_local, pages_local)
    page_used = page_owner >= 0
    owner_safe = jnp.maximum(page_owner, 0)
    page_latent = latent_pool[..., :LATENT]
    page_rope = latent_pool[..., LATENT:]
    scores = jnp.einsum(
        "phl,pkl->phk", query_latent[owner_safe], page_latent, preferred_element_type=jnp.float32
    )
    scores = (
        scores
        + jnp.einsum(
            "phr,pkr->phk", query_rope[owner_safe], page_rope, preferred_element_type=jnp.float32
        )
    ) * score_scale
    raw_max = jnp.max(scores, axis=2)
    weights = jnp.exp(scores - raw_max[..., None])
    page_total = jnp.sum(weights, axis=2)
    page_mix = jnp.einsum(
        "phk,pkl->phl",
        weights.astype(jnp.bfloat16),
        page_latent,
        preferred_element_type=jnp.float32,
    )
    page_max = jnp.where(page_used[:, None], raw_max, MASKED_SCORE)
    member = page_owner[None, :] == jnp.arange(requests, dtype=jnp.int32)[:, None]
    req_max = jnp.max(jnp.where(member[:, :, None], page_max[None], MASKED_SCORE), axis=1)
    rescale = jnp.where(page_used[:, None], jnp.exp(page_max - req_max[owner_safe]), 0.0)
    member_float = member.astype(jnp.float32)
    req_total = jnp.dot(member_float, page_total * rescale, precision=HIGHEST)
    req_mix = jnp.einsum(
        "rp,phl->rhl", member_float, page_mix * rescale[..., None], precision=HIGHEST
    )
    packed = jnp.concatenate([req_mix, req_max[..., None], req_total[..., None]], axis=-1)
    gathered = lax.all_gather(packed, "dp", axis=0, tiled=False)
    gathered = lax.dynamic_slice_in_dim(gathered, group_start, group_rows, 1)
    each_max = gathered[..., LATENT]
    part_max = jnp.max(each_max, axis=0)
    each_weight = jnp.exp(each_max - part_max[None])
    part_total = jnp.sum(gathered[..., LATENT + 1] * each_weight, axis=0)
    part_mix = jnp.sum(gathered[..., :LATENT] * each_weight[..., None], axis=0)
    own_normed = lax.dynamic_slice_in_dim(normed, group_start, group_rows, 0)
    own_position = lax.dynamic_slice_in_dim(position, group_start, group_rows, 0)
    fresh_latent = jnp.dot(own_normed, latent_down, preferred_element_type=jnp.float32)
    new_latent = rms_plain(fresh_latent[:, :LATENT]).astype(jnp.bfloat16)
    new_rope = rotary(fresh_latent[:, LATENT:], own_position).astype(jnp.bfloat16)
    own_query = lax.dynamic_slice_in_dim(query_latent, group_start, group_rows, 0)
    own_rope_query = lax.dynamic_slice_in_dim(query_rope, group_start, group_rows, 0)
    own_score = jnp.einsum("thl,tl->th", own_query, new_latent, preferred_element_type=jnp.float32)
    own_score = (
        own_score
        + jnp.einsum("thr,tr->th", own_rope_query, new_rope, preferred_element_type=jnp.float32)
    ) * score_scale
    highest = jnp.maximum(part_max, own_score)
    kept_part = jnp.exp(part_max - highest)
    own_weight = jnp.exp(own_score - highest)
    denominator = part_total * kept_part + own_weight
    numerator = (
        part_mix * kept_part[..., None]
        + own_weight[..., None] * new_latent.astype(jnp.float32)[:, None, :]
    )
    attended = (numerator / denominator[..., None]).astype(jnp.bfloat16)
    heads_out = jnp.einsum(
        "thl,lhv->thv", attended, up_table[..., NOPE:], preferred_element_type=jnp.float32
    )
    heads_out = heads_out.astype(jnp.bfloat16).reshape(group_rows, head_local * VHEAD)
    partial_value = jnp.dot(heads_out, out_weight, preferred_element_type=jnp.float32)
    partial_value, spread = lax.optimization_barrier((partial_value, spread))
    attn_out = scatter_sum(partial_value, "expert")
    residual = hidden.astype(jnp.float32) + attn_out
    normed_ffn = rms_norm(residual, ffn_gain).astype(jnp.bfloat16)
    slots_local = expert_gate_up.shape[0]
    ff_width = expert_gate_up.shape[2]
    col_width = expert_gate_up.shape[3]
    every_row = gather_rows(normed_ffn)
    outgoing = migrate_route(spread, plan, expert_gate_up, expert_down)
    every_row, outgoing = lax.optimization_barrier((every_row, outgoing))
    unit = (every_row[0, 0].astype(jnp.float32) * 0.0 + 1.0).astype(expert_gate_up.dtype)
    base_gate_up = expert_gate_up * unit
    base_down = expert_down * unit
    arrived = deliver(outgoing)
    my_columns = lax.dynamic_slice_in_dim(every_row, dp_index * col_width, col_width, 1)
    by_group = my_columns.reshape(dp_count, ex_count, req_local, col_width).transpose(1, 0, 2, 3)
    ffn_rows = by_group.reshape(requests, col_width)
    column_rows = lax.dynamic_index_in_dim(by_group, ex_index, 0, keepdims=False).reshape(
        dp_count * req_local, col_width
    )
    top_count = expert_ids.shape[1]
    experts_count = EXP_DEV * ex_count
    ids_order = (
        expert_ids.reshape(dp_count, ex_count, req_local, top_count)
        .transpose(1, 0, 2, 3)
        .reshape(requests, top_count)
    )
    gates_order = (
        expert_gates.reshape(dp_count, ex_count, req_local, top_count)
        .transpose(1, 0, 2, 3)
        .reshape(requests, top_count)
    )
    old_flat = old_place.reshape(-1)
    holds_map = old_flat[None, :] == jnp.arange(experts_count, dtype=jnp.int32)[:, None]
    holder = jnp.argmax(holds_map, axis=1)
    slot_of = holder[ids_order.reshape(-1)]
    capacity = 2 * requests * top_count // experts_count
    local_slot = slot_of - ex_index * slots_local
    slot_hot = local_slot[:, None] == jnp.arange(slots_local, dtype=jnp.int32)[None, :]
    slot_rank = jnp.cumsum(slot_hot.astype(jnp.int32), axis=0) - 1
    position_in = jnp.where(slot_hot, slot_rank, capacity)
    route_hot = (
        position_in[:, :, None] == jnp.arange(capacity, dtype=jnp.int32)[None, None, :]
    ).astype(jnp.float32)
    route_hot = route_hot.reshape(requests, top_count, slots_local, capacity)
    dispatch = jnp.sum(route_hot, axis=1).astype(jnp.bfloat16)
    combine = jnp.sum(route_hot * gates_order[:, :, None, None], axis=1)
    slot_inputs = jnp.einsum(
        "tsc,td->scd", dispatch, ffn_rows, preferred_element_type=jnp.float32
    ).astype(jnp.bfloat16)
    routed_part = jnp.einsum(
        "scd,sgfd->sgcf", slot_inputs, expert_gate_up, preferred_element_type=jnp.float32
    )
    shared_part = jnp.einsum(
        "td,gfd->gtf", column_rows, shared_gate_up, preferred_element_type=jnp.float32
    )
    routed_sum, shared_sum = sum_over(routed_part, "dp"), sum_over(shared_part, "dp")
    activated = (jax.nn.silu(routed_sum[:, 0]) * routed_sum[:, 1]).astype(jnp.bfloat16)
    slot_out = jnp.einsum(
        "scf,sfd->scd", activated, expert_down, preferred_element_type=jnp.float32
    )
    routed = jnp.einsum("tsc,scd->td", combine, slot_out, precision=HIGHEST)
    shared_act = (jax.nn.silu(shared_sum[0]) * shared_sum[1]).astype(jnp.bfloat16)
    shared_term = jnp.dot(shared_act, shared_down, preferred_element_type=jnp.float32)
    routed, arrived = lax.optimization_barrier((routed, arrived))
    moe_rows = scatter_sum(routed, "expert")
    moe_part = lax.all_to_all(moe_rows + shared_term, "dp", split_axis=0, concat_axis=1, tiled=True)
    layer_out = (residual + moe_part).astype(jnp.bfloat16)
    my_moved = plan[-1]
    moved_gate_up = lax.dynamic_update_index_in_dim(base_gate_up, arrived[0, :2], my_moved, 0)
    moved_down = lax.dynamic_update_index_in_dim(base_down, arrived[0, 2], my_moved, 0)
    return (layer_out, moved_gate_up, moved_down)


def solution(mesh):
    in_specs = (
        P(("dp", "expert"), None),
        P(),
        P("expert", None),
        P(),
        P(None, "expert"),
        P("expert", None),
        P("dp", None, None),
        P(),
        P(),
        P(),
        P(),
        P(),
        P(),
        P(),
        P("expert", None, None, "dp"),
        P("expert", None, "dp"),
        P(None, None, "dp"),
        P(None, "dp"),
    )
    out_specs = (P(("dp", "expert"), None), P("expert", None, None, "dp"), P("expert", None, "dp"))
    return jax.shard_map(local, mesh=mesh, in_specs=in_specs, out_specs=out_specs, check_vma=False)
```

```python
import math

import jax
import jax.numpy as jnp
from jax import lax
from jax.sharding import PartitionSpec as P

NOPE = 128
ROPE = 64
VHEAD = 128
LATENT = 512
EXP_DEV = 3
PAGE = 32


EPSILON = 1e-06
ROPE_BASE = 50000.0
MASKED_SCORE = -1e30
HIGHEST = lax.Precision.HIGHEST


def rms_plain(values):
    mean_square = jnp.mean(values * values, axis=-1, keepdims=True)
    return values * lax.rsqrt(mean_square + EPSILON)


def rms_norm(values, norm_gain):
    return rms_plain(values) * norm_gain


def rotary(values, position):
    half_width = values.shape[-1] // 2
    exponent = jnp.arange(half_width).astype(jnp.float32) * (2.0 / values.shape[-1])
    frequency = jnp.exp(-exponent * math.log(ROPE_BASE))
    angles = position[..., None] * frequency
    cosine = jnp.cos(angles)
    sine_part = jnp.sin(angles)
    first_half = values[..., :half_width]
    second = values[..., half_width:]
    return jnp.concatenate(
        [first_half * cosine - second * sine_part, second * cosine + first_half * sine_part],
        axis=-1,
    )


def gather_rows(rows):
    by_expert = lax.all_gather(rows, "expert", axis=0, tiled=True)
    return lax.all_gather(by_expert, "dp", axis=0, tiled=True)


def pick_rows(table, rows):
    return jnp.stack([lax.dynamic_index_in_dim(table, rows[k], 0, False) for k in range(rows.shape[0])])


def pick_slots(gate_up, down, picks):
    return jnp.concatenate([pick_rows(gate_up, picks), pick_rows(down, picks)[:, None]], axis=1)


def spread_slots(chosen, ex_count):
    count, parts, ff_width, col_width = chosen.shape
    pieces = chosen.reshape(count, parts, ex_count, ff_width // ex_count, col_width)
    spread = lax.all_to_all(pieces, "expert", split_axis=2, concat_axis=0, tiled=True)
    return spread.reshape(ex_count * count, parts, ff_width // ex_count, col_width)


def scatter_sum(values, axis):
    count = lax.axis_size(axis)
    share = values.shape[0] // count
    gathered = lax.all_gather(values, axis, axis=0, tiled=False)
    mine = lax.dynamic_slice_in_dim(gathered, lax.axis_index(axis) * share, share, 1)
    return jnp.sum(mine, axis=0)


def sum_over(values, axis):
    return jnp.sum(lax.all_gather(values, axis, axis=0, tiled=False), axis=0)


def migrate_start(expert_gate_up, expert_down, old_place, new_place, ex_index):
    rows, slots_local = old_place.shape
    slots = rows * slots_local
    ex_count = rows
    ff_width = expert_gate_up.shape[2]
    changed = old_place != new_place
    moved_slot = jnp.argmax(changed, axis=1)
    wanted = jnp.take_along_axis(new_place, moved_slot[:, None], axis=1)[:, 0]
    hit = old_place.reshape(-1)[None, :] == wanted[:, None]
    first = jnp.argmax(hit, axis=1).astype(jnp.int32)
    last = (slots - 1 - jnp.argmax(hit[:, ::-1], axis=1)).astype(jnp.int32)
    slot_ids = jnp.arange(slots, dtype=jnp.int32)

    def needed_of(src):
        needed = jnp.any(src[:, None] == slot_ids[None, :], axis=0).reshape(rows, slots_local)
        return needed, jnp.max(jnp.sum(needed.astype(jnp.int32), axis=1))

    need_first, load_first = needed_of(first)
    need_last, load_last = needed_of(last)
    use_last = load_last < load_first
    source = jnp.where(use_last, last, first)
    needed = jnp.where(use_last, need_last, need_first)
    load = jnp.minimum(load_first, load_last)
    rank = jnp.cumsum(needed.astype(jnp.int32), axis=1) - 1
    local_ids = jnp.arange(slots_local, dtype=jnp.int32)
    picks = jnp.stack(
        [jnp.argmax(needed & (rank == k), axis=1).astype(jnp.int32) for k in range(slots_local)],
        axis=1,
    )
    my_picks = picks[ex_index]
    src_dev = source // slots_local
    src_rank = rank.reshape(-1)[source]
    fast = min(2, slots_local)
    chosen = pick_slots(expert_gate_up, expert_down, my_picks[:fast])
    return chosen, (my_picks, src_dev, src_rank, load, moved_slot[ex_index])


def migrate_route(spread, plan, expert_gate_up, expert_down):
    my_picks, src_dev, src_rank, load, my_moved = plan
    ex_count = src_dev.shape[0]
    slots_local = expert_gate_up.shape[0]
    fast = spread.shape[0] // ex_count
    out_a = pick_rows(spread, src_dev * fast + jnp.minimum(src_rank, fast - 1))
    if slots_local > fast:
        rest = slots_local - fast

        def extra():
            spread_b = spread_slots(pick_slots(expert_gate_up, expert_down, my_picks[fast:]), ex_count)
            out_b = pick_rows(spread_b, src_dev * rest + jnp.clip(src_rank - fast, 0, rest - 1))
            return jnp.where((src_rank < fast)[:, None, None, None], out_a, out_b)

        out_a = lax.cond(load > fast, extra, lambda: out_a)
    return out_a


def deliver(outgoing):
    return lax.all_to_all(outgoing, "expert", split_axis=0, concat_axis=2, tiled=True)


def local(
    hidden,
    attn_gain,
    query_weight,
    latent_down,
    latent_up,
    out_weight,
    latent_pool,
    page_table,
    page_counts,
    ffn_gain,
    expert_ids,
    expert_gates,
    old_place,
    new_place,
    expert_gate_up,
    expert_down,
    shared_gate_up,
    shared_down,
):
    dp_count = lax.axis_size("dp")
    ex_count = lax.axis_size("expert")
    dp_index = lax.axis_index("dp")
    ex_index = lax.axis_index("expert")
    req_local = hidden.shape[0]
    group_rows = req_local * ex_count
    requests = page_counts.shape[0]
    head_local = query_weight.shape[0] // (NOPE + ROPE)
    score_scale = (NOPE + ROPE) ** (-0.5)
    group_start = dp_index * group_rows
    chosen, plan = migrate_start(expert_gate_up, expert_down, old_place, new_place, ex_index)
    everyone = gather_rows(hidden)
    everyone, chosen = lax.optimization_barrier((everyone, chosen))
    spread = spread_slots(chosen, ex_count)
    normed = rms_norm(everyone.astype(jnp.float32), attn_gain).astype(jnp.bfloat16)
    queries = jnp.einsum(
        "td,qd->tq", normed, query_weight, preferred_element_type=jnp.float32
    ).reshape(requests, head_local, NOPE + ROPE)
    position = (page_counts * PAGE).astype(jnp.float32)
    query_rope = rotary(queries[..., NOPE:], position[:, None]).astype(jnp.bfloat16)
    up_table = latent_up.reshape(LATENT, head_local, NOPE + VHEAD)
    query_latent = jnp.einsum(
        "thn,lhn->thl",
        queries[..., :NOPE],
        up_table[..., :NOPE].astype(jnp.float32),
        precision=HIGHEST,
    ).astype(jnp.bfloat16)
    pages_local = latent_pool.shape[0]
    pool_total = pages_local * dp_count
    flat_pages = page_table.reshape(-1)
    flat_owner = jnp.repeat(jnp.arange(requests, dtype=jnp.int32), page_table.shape[1])
    target = jnp.where(flat_pages >= 0, flat_pages, pool_total)
    owner_all = jnp.full((pool_total,), -1, jnp.int32).at[target].set(flat_owner, mode="drop")
    page_owner = lax.dynamic_slice_in_dim(owner_all, dp_index * pages_local, pages_local)
    page_used = page_owner >= 0
    owner_safe = jnp.maximum(page_owner, 0)
    page_latent = latent_pool[..., :LATENT]
    page_rope = latent_pool[..., LATENT:]
    scores = jnp.einsum(
        "phl,pkl->phk", query_latent[owner_safe], page_latent, preferred_element_type=jnp.float32
    )
    scores = (
        scores
        + jnp.einsum(
            "phr,pkr->phk", query_rope[owner_safe], page_rope, preferred_element_type=jnp.float32
        )
    ) * score_scale
    raw_max = jnp.max(scores, axis=2)
    weights = jnp.exp(scores - raw_max[..., None])
    page_total = jnp.sum(weights, axis=2)
    page_mix = jnp.einsum(
        "phk,pkl->phl",
        weights.astype(jnp.bfloat16),
        page_latent,
        preferred_element_type=jnp.float32,
    )
    page_max = jnp.where(page_used[:, None], raw_max, MASKED_SCORE)
    member = page_owner[None, :] == jnp.arange(requests, dtype=jnp.int32)[:, None]
    req_max = jnp.max(jnp.where(member[:, :, None], page_max[None], MASKED_SCORE), axis=1)
    rescale = jnp.where(page_used[:, None], jnp.exp(page_max - req_max[owner_safe]), 0.0)
    member_float = member.astype(jnp.float32)
    req_total = jnp.dot(member_float, page_total * rescale, precision=HIGHEST)
    req_mix = jnp.einsum(
        "rp,phl->rhl", member_float, page_mix * rescale[..., None], precision=HIGHEST
    )
    packed = jnp.concatenate([req_mix, req_max[..., None], req_total[..., None]], axis=-1)
    gathered = lax.all_gather(packed, "dp", axis=0, tiled=False)
    gathered = lax.dynamic_slice_in_dim(gathered, group_start, group_rows, 1)
    each_max = gathered[..., LATENT]
    part_max = jnp.max(each_max, axis=0)
    each_weight = jnp.exp(each_max - part_max[None])
    part_total = jnp.sum(gathered[..., LATENT + 1] * each_weight, axis=0)
    part_mix = jnp.sum(gathered[..., :LATENT] * each_weight[..., None], axis=0)
    own_normed = lax.dynamic_slice_in_dim(normed, group_start, group_rows, 0)
    own_position = lax.dynamic_slice_in_dim(position, group_start, group_rows, 0)
    fresh_latent = jnp.dot(own_normed, latent_down, preferred_element_type=jnp.float32)
    new_latent = rms_plain(fresh_latent[:, :LATENT]).astype(jnp.bfloat16)
    new_rope = rotary(fresh_latent[:, LATENT:], own_position).astype(jnp.bfloat16)
    own_query = lax.dynamic_slice_in_dim(query_latent, group_start, group_rows, 0)
    own_rope_query = lax.dynamic_slice_in_dim(query_rope, group_start, group_rows, 0)
    own_score = jnp.einsum("thl,tl->th", own_query, new_latent, preferred_element_type=jnp.float32)
    own_score = (
        own_score
        + jnp.einsum("thr,tr->th", own_rope_query, new_rope, preferred_element_type=jnp.float32)
    ) * score_scale
    highest = jnp.maximum(part_max, own_score)
    kept_part = jnp.exp(part_max - highest)
    own_weight = jnp.exp(own_score - highest)
    denominator = part_total * kept_part + own_weight
    numerator = (
        part_mix * kept_part[..., None]
        + own_weight[..., None] * new_latent.astype(jnp.float32)[:, None, :]
    )
    attended = (numerator / denominator[..., None]).astype(jnp.bfloat16)
    heads_out = jnp.einsum(
        "thl,lhv->thv", attended, up_table[..., NOPE:], preferred_element_type=jnp.float32
    )
    heads_out = heads_out.astype(jnp.bfloat16).reshape(group_rows, head_local * VHEAD)
    partial_value = jnp.dot(heads_out, out_weight, preferred_element_type=jnp.float32)
    partial_value, spread = lax.optimization_barrier((partial_value, spread))
    attn_group = jnp.sum(lax.all_gather(partial_value, "expert", axis=0, tiled=False), axis=0)
    group_hidden = lax.dynamic_slice_in_dim(everyone, group_start, group_rows, 0)
    group_residual = group_hidden.astype(jnp.float32) + attn_group
    residual = lax.dynamic_slice_in_dim(group_residual, ex_index * req_local, req_local, 0)
    normed_group = rms_norm(group_residual, ffn_gain).astype(jnp.bfloat16)
    slots_local = expert_gate_up.shape[0]
    ff_width = expert_gate_up.shape[2]
    col_width = expert_gate_up.shape[3]
    every_row = lax.all_gather(normed_group, "dp", axis=0, tiled=True)
    outgoing = migrate_route(spread, plan, expert_gate_up, expert_down)
    every_row, outgoing = lax.optimization_barrier((every_row, outgoing))
    unit = (every_row[0, 0].astype(jnp.float32) * 0.0 + 1.0).astype(expert_gate_up.dtype)
    base_gate_up = expert_gate_up * unit
    base_down = expert_down * unit
    arrived = deliver(outgoing)
    my_columns = lax.dynamic_slice_in_dim(every_row, dp_index * col_width, col_width, 1)
    by_group = my_columns.reshape(dp_count, ex_count, req_local, col_width).transpose(1, 0, 2, 3)
    ffn_rows = by_group.reshape(requests, col_width)
    column_rows = lax.dynamic_index_in_dim(by_group, ex_index, 0, keepdims=False).reshape(
        dp_count * req_local, col_width
    )
    top_count = expert_ids.shape[1]
    experts_count = EXP_DEV * ex_count
    ids_order = (
        expert_ids.reshape(dp_count, ex_count, req_local, top_count)
        .transpose(1, 0, 2, 3)
        .reshape(requests, top_count)
    )
    gates_order = (
        expert_gates.reshape(dp_count, ex_count, req_local, top_count)
        .transpose(1, 0, 2, 3)
        .reshape(requests, top_count)
    )
    old_flat = old_place.reshape(-1)
    holds_map = old_flat[None, :] == jnp.arange(experts_count, dtype=jnp.int32)[:, None]
    holder = jnp.argmax(holds_map, axis=1)
    slot_of = holder[ids_order.reshape(-1)]
    capacity = 2 * requests * top_count // experts_count
    local_slot = slot_of - ex_index * slots_local
    slot_hot = local_slot[:, None] == jnp.arange(slots_local, dtype=jnp.int32)[None, :]
    slot_rank = jnp.cumsum(slot_hot.astype(jnp.int32), axis=0) - 1
    position_in = jnp.where(slot_hot, slot_rank, capacity)
    route_hot = (
        position_in[:, :, None] == jnp.arange(capacity, dtype=jnp.int32)[None, None, :]
    ).astype(jnp.float32)
    route_hot = route_hot.reshape(requests, top_count, slots_local, capacity)
    dispatch = jnp.sum(route_hot, axis=1).astype(jnp.bfloat16)
    combine = jnp.sum(route_hot * gates_order[:, :, None, None], axis=1)
    slot_inputs = jnp.einsum(
        "tsc,td->scd", dispatch, ffn_rows, preferred_element_type=jnp.float32
    ).astype(jnp.bfloat16)
    routed_part = jnp.einsum(
        "scd,sgfd->sgcf", slot_inputs, expert_gate_up, preferred_element_type=jnp.float32
    )
    shared_part = jnp.einsum(
        "td,gfd->gtf", column_rows, shared_gate_up, preferred_element_type=jnp.float32
    )
    routed_sum, shared_sum = sum_over(routed_part, "dp"), sum_over(shared_part, "dp")
    activated = (jax.nn.silu(routed_sum[:, 0]) * routed_sum[:, 1]).astype(jnp.bfloat16)
    slot_out = jnp.einsum(
        "scf,sfd->scd", activated, expert_down, preferred_element_type=jnp.float32
    )
    routed = jnp.einsum("tsc,scd->td", combine, slot_out, precision=HIGHEST)
    shared_act = (jax.nn.silu(shared_sum[0]) * shared_sum[1]).astype(jnp.bfloat16)
    shared_term = jnp.dot(shared_act, shared_down, preferred_element_type=jnp.float32)
    routed, arrived = lax.optimization_barrier((routed, arrived))
    moe_rows = scatter_sum(routed, "expert")
    moe_part = lax.all_to_all(moe_rows + shared_term, "dp", split_axis=0, concat_axis=1, tiled=True)
    layer_out = (residual + moe_part).astype(jnp.bfloat16)
    my_moved = plan[-1]
    moved_gate_up = lax.dynamic_update_index_in_dim(base_gate_up, arrived[0, :2], my_moved, 0)
    moved_down = lax.dynamic_update_index_in_dim(base_down, arrived[0, 2], my_moved, 0)
    return (layer_out, moved_gate_up, moved_down)


def solution(mesh):
    in_specs = (
        P(("dp", "expert"), None),
        P(),
        P("expert", None),
        P(),
        P(None, "expert"),
        P("expert", None),
        P("dp", None, None),
        P(),
        P(),
        P(),
        P(),
        P(),
        P(),
        P(),
        P("expert", None, None, "dp"),
        P("expert", None, "dp"),
        P(None, None, "dp"),
        P(None, "dp"),
    )
    out_specs = (P(("dp", "expert"), None), P("expert", None, None, "dp"), P("expert", None, "dp"))
    return jax.shard_map(local, mesh=mesh, in_specs=in_specs, out_specs=out_specs, check_vma=False)
```

```python
import math

import jax
import jax.numpy as jnp
from jax import lax
from jax.sharding import PartitionSpec as P

NOPE = 128
ROPE = 64
VHEAD = 128
LATENT = 512
EXP_DEV = 3
PAGE = 32


EPSILON = 1e-06
ROPE_BASE = 50000.0
MASKED_SCORE = -1e30
HIGHEST = lax.Precision.HIGHEST


def rms_plain(values):
    mean_square = jnp.mean(values * values, axis=-1, keepdims=True)
    return values * lax.rsqrt(mean_square + EPSILON)


def rms_norm(values, norm_gain):
    return rms_plain(values) * norm_gain


def rotary(values, position):
    half_width = values.shape[-1] // 2
    exponent = jnp.arange(half_width).astype(jnp.float32) * (2.0 / values.shape[-1])
    frequency = jnp.exp(-exponent * math.log(ROPE_BASE))
    angles = position[..., None] * frequency
    cosine = jnp.cos(angles)
    sine_part = jnp.sin(angles)
    first_half = values[..., :half_width]
    second = values[..., half_width:]
    return jnp.concatenate(
        [first_half * cosine - second * sine_part, second * cosine + first_half * sine_part],
        axis=-1,
    )


def gather_rows(rows):
    by_expert = lax.all_gather(rows, "expert", axis=0, tiled=True)
    return lax.all_gather(by_expert, "dp", axis=0, tiled=True)


def pick_rows(table, rows):
    return jnp.stack([lax.dynamic_index_in_dim(table, rows[k], 0, False) for k in range(rows.shape[0])])


def pick_slots(gate_up, down, picks):
    return jnp.concatenate([pick_rows(gate_up, picks), pick_rows(down, picks)[:, None]], axis=1)


def spread_slots(chosen, ex_count):
    count, parts, ff_width, col_width = chosen.shape
    pieces = chosen.reshape(count, parts, ex_count, ff_width // ex_count, col_width)
    pieces = pieces.transpose(2, 0, 1, 3, 4)
    spread = lax.all_to_all(pieces, "expert", split_axis=0, concat_axis=0, tiled=True)
    return spread.reshape(ex_count * count, parts, ff_width // ex_count, col_width)


def scatter_sum(values, axis):
    count = lax.axis_size(axis)
    share = values.shape[0] // count
    gathered = lax.all_gather(values, axis, axis=0, tiled=False)
    mine = lax.dynamic_slice_in_dim(gathered, lax.axis_index(axis) * share, share, 1)
    return jnp.sum(mine, axis=0)


def sum_over(values, axis):
    return jnp.sum(lax.all_gather(values, axis, axis=0, tiled=False), axis=0)


def migrate_start(expert_gate_up, expert_down, old_place, new_place, ex_index):
    rows, slots_local = old_place.shape
    slots = rows * slots_local
    ex_count = rows
    ff_width = expert_gate_up.shape[2]
    changed = old_place != new_place
    moved_slot = jnp.argmax(changed, axis=1)
    wanted = jnp.take_along_axis(new_place, moved_slot[:, None], axis=1)[:, 0]
    hit = old_place.reshape(-1)[None, :] == wanted[:, None]
    first = jnp.argmax(hit, axis=1).astype(jnp.int32)
    last = (slots - 1 - jnp.argmax(hit[:, ::-1], axis=1)).astype(jnp.int32)
    slot_ids = jnp.arange(slots, dtype=jnp.int32)

    def needed_of(src):
        needed = jnp.any(src[:, None] == slot_ids[None, :], axis=0).reshape(rows, slots_local)
        return needed, jnp.max(jnp.sum(needed.astype(jnp.int32), axis=1))

    need_first, load_first = needed_of(first)
    need_last, load_last = needed_of(last)
    use_last = load_last < load_first
    source = jnp.where(use_last, last, first)
    needed = jnp.where(use_last, need_last, need_first)
    load = jnp.minimum(load_first, load_last)
    rank = jnp.cumsum(needed.astype(jnp.int32), axis=1) - 1
    local_ids = jnp.arange(slots_local, dtype=jnp.int32)
    picks = jnp.stack(
        [jnp.argmax(needed & (rank == k), axis=1).astype(jnp.int32) for k in range(slots_local)],
        axis=1,
    )
    my_picks = picks[ex_index]
    src_dev = source // slots_local
    src_rank = rank.reshape(-1)[source]
    fast = min(2, slots_local)
    chosen = pick_slots(expert_gate_up, expert_down, my_picks[:fast])
    return chosen, (my_picks, src_dev, src_rank, load, moved_slot[ex_index])


def migrate_route(spread, plan, expert_gate_up, expert_down):
    my_picks, src_dev, src_rank, load, my_moved = plan
    ex_count = src_dev.shape[0]
    slots_local = expert_gate_up.shape[0]
    fast = spread.shape[0] // ex_count
    out_a = pick_rows(spread, src_dev * fast + jnp.minimum(src_rank, fast - 1))
    if slots_local > fast:
        rest = slots_local - fast

        def extra():
            spread_b = spread_slots(pick_slots(expert_gate_up, expert_down, my_picks[fast:]), ex_count)
            out_b = pick_rows(spread_b, src_dev * rest + jnp.clip(src_rank - fast, 0, rest - 1))
            return jnp.where((src_rank < fast)[:, None, None, None], out_a, out_b)

        out_a = lax.cond(load > fast, extra, lambda: out_a)
    return out_a


def deliver(outgoing):
    return lax.all_to_all(outgoing, "expert", split_axis=0, concat_axis=2, tiled=True)


def local(
    hidden,
    attn_gain,
    query_weight,
    latent_down,
    latent_up,
    out_weight,
    latent_pool,
    page_table,
    page_counts,
    ffn_gain,
    expert_ids,
    expert_gates,
    old_place,
    new_place,
    expert_gate_up,
    expert_down,
    shared_gate_up,
    shared_down,
):
    dp_count = lax.axis_size("dp")
    ex_count = lax.axis_size("expert")
    dp_index = lax.axis_index("dp")
    ex_index = lax.axis_index("expert")
    req_local = hidden.shape[0]
    group_rows = req_local * ex_count
    requests = page_counts.shape[0]
    head_local = query_weight.shape[0] // (NOPE + ROPE)
    score_scale = (NOPE + ROPE) ** (-0.5)
    group_start = dp_index * group_rows
    chosen, plan = migrate_start(expert_gate_up, expert_down, old_place, new_place, ex_index)
    everyone = gather_rows(hidden)
    everyone, chosen = lax.optimization_barrier((everyone, chosen))
    spread = spread_slots(chosen, ex_count)
    normed = rms_norm(everyone.astype(jnp.float32), attn_gain).astype(jnp.bfloat16)
    queries = jnp.einsum(
        "td,qd->tq", normed, query_weight, preferred_element_type=jnp.float32
    ).reshape(requests, head_local, NOPE + ROPE)
    position = (page_counts * PAGE).astype(jnp.float32)
    query_rope = rotary(queries[..., NOPE:], position[:, None]).astype(jnp.bfloat16)
    up_table = latent_up.reshape(LATENT, head_local, NOPE + VHEAD)
    query_latent = jnp.einsum(
        "thn,lhn->thl",
        queries[..., :NOPE],
        up_table[..., :NOPE].astype(jnp.float32),
        precision=HIGHEST,
    ).astype(jnp.bfloat16)
    pages_local = latent_pool.shape[0]
    pool_total = pages_local * dp_count
    flat_pages = page_table.reshape(-1)
    flat_owner = jnp.repeat(jnp.arange(requests, dtype=jnp.int32), page_table.shape[1])
    target = jnp.where(flat_pages >= 0, flat_pages, pool_total)
    owner_all = jnp.full((pool_total,), -1, jnp.int32).at[target].set(flat_owner, mode="drop")
    page_owner = lax.dynamic_slice_in_dim(owner_all, dp_index * pages_local, pages_local)
    page_used = page_owner >= 0
    owner_safe = jnp.maximum(page_owner, 0)
    page_latent = latent_pool[..., :LATENT]
    page_rope = latent_pool[..., LATENT:]
    scores = jnp.einsum(
        "phl,pkl->phk", query_latent[owner_safe], page_latent, preferred_element_type=jnp.float32
    )
    scores = (
        scores
        + jnp.einsum(
            "phr,pkr->phk", query_rope[owner_safe], page_rope, preferred_element_type=jnp.float32
        )
    ) * score_scale
    raw_max = jnp.max(scores, axis=2)
    weights = jnp.exp(scores - raw_max[..., None])
    page_total = jnp.sum(weights, axis=2)
    page_mix = jnp.einsum(
        "phk,pkl->phl",
        weights.astype(jnp.bfloat16),
        page_latent,
        preferred_element_type=jnp.float32,
    )
    page_max = jnp.where(page_used[:, None], raw_max, MASKED_SCORE)
    member = page_owner[None, :] == jnp.arange(requests, dtype=jnp.int32)[:, None]
    req_max = jnp.max(jnp.where(member[:, :, None], page_max[None], MASKED_SCORE), axis=1)
    rescale = jnp.where(page_used[:, None], jnp.exp(page_max - req_max[owner_safe]), 0.0)
    member_float = member.astype(jnp.float32)
    req_total = jnp.dot(member_float, page_total * rescale, precision=HIGHEST)
    req_mix = jnp.einsum(
        "rp,phl->rhl", member_float, page_mix * rescale[..., None], precision=HIGHEST
    )
    packed = jnp.concatenate([req_mix, req_max[..., None], req_total[..., None]], axis=-1)
    gathered = lax.all_gather(packed, "dp", axis=0, tiled=False)
    gathered = lax.dynamic_slice_in_dim(gathered, group_start, group_rows, 1)
    each_max = gathered[..., LATENT]
    part_max = jnp.max(each_max, axis=0)
    each_weight = jnp.exp(each_max - part_max[None])
    part_total = jnp.sum(gathered[..., LATENT + 1] * each_weight, axis=0)
    part_mix = jnp.sum(gathered[..., :LATENT] * each_weight[..., None], axis=0)
    own_normed = lax.dynamic_slice_in_dim(normed, group_start, group_rows, 0)
    own_position = lax.dynamic_slice_in_dim(position, group_start, group_rows, 0)
    fresh_latent = jnp.dot(own_normed, latent_down, preferred_element_type=jnp.float32)
    new_latent = rms_plain(fresh_latent[:, :LATENT]).astype(jnp.bfloat16)
    new_rope = rotary(fresh_latent[:, LATENT:], own_position).astype(jnp.bfloat16)
    own_query = lax.dynamic_slice_in_dim(query_latent, group_start, group_rows, 0)
    own_rope_query = lax.dynamic_slice_in_dim(query_rope, group_start, group_rows, 0)
    own_score = jnp.einsum("thl,tl->th", own_query, new_latent, preferred_element_type=jnp.float32)
    own_score = (
        own_score
        + jnp.einsum("thr,tr->th", own_rope_query, new_rope, preferred_element_type=jnp.float32)
    ) * score_scale
    highest = jnp.maximum(part_max, own_score)
    kept_part = jnp.exp(part_max - highest)
    own_weight = jnp.exp(own_score - highest)
    denominator = part_total * kept_part + own_weight
    numerator = (
        part_mix * kept_part[..., None]
        + own_weight[..., None] * new_latent.astype(jnp.float32)[:, None, :]
    )
    attended = (numerator / denominator[..., None]).astype(jnp.bfloat16)
    heads_out = jnp.einsum(
        "thl,lhv->thv", attended, up_table[..., NOPE:], preferred_element_type=jnp.float32
    )
    heads_out = heads_out.astype(jnp.bfloat16).reshape(group_rows, head_local * VHEAD)
    partial_value = jnp.dot(heads_out, out_weight, preferred_element_type=jnp.float32)
    partial_value, spread = lax.optimization_barrier((partial_value, spread))
    attn_group = jnp.sum(lax.all_gather(partial_value, "expert", axis=0, tiled=False), axis=0)
    group_hidden = lax.dynamic_slice_in_dim(everyone, group_start, group_rows, 0)
    group_residual = group_hidden.astype(jnp.float32) + attn_group
    residual = lax.dynamic_slice_in_dim(group_residual, ex_index * req_local, req_local, 0)
    normed_group = rms_norm(group_residual, ffn_gain).astype(jnp.bfloat16)
    slots_local = expert_gate_up.shape[0]
    ff_width = expert_gate_up.shape[2]
    col_width = expert_gate_up.shape[3]
    outgoing = migrate_route(spread, plan, expert_gate_up, expert_down)
    normed_group, outgoing = lax.optimization_barrier((normed_group, outgoing))
    every_row = lax.all_gather(normed_group, "dp", axis=0, tiled=True)
    unit = (every_row[0, 0].astype(jnp.float32) * 0.0 + 1.0).astype(expert_gate_up.dtype)
    base_gate_up = expert_gate_up * unit
    base_down = expert_down * unit
    arrived = deliver(outgoing)
    my_columns = lax.dynamic_slice_in_dim(every_row, dp_index * col_width, col_width, 1)
    by_group = my_columns.reshape(dp_count, ex_count, req_local, col_width).transpose(1, 0, 2, 3)
    ffn_rows = by_group.reshape(requests, col_width)
    column_rows = lax.dynamic_index_in_dim(by_group, ex_index, 0, keepdims=False).reshape(
        dp_count * req_local, col_width
    )
    top_count = expert_ids.shape[1]
    experts_count = EXP_DEV * ex_count
    ids_order = (
        expert_ids.reshape(dp_count, ex_count, req_local, top_count)
        .transpose(1, 0, 2, 3)
        .reshape(requests, top_count)
    )
    gates_order = (
        expert_gates.reshape(dp_count, ex_count, req_local, top_count)
        .transpose(1, 0, 2, 3)
        .reshape(requests, top_count)
    )
    old_flat = old_place.reshape(-1)
    holds_map = old_flat[None, :] == jnp.arange(experts_count, dtype=jnp.int32)[:, None]
    holder = jnp.argmax(holds_map, axis=1)
    slot_of = holder[ids_order.reshape(-1)]
    capacity = 2 * requests * top_count // experts_count
    local_slot = slot_of - ex_index * slots_local
    slot_hot = local_slot[:, None] == jnp.arange(slots_local, dtype=jnp.int32)[None, :]
    slot_rank = jnp.cumsum(slot_hot.astype(jnp.int32), axis=0) - 1
    position_in = jnp.where(slot_hot, slot_rank, capacity)
    route_hot = (
        position_in[:, :, None] == jnp.arange(capacity, dtype=jnp.int32)[None, None, :]
    ).astype(jnp.float32)
    route_hot = route_hot.reshape(requests, top_count, slots_local, capacity)
    dispatch = jnp.sum(route_hot, axis=1).astype(jnp.bfloat16)
    combine = jnp.sum(route_hot * gates_order[:, :, None, None], axis=1)
    slot_inputs = jnp.einsum(
        "tsc,td->scd", dispatch, ffn_rows, preferred_element_type=jnp.float32
    ).astype(jnp.bfloat16)
    routed_part = jnp.einsum(
        "scd,sgfd->sgcf", slot_inputs, expert_gate_up, preferred_element_type=jnp.float32
    )
    shared_part = jnp.einsum(
        "td,gfd->gtf", column_rows, shared_gate_up, preferred_element_type=jnp.float32
    )
    routed_sum, shared_sum = sum_over(routed_part, "dp"), sum_over(shared_part, "dp")
    activated = (jax.nn.silu(routed_sum[:, 0]) * routed_sum[:, 1]).astype(jnp.bfloat16)
    slot_out = jnp.einsum(
        "scf,sfd->scd", activated, expert_down, preferred_element_type=jnp.float32
    )
    routed = jnp.einsum("tsc,scd->td", combine, slot_out, precision=HIGHEST)
    shared_act = (jax.nn.silu(shared_sum[0]) * shared_sum[1]).astype(jnp.bfloat16)
    shared_term = jnp.dot(shared_act, shared_down, preferred_element_type=jnp.float32)
    routed, arrived = lax.optimization_barrier((routed, arrived))
    shared_at = ex_index * dp_count * req_local
    own_block = lax.dynamic_slice_in_dim(routed, shared_at, dp_count * req_local, 0) + shared_term
    routed = lax.dynamic_update_slice_in_dim(routed, own_block, shared_at, 0)
    by_token = routed.reshape(ex_count, dp_count, req_local, col_width).transpose(1, 0, 2, 3)
    by_token = by_token.reshape(requests, col_width)
    received = lax.all_to_all(by_token, ("dp", "expert"), split_axis=0, concat_axis=0, tiled=True)
    moe_cols = jnp.sum(received.reshape(dp_count, ex_count, req_local, col_width), axis=1)
    moe_part = moe_cols.transpose(1, 0, 2).reshape(req_local, dp_count * col_width)
    layer_out = (residual + moe_part).astype(jnp.bfloat16)
    my_moved = plan[-1]
    moved_gate_up = lax.dynamic_update_index_in_dim(base_gate_up, arrived[0, :2], my_moved, 0)
    moved_down = lax.dynamic_update_index_in_dim(base_down, arrived[0, 2], my_moved, 0)
    return (layer_out, moved_gate_up, moved_down)


def solution(mesh):
    in_specs = (
        P(("dp", "expert"), None),
        P(),
        P("expert", None),
        P(),
        P(None, "expert"),
        P("expert", None),
        P("dp", None, None),
        P(),
        P(),
        P(),
        P(),
        P(),
        P(),
        P(),
        P("expert", None, None, "dp"),
        P("expert", None, "dp"),
        P(None, None, "dp"),
        P(None, "dp"),
    )
    out_specs = (P(("dp", "expert"), None), P("expert", None, None, "dp"), P("expert", None, "dp"))
    return jax.shard_map(local, mesh=mesh, in_specs=in_specs, out_specs=out_specs, check_vma=False)
```

```python
import math

import jax
import jax.numpy as jnp
from jax import lax
from jax.sharding import PartitionSpec as P

NOPE = 128
ROPE = 64
VHEAD = 128
LATENT = 512
EXP_DEV = 3
PAGE = 32


EPSILON = 1e-06
ROPE_BASE = 50000.0
MASKED_SCORE = -1e30
HIGHEST = lax.Precision.HIGHEST


def rms_plain(values):
    mean_square = jnp.mean(values * values, axis=-1, keepdims=True)
    return values * lax.rsqrt(mean_square + EPSILON)


def rms_norm(values, norm_gain):
    return rms_plain(values) * norm_gain


def rotary(values, position):
    half_width = values.shape[-1] // 2
    exponent = jnp.arange(half_width).astype(jnp.float32) * (2.0 / values.shape[-1])
    frequency = jnp.exp(-exponent * math.log(ROPE_BASE))
    angles = position[..., None] * frequency
    cosine = jnp.cos(angles)
    sine_part = jnp.sin(angles)
    first_half = values[..., :half_width]
    second = values[..., half_width:]
    return jnp.concatenate(
        [first_half * cosine - second * sine_part, second * cosine + first_half * sine_part],
        axis=-1,
    )


def gather_rows(rows):
    by_expert = lax.all_gather(rows, "expert", axis=0, tiled=True)
    return lax.all_gather(by_expert, "dp", axis=0, tiled=True)


def pick_rows(table, rows):
    return jnp.stack([lax.dynamic_index_in_dim(table, rows[k], 0, False) for k in range(rows.shape[0])])


def pick_slots(gate_up, down, picks, ex_count):
    slots, parts, ff_width, col_width = gate_up.shape
    rows = ff_width // ex_count
    gate_up_blocks = gate_up.reshape(slots, parts, ex_count, rows, col_width)
    down_blocks = down.reshape(slots, ex_count, rows, col_width)
    chunks = []
    for c in range(ex_count):
        held = []
        for k in range(picks.shape[0]):
            pair = lax.dynamic_index_in_dim(gate_up_blocks[:, :, c], picks[k], 0, False)
            single = lax.dynamic_index_in_dim(down_blocks[:, c], picks[k], 0, False)
            held.append(jnp.concatenate([pair, single[None]], axis=0))
        chunks.append(jnp.stack(held))
    return jnp.stack(chunks)


def spread_slots(pieces):
    ex_count, count, parts, rows, col_width = pieces.shape
    spread = lax.all_to_all(pieces, "expert", split_axis=0, concat_axis=0, tiled=True)
    return spread.reshape(ex_count * count, parts, rows, col_width)


def scatter_sum(values, axis):
    count = lax.axis_size(axis)
    share = values.shape[0] // count
    gathered = lax.all_gather(values, axis, axis=0, tiled=False)
    mine = lax.dynamic_slice_in_dim(gathered, lax.axis_index(axis) * share, share, 1)
    return jnp.sum(mine, axis=0)


def sum_over(values, axis):
    return jnp.sum(lax.all_gather(values, axis, axis=0, tiled=False), axis=0)


def migrate_start(expert_gate_up, expert_down, old_place, new_place, ex_index):
    rows, slots_local = old_place.shape
    slots = rows * slots_local
    ex_count = rows
    ff_width = expert_gate_up.shape[2]
    changed = old_place != new_place
    moved_slot = jnp.argmax(changed, axis=1)
    wanted = jnp.take_along_axis(new_place, moved_slot[:, None], axis=1)[:, 0]
    hit = old_place.reshape(-1)[None, :] == wanted[:, None]
    first = jnp.argmax(hit, axis=1).astype(jnp.int32)
    last = (slots - 1 - jnp.argmax(hit[:, ::-1], axis=1)).astype(jnp.int32)
    slot_ids = jnp.arange(slots, dtype=jnp.int32)

    def needed_of(src):
        needed = jnp.any(src[:, None] == slot_ids[None, :], axis=0).reshape(rows, slots_local)
        return needed, jnp.max(jnp.sum(needed.astype(jnp.int32), axis=1))

    need_first, load_first = needed_of(first)
    need_last, load_last = needed_of(last)
    use_last = load_last < load_first
    source = jnp.where(use_last, last, first)
    needed = jnp.where(use_last, need_last, need_first)
    load = jnp.minimum(load_first, load_last)
    rank = jnp.cumsum(needed.astype(jnp.int32), axis=1) - 1
    local_ids = jnp.arange(slots_local, dtype=jnp.int32)
    picks = jnp.stack(
        [jnp.argmax(needed & (rank == k), axis=1).astype(jnp.int32) for k in range(slots_local)],
        axis=1,
    )
    my_picks = picks[ex_index]
    src_dev = source // slots_local
    src_rank = rank.reshape(-1)[source]
    fast = min(2, slots_local)
    chosen = pick_slots(expert_gate_up, expert_down, my_picks[:fast], ex_count)
    return chosen, (my_picks, src_dev, src_rank, load, moved_slot[ex_index])


def migrate_route(spread, plan, expert_gate_up, expert_down):
    my_picks, src_dev, src_rank, load, my_moved = plan
    ex_count = src_dev.shape[0]
    slots_local = expert_gate_up.shape[0]
    fast = spread.shape[0] // ex_count
    out_a = jnp.take(spread, src_dev * fast + jnp.minimum(src_rank, fast - 1), axis=0)
    if slots_local > fast:
        rest = slots_local - fast

        def extra():
            spread_b = spread_slots(pick_slots(expert_gate_up, expert_down, my_picks[fast:], ex_count))
            out_b = jnp.take(spread_b, src_dev * rest + jnp.clip(src_rank - fast, 0, rest - 1), axis=0)
            return jnp.where((src_rank < fast)[:, None, None, None], out_a, out_b)

        out_a = lax.cond(load > fast, extra, lambda: out_a)
    return out_a


def deliver(outgoing):
    return lax.all_to_all(outgoing, "expert", split_axis=0, concat_axis=2, tiled=True)


def local(
    hidden,
    attn_gain,
    query_weight,
    latent_down,
    latent_up,
    out_weight,
    latent_pool,
    page_table,
    page_counts,
    ffn_gain,
    expert_ids,
    expert_gates,
    old_place,
    new_place,
    expert_gate_up,
    expert_down,
    shared_gate_up,
    shared_down,
):
    dp_count = lax.axis_size("dp")
    ex_count = lax.axis_size("expert")
    dp_index = lax.axis_index("dp")
    ex_index = lax.axis_index("expert")
    req_local = hidden.shape[0]
    group_rows = req_local * ex_count
    requests = page_counts.shape[0]
    head_local = query_weight.shape[0] // (NOPE + ROPE)
    score_scale = (NOPE + ROPE) ** (-0.5)
    group_start = dp_index * group_rows
    chosen, plan = migrate_start(expert_gate_up, expert_down, old_place, new_place, ex_index)
    everyone = gather_rows(hidden)
    everyone, chosen = lax.optimization_barrier((everyone, chosen))
    spread = spread_slots(chosen)
    normed = rms_norm(everyone.astype(jnp.float32), attn_gain).astype(jnp.bfloat16)
    queries = jnp.einsum(
        "td,qd->tq", normed, query_weight, preferred_element_type=jnp.float32
    ).reshape(requests, head_local, NOPE + ROPE)
    position = (page_counts * PAGE).astype(jnp.float32)
    query_rope = rotary(queries[..., NOPE:], position[:, None]).astype(jnp.bfloat16)
    up_table = latent_up.reshape(LATENT, head_local, NOPE + VHEAD)
    query_latent = jnp.einsum(
        "thn,lhn->thl",
        queries[..., :NOPE],
        up_table[..., :NOPE].astype(jnp.float32),
        precision=HIGHEST,
    ).astype(jnp.bfloat16)
    pages_local = latent_pool.shape[0]
    pool_total = pages_local * dp_count
    flat_pages = page_table.reshape(-1)
    flat_owner = jnp.repeat(jnp.arange(requests, dtype=jnp.int32), page_table.shape[1])
    target = jnp.where(flat_pages >= 0, flat_pages, pool_total)
    owner_all = jnp.full((pool_total,), -1, jnp.int32).at[target].set(flat_owner, mode="drop")
    page_owner = lax.dynamic_slice_in_dim(owner_all, dp_index * pages_local, pages_local)
    page_used = page_owner >= 0
    owner_safe = jnp.maximum(page_owner, 0)
    page_latent = latent_pool[..., :LATENT]
    page_rope = latent_pool[..., LATENT:]
    scores = jnp.einsum(
        "phl,pkl->phk", query_latent[owner_safe], page_latent, preferred_element_type=jnp.float32
    )
    scores = (
        scores
        + jnp.einsum(
            "phr,pkr->phk", query_rope[owner_safe], page_rope, preferred_element_type=jnp.float32
        )
    ) * score_scale
    raw_max = jnp.max(scores, axis=2)
    weights = jnp.exp(scores - raw_max[..., None])
    page_total = jnp.sum(weights, axis=2)
    page_mix = jnp.einsum(
        "phk,pkl->phl",
        weights.astype(jnp.bfloat16),
        page_latent,
        preferred_element_type=jnp.float32,
    )
    page_max = jnp.where(page_used[:, None], raw_max, MASKED_SCORE)
    member = page_owner[None, :] == jnp.arange(requests, dtype=jnp.int32)[:, None]
    req_max = jnp.max(jnp.where(member[:, :, None], page_max[None], MASKED_SCORE), axis=1)
    rescale = jnp.where(page_used[:, None], jnp.exp(page_max - req_max[owner_safe]), 0.0)
    member_float = member.astype(jnp.float32)
    req_total = jnp.dot(member_float, page_total * rescale, precision=HIGHEST)
    req_mix = jnp.einsum(
        "rp,phl->rhl", member_float, page_mix * rescale[..., None], precision=HIGHEST
    )
    packed = jnp.concatenate([req_mix, req_max[..., None], req_total[..., None]], axis=-1)
    gathered = lax.all_gather(packed, "dp", axis=0, tiled=False)
    gathered = lax.dynamic_slice_in_dim(gathered, group_start, group_rows, 1)
    each_max = gathered[..., LATENT]
    part_max = jnp.max(each_max, axis=0)
    each_weight = jnp.exp(each_max - part_max[None])
    part_total = jnp.sum(gathered[..., LATENT + 1] * each_weight, axis=0)
    part_mix = jnp.sum(gathered[..., :LATENT] * each_weight[..., None], axis=0)
    own_normed = lax.dynamic_slice_in_dim(normed, group_start, group_rows, 0)
    own_position = lax.dynamic_slice_in_dim(position, group_start, group_rows, 0)
    fresh_latent = jnp.dot(own_normed, latent_down, preferred_element_type=jnp.float32)
    new_latent = rms_plain(fresh_latent[:, :LATENT]).astype(jnp.bfloat16)
    new_rope = rotary(fresh_latent[:, LATENT:], own_position).astype(jnp.bfloat16)
    own_query = lax.dynamic_slice_in_dim(query_latent, group_start, group_rows, 0)
    own_rope_query = lax.dynamic_slice_in_dim(query_rope, group_start, group_rows, 0)
    own_score = jnp.einsum("thl,tl->th", own_query, new_latent, preferred_element_type=jnp.float32)
    own_score = (
        own_score
        + jnp.einsum("thr,tr->th", own_rope_query, new_rope, preferred_element_type=jnp.float32)
    ) * score_scale
    highest = jnp.maximum(part_max, own_score)
    kept_part = jnp.exp(part_max - highest)
    own_weight = jnp.exp(own_score - highest)
    denominator = part_total * kept_part + own_weight
    numerator = (
        part_mix * kept_part[..., None]
        + own_weight[..., None] * new_latent.astype(jnp.float32)[:, None, :]
    )
    attended = (numerator / denominator[..., None]).astype(jnp.bfloat16)
    heads_out = jnp.einsum(
        "thl,lhv->thv", attended, up_table[..., NOPE:], preferred_element_type=jnp.float32
    )
    heads_out = heads_out.astype(jnp.bfloat16).reshape(group_rows, head_local * VHEAD)
    partial_value = jnp.dot(heads_out, out_weight, preferred_element_type=jnp.float32)
    partial_value, spread = lax.optimization_barrier((partial_value, spread))
    attn_group = jnp.sum(lax.all_gather(partial_value, "expert", axis=0, tiled=False), axis=0)
    group_hidden = lax.dynamic_slice_in_dim(everyone, group_start, group_rows, 0)
    group_residual = group_hidden.astype(jnp.float32) + attn_group
    residual = lax.dynamic_slice_in_dim(group_residual, ex_index * req_local, req_local, 0)
    normed_group = rms_norm(group_residual, ffn_gain).astype(jnp.bfloat16)
    slots_local = expert_gate_up.shape[0]
    ff_width = expert_gate_up.shape[2]
    col_width = expert_gate_up.shape[3]
    outgoing = migrate_route(spread, plan, expert_gate_up, expert_down)
    normed_group, outgoing = lax.optimization_barrier((normed_group, outgoing))
    every_row = lax.all_gather(normed_group, "dp", axis=0, tiled=True)
    unit = (every_row[0, 0].astype(jnp.float32) * 0.0 + 1.0).astype(expert_gate_up.dtype)
    base_gate_up = expert_gate_up * unit
    base_down = expert_down * unit
    arrived = deliver(outgoing)
    my_columns = lax.dynamic_slice_in_dim(every_row, dp_index * col_width, col_width, 1)
    by_group = my_columns.reshape(dp_count, ex_count, req_local, col_width).transpose(1, 0, 2, 3)
    ffn_rows = by_group.reshape(requests, col_width)
    column_rows = lax.dynamic_index_in_dim(by_group, ex_index, 0, keepdims=False).reshape(
        dp_count * req_local, col_width
    )
    top_count = expert_ids.shape[1]
    experts_count = EXP_DEV * ex_count
    ids_order = (
        expert_ids.reshape(dp_count, ex_count, req_local, top_count)
        .transpose(1, 0, 2, 3)
        .reshape(requests, top_count)
    )
    gates_order = (
        expert_gates.reshape(dp_count, ex_count, req_local, top_count)
        .transpose(1, 0, 2, 3)
        .reshape(requests, top_count)
    )
    old_flat = old_place.reshape(-1)
    holds_map = old_flat[None, :] == jnp.arange(experts_count, dtype=jnp.int32)[:, None]
    holder = jnp.argmax(holds_map, axis=1)
    slot_of = holder[ids_order.reshape(-1)]
    capacity = 2 * requests * top_count // experts_count
    local_slot = slot_of - ex_index * slots_local
    slot_hot = local_slot[:, None] == jnp.arange(slots_local, dtype=jnp.int32)[None, :]
    slot_rank = jnp.cumsum(slot_hot.astype(jnp.int32), axis=0) - 1
    position_in = jnp.where(slot_hot, slot_rank, capacity)
    route_hot = (
        position_in[:, :, None] == jnp.arange(capacity, dtype=jnp.int32)[None, None, :]
    ).astype(jnp.float32)
    route_hot = route_hot.reshape(requests, top_count, slots_local, capacity)
    dispatch = jnp.sum(route_hot, axis=1).astype(jnp.bfloat16)
    combine = jnp.sum(route_hot * gates_order[:, :, None, None], axis=1)
    slot_inputs = jnp.einsum(
        "tsc,td->scd", dispatch, ffn_rows, preferred_element_type=jnp.float32
    ).astype(jnp.bfloat16)
    routed_part = jnp.einsum(
        "scd,sgfd->sgcf", slot_inputs, expert_gate_up, preferred_element_type=jnp.float32
    )
    shared_part = jnp.einsum(
        "td,gfd->gtf", column_rows, shared_gate_up, preferred_element_type=jnp.float32
    )
    routed_sum, shared_sum = sum_over(routed_part, "dp"), sum_over(shared_part, "dp")
    activated = (jax.nn.silu(routed_sum[:, 0]) * routed_sum[:, 1]).astype(jnp.bfloat16)
    slot_out = jnp.einsum(
        "scf,sfd->scd", activated, expert_down, preferred_element_type=jnp.float32
    )
    routed = jnp.einsum("tsc,scd->td", combine, slot_out, precision=HIGHEST)
    shared_act = (jax.nn.silu(shared_sum[0]) * shared_sum[1]).astype(jnp.bfloat16)
    shared_term = jnp.dot(shared_act, shared_down, preferred_element_type=jnp.float32)
    routed, arrived = lax.optimization_barrier((routed, arrived))
    shared_at = ex_index * dp_count * req_local
    own_block = lax.dynamic_slice_in_dim(routed, shared_at, dp_count * req_local, 0) + shared_term
    routed = lax.dynamic_update_slice_in_dim(routed, own_block, shared_at, 0)
    by_token = routed.reshape(ex_count, dp_count, req_local, col_width).transpose(1, 0, 2, 3)
    by_token = by_token.reshape(requests, col_width)
    received = lax.all_to_all(by_token, ("dp", "expert"), split_axis=0, concat_axis=0, tiled=True)
    moe_cols = jnp.sum(received.reshape(dp_count, ex_count, req_local, col_width), axis=1)
    moe_part = moe_cols.transpose(1, 0, 2).reshape(req_local, dp_count * col_width)
    layer_out = (residual + moe_part).astype(jnp.bfloat16)
    my_moved = plan[-1]
    moved_gate_up = lax.dynamic_update_index_in_dim(base_gate_up, arrived[0, :2], my_moved, 0)
    moved_down = lax.dynamic_update_index_in_dim(base_down, arrived[0, 2], my_moved, 0)
    return (layer_out, moved_gate_up, moved_down)


def solution(mesh):
    in_specs = (
        P(("dp", "expert"), None),
        P(),
        P("expert", None),
        P(),
        P(None, "expert"),
        P("expert", None),
        P("dp", None, None),
        P(),
        P(),
        P(),
        P(),
        P(),
        P(),
        P(),
        P("expert", None, None, "dp"),
        P("expert", None, "dp"),
        P(None, None, "dp"),
        P(None, "dp"),
    )
    out_specs = (P(("dp", "expert"), None), P("expert", None, None, "dp"), P("expert", None, "dp"))
    return jax.shard_map(local, mesh=mesh, in_specs=in_specs, out_specs=out_specs, check_vma=False)
```

```python
import math

import jax
import jax.numpy as jnp
from jax import lax
from jax.sharding import PartitionSpec as P

NOPE = 128
ROPE = 64
VHEAD = 128
LATENT = 512
EXP_DEV = 3
PAGE = 32


EPSILON = 1e-06
ROPE_BASE = 50000.0
MASKED_SCORE = -1e30
HIGHEST = lax.Precision.HIGHEST


def rms_plain(values):
    mean_square = jnp.mean(values * values, axis=-1, keepdims=True)
    return values * lax.rsqrt(mean_square + EPSILON)


def rms_norm(values, norm_gain):
    return rms_plain(values) * norm_gain


def rotary(values, position):
    half_width = values.shape[-1] // 2
    exponent = jnp.arange(half_width).astype(jnp.float32) * (2.0 / values.shape[-1])
    frequency = jnp.exp(-exponent * math.log(ROPE_BASE))
    angles = position[..., None] * frequency
    cosine = jnp.cos(angles)
    sine_part = jnp.sin(angles)
    first_half = values[..., :half_width]
    second = values[..., half_width:]
    return jnp.concatenate(
        [first_half * cosine - second * sine_part, second * cosine + first_half * sine_part],
        axis=-1,
    )


def gather_rows(rows):
    by_expert = lax.all_gather(rows, "expert", axis=0, tiled=True)
    return lax.all_gather(by_expert, "dp", axis=0, tiled=True)


def pick_rows(table, rows):
    return jnp.stack([lax.dynamic_index_in_dim(table, rows[k], 0, False) for k in range(rows.shape[0])])


def pick_slots(gate_up, down, picks):
    return jnp.concatenate([pick_rows(gate_up, picks), pick_rows(down, picks)[:, None]], axis=1)


def spread_slots(chosen, ex_count):
    count, parts, ff_width, col_width = chosen.shape
    pieces = chosen.reshape(count, parts, ex_count, ff_width // ex_count, col_width)
    pieces = pieces.transpose(2, 0, 1, 3, 4)
    spread = lax.all_to_all(pieces, "expert", split_axis=0, concat_axis=0, tiled=True)
    return spread.reshape(ex_count * count, parts, ff_width // ex_count, col_width)


def scatter_sum(values, axis):
    count = lax.axis_size(axis)
    share = values.shape[0] // count
    gathered = lax.all_gather(values, axis, axis=0, tiled=False)
    mine = lax.dynamic_slice_in_dim(gathered, lax.axis_index(axis) * share, share, 1)
    return jnp.sum(mine, axis=0)


def sum_over(values, axis):
    return jnp.sum(lax.all_gather(values, axis, axis=0, tiled=False), axis=0)


def migrate_start(expert_gate_up, expert_down, old_place, new_place, ex_index):
    rows, slots_local = old_place.shape
    slots = rows * slots_local
    ex_count = rows
    ff_width = expert_gate_up.shape[2]
    changed = old_place != new_place
    moved_slot = jnp.argmax(changed, axis=1)
    wanted = jnp.take_along_axis(new_place, moved_slot[:, None], axis=1)[:, 0]
    hit = old_place.reshape(-1)[None, :] == wanted[:, None]
    first = jnp.argmax(hit, axis=1).astype(jnp.int32)
    last = (slots - 1 - jnp.argmax(hit[:, ::-1], axis=1)).astype(jnp.int32)
    slot_ids = jnp.arange(slots, dtype=jnp.int32)

    def needed_of(src):
        needed = jnp.any(src[:, None] == slot_ids[None, :], axis=0).reshape(rows, slots_local)
        return needed, jnp.max(jnp.sum(needed.astype(jnp.int32), axis=1))

    need_first, load_first = needed_of(first)
    need_last, load_last = needed_of(last)
    use_last = load_last < load_first
    source = jnp.where(use_last, last, first)
    needed = jnp.where(use_last, need_last, need_first)
    load = jnp.minimum(load_first, load_last)
    rank = jnp.cumsum(needed.astype(jnp.int32), axis=1) - 1
    local_ids = jnp.arange(slots_local, dtype=jnp.int32)
    picks = jnp.stack(
        [jnp.argmax(needed & (rank == k), axis=1).astype(jnp.int32) for k in range(slots_local)],
        axis=1,
    )
    my_picks = picks[ex_index]
    src_dev = source // slots_local
    src_rank = rank.reshape(-1)[source]
    fast = min(2, slots_local)
    chosen = pick_slots(expert_gate_up, expert_down, my_picks[:fast])
    return chosen, (my_picks, src_dev, src_rank, load, moved_slot[ex_index])


def migrate_route(spread, plan, expert_gate_up, expert_down):
    my_picks, src_dev, src_rank, load, my_moved = plan
    ex_count = src_dev.shape[0]
    slots_local = expert_gate_up.shape[0]
    fast = spread.shape[0] // ex_count
    out_a = jnp.take(spread, src_dev * fast + jnp.minimum(src_rank, fast - 1), axis=0, mode="clip")
    if slots_local > fast:
        rest = slots_local - fast

        def extra():
            spread_b = spread_slots(pick_slots(expert_gate_up, expert_down, my_picks[fast:]), ex_count)
            out_b = jnp.take(spread_b, src_dev * rest + jnp.clip(src_rank - fast, 0, rest - 1), axis=0, mode="clip")
            return jnp.where((src_rank < fast)[:, None, None, None], out_a, out_b)

        out_a = lax.cond(load > fast, extra, lambda: out_a)
    return out_a


def deliver(outgoing):
    return lax.all_to_all(outgoing, "expert", split_axis=0, concat_axis=2, tiled=True)


def local(
    hidden,
    attn_gain,
    query_weight,
    latent_down,
    latent_up,
    out_weight,
    latent_pool,
    page_table,
    page_counts,
    ffn_gain,
    expert_ids,
    expert_gates,
    old_place,
    new_place,
    expert_gate_up,
    expert_down,
    shared_gate_up,
    shared_down,
):
    dp_count = lax.axis_size("dp")
    ex_count = lax.axis_size("expert")
    dp_index = lax.axis_index("dp")
    ex_index = lax.axis_index("expert")
    req_local = hidden.shape[0]
    group_rows = req_local * ex_count
    requests = page_counts.shape[0]
    head_local = query_weight.shape[0] // (NOPE + ROPE)
    score_scale = (NOPE + ROPE) ** (-0.5)
    group_start = dp_index * group_rows
    chosen, plan = migrate_start(expert_gate_up, expert_down, old_place, new_place, ex_index)
    everyone = gather_rows(hidden)
    everyone, chosen = lax.optimization_barrier((everyone, chosen))
    spread = spread_slots(chosen, ex_count)
    normed = rms_norm(everyone.astype(jnp.float32), attn_gain).astype(jnp.bfloat16)
    queries = jnp.einsum(
        "td,qd->tq", normed, query_weight, preferred_element_type=jnp.float32
    ).reshape(requests, head_local, NOPE + ROPE)
    position = (page_counts * PAGE).astype(jnp.float32)
    query_rope = rotary(queries[..., NOPE:], position[:, None]).astype(jnp.bfloat16)
    up_table = latent_up.reshape(LATENT, head_local, NOPE + VHEAD)
    query_latent = jnp.einsum(
        "thn,lhn->thl",
        queries[..., :NOPE],
        up_table[..., :NOPE].astype(jnp.float32),
        precision=HIGHEST,
    ).astype(jnp.bfloat16)
    pages_local = latent_pool.shape[0]
    pool_total = pages_local * dp_count
    flat_pages = page_table.reshape(-1)
    flat_owner = jnp.repeat(jnp.arange(requests, dtype=jnp.int32), page_table.shape[1])
    target = jnp.where(flat_pages >= 0, flat_pages, pool_total)
    owner_all = jnp.full((pool_total,), -1, jnp.int32).at[target].set(flat_owner, mode="drop")
    page_owner = lax.dynamic_slice_in_dim(owner_all, dp_index * pages_local, pages_local)
    page_used = page_owner >= 0
    owner_safe = jnp.maximum(page_owner, 0)
    page_latent = latent_pool[..., :LATENT]
    page_rope = latent_pool[..., LATENT:]
    scores = jnp.einsum(
        "phl,pkl->phk", query_latent[owner_safe], page_latent, preferred_element_type=jnp.float32
    )
    scores = (
        scores
        + jnp.einsum(
            "phr,pkr->phk", query_rope[owner_safe], page_rope, preferred_element_type=jnp.float32
        )
    ) * score_scale
    raw_max = jnp.max(scores, axis=2)
    weights = jnp.exp(scores - raw_max[..., None])
    page_total = jnp.sum(weights, axis=2)
    page_mix = jnp.einsum(
        "phk,pkl->phl",
        weights.astype(jnp.bfloat16),
        page_latent,
        preferred_element_type=jnp.float32,
    )
    page_max = jnp.where(page_used[:, None], raw_max, MASKED_SCORE)
    member = page_owner[None, :] == jnp.arange(requests, dtype=jnp.int32)[:, None]
    req_max = jnp.max(jnp.where(member[:, :, None], page_max[None], MASKED_SCORE), axis=1)
    rescale = jnp.where(page_used[:, None], jnp.exp(page_max - req_max[owner_safe]), 0.0)
    member_float = member.astype(jnp.float32)
    req_total = jnp.dot(member_float, page_total * rescale, precision=HIGHEST)
    req_mix = jnp.einsum(
        "rp,phl->rhl", member_float, page_mix * rescale[..., None], precision=HIGHEST
    )
    packed = jnp.concatenate([req_mix, req_max[..., None], req_total[..., None]], axis=-1)
    gathered = lax.all_gather(packed, "dp", axis=0, tiled=False)
    gathered = lax.dynamic_slice_in_dim(gathered, group_start, group_rows, 1)
    each_max = gathered[..., LATENT]
    part_max = jnp.max(each_max, axis=0)
    each_weight = jnp.exp(each_max - part_max[None])
    part_total = jnp.sum(gathered[..., LATENT + 1] * each_weight, axis=0)
    part_mix = jnp.sum(gathered[..., :LATENT] * each_weight[..., None], axis=0)
    own_normed = lax.dynamic_slice_in_dim(normed, group_start, group_rows, 0)
    own_position = lax.dynamic_slice_in_dim(position, group_start, group_rows, 0)
    fresh_latent = jnp.dot(own_normed, latent_down, preferred_element_type=jnp.float32)
    new_latent = rms_plain(fresh_latent[:, :LATENT]).astype(jnp.bfloat16)
    new_rope = rotary(fresh_latent[:, LATENT:], own_position).astype(jnp.bfloat16)
    own_query = lax.dynamic_slice_in_dim(query_latent, group_start, group_rows, 0)
    own_rope_query = lax.dynamic_slice_in_dim(query_rope, group_start, group_rows, 0)
    own_score = jnp.einsum("thl,tl->th", own_query, new_latent, preferred_element_type=jnp.float32)
    own_score = (
        own_score
        + jnp.einsum("thr,tr->th", own_rope_query, new_rope, preferred_element_type=jnp.float32)
    ) * score_scale
    highest = jnp.maximum(part_max, own_score)
    kept_part = jnp.exp(part_max - highest)
    own_weight = jnp.exp(own_score - highest)
    denominator = part_total * kept_part + own_weight
    numerator = (
        part_mix * kept_part[..., None]
        + own_weight[..., None] * new_latent.astype(jnp.float32)[:, None, :]
    )
    attended = (numerator / denominator[..., None]).astype(jnp.bfloat16)
    heads_out = jnp.einsum(
        "thl,lhv->thv", attended, up_table[..., NOPE:], preferred_element_type=jnp.float32
    )
    heads_out = heads_out.astype(jnp.bfloat16).reshape(group_rows, head_local * VHEAD)
    partial_value = jnp.dot(heads_out, out_weight, preferred_element_type=jnp.float32)
    partial_value, spread = lax.optimization_barrier((partial_value, spread))
    attn_group = jnp.sum(lax.all_gather(partial_value, "expert", axis=0, tiled=False), axis=0)
    group_hidden = lax.dynamic_slice_in_dim(everyone, group_start, group_rows, 0)
    group_residual = group_hidden.astype(jnp.float32) + attn_group
    residual = lax.dynamic_slice_in_dim(group_residual, ex_index * req_local, req_local, 0)
    normed_group = rms_norm(group_residual, ffn_gain).astype(jnp.bfloat16)
    slots_local = expert_gate_up.shape[0]
    ff_width = expert_gate_up.shape[2]
    col_width = expert_gate_up.shape[3]
    outgoing = migrate_route(spread, plan, expert_gate_up, expert_down)
    normed_group, outgoing = lax.optimization_barrier((normed_group, outgoing))
    every_row = lax.all_gather(normed_group, "dp", axis=0, tiled=True)
    unit = (every_row[0, 0].astype(jnp.float32) * 0.0 + 1.0).astype(expert_gate_up.dtype)
    base_gate_up = expert_gate_up * unit
    base_down = expert_down * unit
    arrived = deliver(outgoing)
    my_columns = lax.dynamic_slice_in_dim(every_row, dp_index * col_width, col_width, 1)
    by_group = my_columns.reshape(dp_count, ex_count, req_local, col_width).transpose(1, 0, 2, 3)
    ffn_rows = by_group.reshape(requests, col_width)
    column_rows = lax.dynamic_index_in_dim(by_group, ex_index, 0, keepdims=False).reshape(
        dp_count * req_local, col_width
    )
    top_count = expert_ids.shape[1]
    experts_count = EXP_DEV * ex_count
    ids_order = (
        expert_ids.reshape(dp_count, ex_count, req_local, top_count)
        .transpose(1, 0, 2, 3)
        .reshape(requests, top_count)
    )
    gates_order = (
        expert_gates.reshape(dp_count, ex_count, req_local, top_count)
        .transpose(1, 0, 2, 3)
        .reshape(requests, top_count)
    )
    old_flat = old_place.reshape(-1)
    holds_map = old_flat[None, :] == jnp.arange(experts_count, dtype=jnp.int32)[:, None]
    holder = jnp.argmax(holds_map, axis=1)
    slot_of = holder[ids_order.reshape(-1)]
    capacity = 2 * requests * top_count // experts_count
    local_slot = slot_of - ex_index * slots_local
    slot_hot = local_slot[:, None] == jnp.arange(slots_local, dtype=jnp.int32)[None, :]
    slot_rank = jnp.cumsum(slot_hot.astype(jnp.int32), axis=0) - 1
    position_in = jnp.where(slot_hot, slot_rank, capacity)
    route_hot = (
        position_in[:, :, None] == jnp.arange(capacity, dtype=jnp.int32)[None, None, :]
    ).astype(jnp.float32)
    route_hot = route_hot.reshape(requests, top_count, slots_local, capacity)
    dispatch = jnp.sum(route_hot, axis=1).astype(jnp.bfloat16)
    combine = jnp.sum(route_hot * gates_order[:, :, None, None], axis=1)
    slot_inputs = jnp.einsum(
        "tsc,td->scd", dispatch, ffn_rows, preferred_element_type=jnp.float32
    ).astype(jnp.bfloat16)
    routed_part = jnp.einsum(
        "scd,sgfd->sgcf", slot_inputs, expert_gate_up, preferred_element_type=jnp.float32
    )
    shared_part = jnp.einsum(
        "td,gfd->gtf", column_rows, shared_gate_up, preferred_element_type=jnp.float32
    )
    routed_sum, shared_sum = sum_over(routed_part, "dp"), sum_over(shared_part, "dp")
    activated = (jax.nn.silu(routed_sum[:, 0]) * routed_sum[:, 1]).astype(jnp.bfloat16)
    slot_out = jnp.einsum(
        "scf,sfd->scd", activated, expert_down, preferred_element_type=jnp.float32
    )
    routed = jnp.einsum("tsc,scd->td", combine, slot_out, precision=HIGHEST)
    shared_act = (jax.nn.silu(shared_sum[0]) * shared_sum[1]).astype(jnp.bfloat16)
    shared_term = jnp.dot(shared_act, shared_down, preferred_element_type=jnp.float32)
    routed, arrived = lax.optimization_barrier((routed, arrived))
    shared_at = ex_index * dp_count * req_local
    own_block = lax.dynamic_slice_in_dim(routed, shared_at, dp_count * req_local, 0) + shared_term
    routed = lax.dynamic_update_slice_in_dim(routed, own_block, shared_at, 0)
    by_token = routed.reshape(ex_count, dp_count, req_local, col_width).transpose(1, 0, 2, 3)
    by_token = by_token.reshape(requests, col_width)
    received = lax.all_to_all(by_token, ("dp", "expert"), split_axis=0, concat_axis=0, tiled=True)
    moe_cols = jnp.sum(received.reshape(dp_count, ex_count, req_local, col_width), axis=1)
    moe_part = moe_cols.transpose(1, 0, 2).reshape(req_local, dp_count * col_width)
    layer_out = (residual + moe_part).astype(jnp.bfloat16)
    my_moved = plan[-1]
    moved_gate_up = lax.dynamic_update_index_in_dim(base_gate_up, arrived[0, :2], my_moved, 0)
    moved_down = lax.dynamic_update_index_in_dim(base_down, arrived[0, 2], my_moved, 0)
    return (layer_out, moved_gate_up, moved_down)


def solution(mesh):
    in_specs = (
        P(("dp", "expert"), None),
        P(),
        P("expert", None),
        P(),
        P(None, "expert"),
        P("expert", None),
        P("dp", None, None),
        P(),
        P(),
        P(),
        P(),
        P(),
        P(),
        P(),
        P("expert", None, None, "dp"),
        P("expert", None, "dp"),
        P(None, None, "dp"),
        P(None, "dp"),
    )
    out_specs = (P(("dp", "expert"), None), P("expert", None, None, "dp"), P("expert", None, "dp"))
    return jax.shard_map(local, mesh=mesh, in_specs=in_specs, out_specs=out_specs, check_vma=False)
```

```python
import math

import jax
import jax.numpy as jnp
from jax import lax
from jax.sharding import PartitionSpec as P

NOPE = 128
ROPE = 64
VHEAD = 128
LATENT = 512
EXP_DEV = 3
PAGE = 32


EPSILON = 1e-06
ROPE_BASE = 50000.0
MASKED_SCORE = -1e30
HIGHEST = lax.Precision.HIGHEST


def rms_plain(values):
    mean_square = jnp.mean(values * values, axis=-1, keepdims=True)
    return values * lax.rsqrt(mean_square + EPSILON)


def rms_norm(values, norm_gain):
    return rms_plain(values) * norm_gain


def rotary(values, position):
    half_width = values.shape[-1] // 2
    exponent = jnp.arange(half_width).astype(jnp.float32) * (2.0 / values.shape[-1])
    frequency = jnp.exp(-exponent * math.log(ROPE_BASE))
    angles = position[..., None] * frequency
    cosine = jnp.cos(angles)
    sine_part = jnp.sin(angles)
    first_half = values[..., :half_width]
    second = values[..., half_width:]
    return jnp.concatenate(
        [first_half * cosine - second * sine_part, second * cosine + first_half * sine_part],
        axis=-1,
    )


def gather_rows(rows):
    by_expert = lax.all_gather(rows, "expert", axis=0, tiled=True)
    return lax.all_gather(by_expert, "dp", axis=0, tiled=True)


def pick_rows(table, rows):
    return jnp.stack([lax.dynamic_index_in_dim(table, rows[k], 0, False) for k in range(rows.shape[0])])


def pick_slots(gate_up, down, picks):
    return jnp.concatenate([pick_rows(gate_up, picks), pick_rows(down, picks)[:, None]], axis=1)


def spread_slots(chosen, ex_count):
    count, parts, ff_width, col_width = chosen.shape
    pieces = chosen.reshape(count, parts, ex_count, ff_width // ex_count, col_width)
    pieces = pieces.transpose(2, 0, 1, 3, 4)
    spread = lax.all_to_all(pieces, "expert", split_axis=0, concat_axis=0, tiled=True)
    return spread.reshape(ex_count * count, parts, ff_width // ex_count, col_width)


def scatter_sum(values, axis):
    count = lax.axis_size(axis)
    share = values.shape[0] // count
    gathered = lax.all_gather(values, axis, axis=0, tiled=False)
    mine = lax.dynamic_slice_in_dim(gathered, lax.axis_index(axis) * share, share, 1)
    return jnp.sum(mine, axis=0)


def sum_over(values, axis):
    return jnp.sum(lax.all_gather(values, axis, axis=0, tiled=False), axis=0)


def migrate_start(expert_gate_up, expert_down, old_place, new_place, ex_index):
    rows, slots_local = old_place.shape
    slots = rows * slots_local
    ex_count = rows
    ff_width = expert_gate_up.shape[2]
    local_ids = jnp.arange(slots_local, dtype=jnp.int32)
    slot_ids = jnp.arange(slots, dtype=jnp.int32)
    changed = old_place != new_place
    moved_slot = jnp.min(jnp.where(changed, local_ids[None, :], slots_local), axis=1)
    wanted = jnp.sum(jnp.where(local_ids[None, :] == moved_slot[:, None], new_place, 0), axis=1)
    hit = old_place.reshape(-1)[None, :] == wanted[:, None]
    first = jnp.min(jnp.where(hit, slot_ids[None, :], slots), axis=1)
    last = jnp.max(jnp.where(hit, slot_ids[None, :], -1), axis=1)
    both = jnp.stack([first, last])
    needed_both = jnp.any(both[:, :, None] == slot_ids[None, None, :], axis=1)
    needed_both = needed_both.reshape(2, rows, slots_local)
    loads = jnp.max(jnp.sum(needed_both.astype(jnp.int32), axis=2), axis=1)
    use_last = loads[1] < loads[0]
    source = jnp.where(use_last, last, first)
    needed = jnp.where(use_last, needed_both[1], needed_both[0]).astype(jnp.int32)
    load = jnp.min(loads)
    before = local_ids[None, None, :] <= local_ids[None, :, None]
    rank = jnp.sum(jnp.where(before, needed[:, None, :], 0), axis=2) - 1
    my_needed = lax.dynamic_index_in_dim(needed, ex_index, 0, False) > 0
    my_rank = lax.dynamic_index_in_dim(rank, ex_index, 0, False)
    at_rank = my_needed[None, :] & (my_rank[None, :] == local_ids[:, None])
    my_picks = jnp.sum(jnp.where(at_rank, local_ids[None, :], 0), axis=1)
    src_dev = source // slots_local
    src_rank = jnp.sum(jnp.where(source[:, None] == slot_ids[None, :], rank.reshape(-1)[None, :], 0), axis=1)
    fast = min(2, slots_local)
    chosen = pick_slots(expert_gate_up, expert_down, my_picks[:fast])
    return chosen, (my_picks, src_dev, src_rank, load, lax.dynamic_index_in_dim(moved_slot, ex_index, 0, False))


def migrate_route(spread, plan, expert_gate_up, expert_down):
    my_picks, src_dev, src_rank, load, my_moved = plan
    ex_count = src_dev.shape[0]
    slots_local = expert_gate_up.shape[0]
    fast = spread.shape[0] // ex_count
    out_a = jnp.take(spread, src_dev * fast + jnp.minimum(src_rank, fast - 1), axis=0, mode="clip")
    if slots_local > fast:
        rest = slots_local - fast

        def extra():
            spread_b = spread_slots(pick_slots(expert_gate_up, expert_down, my_picks[fast:]), ex_count)
            out_b = jnp.take(spread_b, src_dev * rest + jnp.clip(src_rank - fast, 0, rest - 1), axis=0, mode="clip")
            return jnp.where((src_rank < fast)[:, None, None, None], out_a, out_b)

        out_a = lax.cond(load > fast, extra, lambda: out_a)
    return out_a


def deliver(outgoing):
    return lax.all_to_all(outgoing, "expert", split_axis=0, concat_axis=2, tiled=True)


def local(
    hidden,
    attn_gain,
    query_weight,
    latent_down,
    latent_up,
    out_weight,
    latent_pool,
    page_table,
    page_counts,
    ffn_gain,
    expert_ids,
    expert_gates,
    old_place,
    new_place,
    expert_gate_up,
    expert_down,
    shared_gate_up,
    shared_down,
):
    dp_count = lax.axis_size("dp")
    ex_count = lax.axis_size("expert")
    dp_index = lax.axis_index("dp")
    ex_index = lax.axis_index("expert")
    req_local = hidden.shape[0]
    group_rows = req_local * ex_count
    requests = page_counts.shape[0]
    head_local = query_weight.shape[0] // (NOPE + ROPE)
    score_scale = (NOPE + ROPE) ** (-0.5)
    group_start = dp_index * group_rows
    chosen, plan = migrate_start(expert_gate_up, expert_down, old_place, new_place, ex_index)
    everyone = gather_rows(hidden)
    everyone, chosen = lax.optimization_barrier((everyone, chosen))
    spread = spread_slots(chosen, ex_count)
    normed = rms_norm(everyone.astype(jnp.float32), attn_gain).astype(jnp.bfloat16)
    queries = jnp.einsum(
        "td,qd->tq", normed, query_weight, preferred_element_type=jnp.float32
    ).reshape(requests, head_local, NOPE + ROPE)
    position = (page_counts * PAGE).astype(jnp.float32)
    query_rope = rotary(queries[..., NOPE:], position[:, None]).astype(jnp.bfloat16)
    up_table = latent_up.reshape(LATENT, head_local, NOPE + VHEAD)
    query_latent = jnp.einsum(
        "thn,lhn->thl",
        queries[..., :NOPE],
        up_table[..., :NOPE].astype(jnp.float32),
        precision=HIGHEST,
    ).astype(jnp.bfloat16)
    pages_local = latent_pool.shape[0]
    pool_total = pages_local * dp_count
    flat_pages = page_table.reshape(-1)
    flat_owner = jnp.repeat(jnp.arange(requests, dtype=jnp.int32), page_table.shape[1])
    target = jnp.where(flat_pages >= 0, flat_pages, pool_total)
    owner_all = jnp.full((pool_total,), -1, jnp.int32).at[target].set(flat_owner, mode="drop")
    page_owner = lax.dynamic_slice_in_dim(owner_all, dp_index * pages_local, pages_local)
    page_used = page_owner >= 0
    owner_safe = jnp.maximum(page_owner, 0)
    page_latent = latent_pool[..., :LATENT]
    page_rope = latent_pool[..., LATENT:]
    scores = jnp.einsum(
        "phl,pkl->phk", query_latent[owner_safe], page_latent, preferred_element_type=jnp.float32
    )
    scores = (
        scores
        + jnp.einsum(
            "phr,pkr->phk", query_rope[owner_safe], page_rope, preferred_element_type=jnp.float32
        )
    ) * score_scale
    raw_max = jnp.max(scores, axis=2)
    weights = jnp.exp(scores - raw_max[..., None])
    page_total = jnp.sum(weights, axis=2)
    page_mix = jnp.einsum(
        "phk,pkl->phl",
        weights.astype(jnp.bfloat16),
        page_latent,
        preferred_element_type=jnp.float32,
    )
    page_max = jnp.where(page_used[:, None], raw_max, MASKED_SCORE)
    member = page_owner[None, :] == jnp.arange(requests, dtype=jnp.int32)[:, None]
    req_max = jnp.max(jnp.where(member[:, :, None], page_max[None], MASKED_SCORE), axis=1)
    rescale = jnp.where(page_used[:, None], jnp.exp(page_max - req_max[owner_safe]), 0.0)
    member_float = member.astype(jnp.float32)
    req_total = jnp.dot(member_float, page_total * rescale, precision=HIGHEST)
    req_mix = jnp.einsum(
        "rp,phl->rhl", member_float, page_mix * rescale[..., None], precision=HIGHEST
    )
    packed = jnp.concatenate([req_mix, req_max[..., None], req_total[..., None]], axis=-1)
    gathered = lax.all_gather(packed, "dp", axis=0, tiled=False)
    gathered = lax.dynamic_slice_in_dim(gathered, group_start, group_rows, 1)
    each_max = gathered[..., LATENT]
    part_max = jnp.max(each_max, axis=0)
    each_weight = jnp.exp(each_max - part_max[None])
    part_total = jnp.sum(gathered[..., LATENT + 1] * each_weight, axis=0)
    part_mix = jnp.sum(gathered[..., :LATENT] * each_weight[..., None], axis=0)
    own_normed = lax.dynamic_slice_in_dim(normed, group_start, group_rows, 0)
    own_position = lax.dynamic_slice_in_dim(position, group_start, group_rows, 0)
    fresh_latent = jnp.dot(own_normed, latent_down, preferred_element_type=jnp.float32)
    new_latent = rms_plain(fresh_latent[:, :LATENT]).astype(jnp.bfloat16)
    new_rope = rotary(fresh_latent[:, LATENT:], own_position).astype(jnp.bfloat16)
    own_query = lax.dynamic_slice_in_dim(query_latent, group_start, group_rows, 0)
    own_rope_query = lax.dynamic_slice_in_dim(query_rope, group_start, group_rows, 0)
    own_score = jnp.einsum("thl,tl->th", own_query, new_latent, preferred_element_type=jnp.float32)
    own_score = (
        own_score
        + jnp.einsum("thr,tr->th", own_rope_query, new_rope, preferred_element_type=jnp.float32)
    ) * score_scale
    highest = jnp.maximum(part_max, own_score)
    kept_part = jnp.exp(part_max - highest)
    own_weight = jnp.exp(own_score - highest)
    denominator = part_total * kept_part + own_weight
    numerator = (
        part_mix * kept_part[..., None]
        + own_weight[..., None] * new_latent.astype(jnp.float32)[:, None, :]
    )
    attended = (numerator / denominator[..., None]).astype(jnp.bfloat16)
    heads_out = jnp.einsum(
        "thl,lhv->thv", attended, up_table[..., NOPE:], preferred_element_type=jnp.float32
    )
    heads_out = heads_out.astype(jnp.bfloat16).reshape(group_rows, head_local * VHEAD)
    partial_value = jnp.dot(heads_out, out_weight, preferred_element_type=jnp.float32)
    partial_value, spread = lax.optimization_barrier((partial_value, spread))
    attn_group = jnp.sum(lax.all_gather(partial_value, "expert", axis=0, tiled=False), axis=0)
    group_hidden = lax.dynamic_slice_in_dim(everyone, group_start, group_rows, 0)
    group_residual = group_hidden.astype(jnp.float32) + attn_group
    residual = lax.dynamic_slice_in_dim(group_residual, ex_index * req_local, req_local, 0)
    normed_group = rms_norm(group_residual, ffn_gain).astype(jnp.bfloat16)
    slots_local = expert_gate_up.shape[0]
    ff_width = expert_gate_up.shape[2]
    col_width = expert_gate_up.shape[3]
    outgoing = migrate_route(spread, plan, expert_gate_up, expert_down)
    normed_group, outgoing = lax.optimization_barrier((normed_group, outgoing))
    every_row = lax.all_gather(normed_group, "dp", axis=0, tiled=True)
    unit = (every_row[0, 0].astype(jnp.float32) * 0.0 + 1.0).astype(expert_gate_up.dtype)
    base_gate_up = expert_gate_up * unit
    base_down = expert_down * unit
    arrived = deliver(outgoing)
    my_columns = lax.dynamic_slice_in_dim(every_row, dp_index * col_width, col_width, 1)
    by_group = my_columns.reshape(dp_count, ex_count, req_local, col_width).transpose(1, 0, 2, 3)
    ffn_rows = by_group.reshape(requests, col_width)
    column_rows = lax.dynamic_index_in_dim(by_group, ex_index, 0, keepdims=False).reshape(
        dp_count * req_local, col_width
    )
    top_count = expert_ids.shape[1]
    experts_count = EXP_DEV * ex_count
    ids_order = (
        expert_ids.reshape(dp_count, ex_count, req_local, top_count)
        .transpose(1, 0, 2, 3)
        .reshape(requests, top_count)
    )
    gates_order = (
        expert_gates.reshape(dp_count, ex_count, req_local, top_count)
        .transpose(1, 0, 2, 3)
        .reshape(requests, top_count)
    )
    old_flat = old_place.reshape(-1)
    holds_map = old_flat[None, :] == jnp.arange(experts_count, dtype=jnp.int32)[:, None]
    holder = jnp.argmax(holds_map, axis=1)
    slot_of = holder[ids_order.reshape(-1)]
    capacity = 2 * requests * top_count // experts_count
    local_slot = slot_of - ex_index * slots_local
    slot_hot = local_slot[:, None] == jnp.arange(slots_local, dtype=jnp.int32)[None, :]
    slot_rank = jnp.cumsum(slot_hot.astype(jnp.int32), axis=0) - 1
    position_in = jnp.where(slot_hot, slot_rank, capacity)
    route_hot = (
        position_in[:, :, None] == jnp.arange(capacity, dtype=jnp.int32)[None, None, :]
    ).astype(jnp.float32)
    route_hot = route_hot.reshape(requests, top_count, slots_local, capacity)
    dispatch = jnp.sum(route_hot, axis=1).astype(jnp.bfloat16)
    combine = jnp.sum(route_hot * gates_order[:, :, None, None], axis=1)
    slot_inputs = jnp.einsum(
        "tsc,td->scd", dispatch, ffn_rows, preferred_element_type=jnp.float32
    ).astype(jnp.bfloat16)
    routed_part = jnp.einsum(
        "scd,sgfd->sgcf", slot_inputs, expert_gate_up, preferred_element_type=jnp.float32
    )
    shared_part = jnp.einsum(
        "td,gfd->gtf", column_rows, shared_gate_up, preferred_element_type=jnp.float32
    )
    routed_sum, shared_sum = sum_over(routed_part, "dp"), sum_over(shared_part, "dp")
    activated = (jax.nn.silu(routed_sum[:, 0]) * routed_sum[:, 1]).astype(jnp.bfloat16)
    slot_out = jnp.einsum(
        "scf,sfd->scd", activated, expert_down, preferred_element_type=jnp.float32
    )
    routed = jnp.einsum("tsc,scd->td", combine, slot_out, precision=HIGHEST)
    shared_act = (jax.nn.silu(shared_sum[0]) * shared_sum[1]).astype(jnp.bfloat16)
    shared_term = jnp.dot(shared_act, shared_down, preferred_element_type=jnp.float32)
    routed, arrived = lax.optimization_barrier((routed, arrived))
    shared_at = ex_index * dp_count * req_local
    own_block = lax.dynamic_slice_in_dim(routed, shared_at, dp_count * req_local, 0) + shared_term
    routed = lax.dynamic_update_slice_in_dim(routed, own_block, shared_at, 0)
    by_token = routed.reshape(ex_count, dp_count, req_local, col_width).transpose(1, 0, 2, 3)
    by_token = by_token.reshape(requests, col_width)
    received = lax.all_to_all(by_token, ("dp", "expert"), split_axis=0, concat_axis=0, tiled=True)
    moe_cols = jnp.sum(received.reshape(dp_count, ex_count, req_local, col_width), axis=1)
    moe_part = moe_cols.transpose(1, 0, 2).reshape(req_local, dp_count * col_width)
    layer_out = (residual + moe_part).astype(jnp.bfloat16)
    my_moved = plan[-1]
    moved_gate_up = lax.dynamic_update_index_in_dim(base_gate_up, arrived[0, :2], my_moved, 0)
    moved_down = lax.dynamic_update_index_in_dim(base_down, arrived[0, 2], my_moved, 0)
    return (layer_out, moved_gate_up, moved_down)


def solution(mesh):
    in_specs = (
        P(("dp", "expert"), None),
        P(),
        P("expert", None),
        P(),
        P(None, "expert"),
        P("expert", None),
        P("dp", None, None),
        P(),
        P(),
        P(),
        P(),
        P(),
        P(),
        P(),
        P("expert", None, None, "dp"),
        P("expert", None, "dp"),
        P(None, None, "dp"),
        P(None, "dp"),
    )
    out_specs = (P(("dp", "expert"), None), P("expert", None, None, "dp"), P("expert", None, "dp"))
    return jax.shard_map(local, mesh=mesh, in_specs=in_specs, out_specs=out_specs, check_vma=False)
```

```python
import math

import jax
import jax.numpy as jnp
from jax import lax
from jax.sharding import PartitionSpec as P

NOPE = 128
ROPE = 64
VHEAD = 128
LATENT = 512
EXP_DEV = 3
PAGE = 32


EPSILON = 1e-06
ROPE_BASE = 50000.0
MASKED_SCORE = -1e30
HIGHEST = lax.Precision.HIGHEST


def rms_plain(values):
    mean_square = jnp.mean(values * values, axis=-1, keepdims=True)
    return values * lax.rsqrt(mean_square + EPSILON)


def rms_norm(values, norm_gain):
    return rms_plain(values) * norm_gain


def rotary(values, position):
    half_width = values.shape[-1] // 2
    exponent = jnp.arange(half_width).astype(jnp.float32) * (2.0 / values.shape[-1])
    frequency = jnp.exp(-exponent * math.log(ROPE_BASE))
    angles = position[..., None] * frequency
    cosine = jnp.cos(angles)
    sine_part = jnp.sin(angles)
    first_half = values[..., :half_width]
    second = values[..., half_width:]
    return jnp.concatenate(
        [first_half * cosine - second * sine_part, second * cosine + first_half * sine_part],
        axis=-1,
    )


def pick_rows(table, rows):
    return jnp.stack([lax.dynamic_index_in_dim(table, rows[k], 0, False) for k in range(rows.shape[0])])


def pick_slots(gate_up, down, picks):
    return jnp.concatenate([pick_rows(gate_up, picks), pick_rows(down, picks)[:, None]], axis=1)


def spread_slots(chosen, ex_count):
    count, parts, ff_width, col_width = chosen.shape
    pieces = chosen.reshape(count, parts, ex_count, ff_width // ex_count, col_width)
    pieces = pieces.transpose(2, 0, 1, 3, 4)
    spread = lax.all_to_all(pieces, "expert", split_axis=0, concat_axis=0, tiled=True)
    return spread.reshape(ex_count * count, parts, ff_width // ex_count, col_width)


def scatter_sum(values, axis):
    count = lax.axis_size(axis)
    share = values.shape[0] // count
    gathered = lax.all_gather(values, axis, axis=0, tiled=False)
    mine = lax.dynamic_slice_in_dim(gathered, lax.axis_index(axis) * share, share, 1)
    return jnp.sum(mine, axis=0)


def sum_over(values, axis):
    return jnp.sum(lax.all_gather(values, axis, axis=0, tiled=False), axis=0)


def migrate_start(expert_gate_up, expert_down, old_place, new_place, ex_index):
    rows, slots_local = old_place.shape
    slots = rows * slots_local
    ex_count = rows
    ff_width = expert_gate_up.shape[2]
    local_ids = jnp.arange(slots_local, dtype=jnp.int32)
    slot_ids = jnp.arange(slots, dtype=jnp.int32)
    changed = old_place != new_place
    moved_slot = jnp.min(jnp.where(changed, local_ids[None, :], slots_local), axis=1)
    wanted = jnp.sum(jnp.where(local_ids[None, :] == moved_slot[:, None], new_place, 0), axis=1)
    hit = old_place.reshape(-1)[None, :] == wanted[:, None]
    first = jnp.min(jnp.where(hit, slot_ids[None, :], slots), axis=1)
    last = jnp.max(jnp.where(hit, slot_ids[None, :], -1), axis=1)
    both = jnp.stack([first, last])
    needed_both = jnp.any(both[:, :, None] == slot_ids[None, None, :], axis=1)
    needed_both = needed_both.reshape(2, rows, slots_local)
    loads = jnp.max(jnp.sum(needed_both.astype(jnp.int32), axis=2), axis=1)
    use_last = loads[1] < loads[0]
    source = jnp.where(use_last, last, first)
    needed = jnp.where(use_last, needed_both[1], needed_both[0]).astype(jnp.int32)
    load = jnp.min(loads)
    before = local_ids[None, None, :] <= local_ids[None, :, None]
    rank = jnp.sum(jnp.where(before, needed[:, None, :], 0), axis=2) - 1
    my_needed = lax.dynamic_index_in_dim(needed, ex_index, 0, False) > 0
    my_rank = lax.dynamic_index_in_dim(rank, ex_index, 0, False)
    at_rank = my_needed[None, :] & (my_rank[None, :] == local_ids[:, None])
    my_picks = jnp.sum(jnp.where(at_rank, local_ids[None, :], 0), axis=1)
    src_dev = source // slots_local
    src_rank = jnp.sum(jnp.where(source[:, None] == slot_ids[None, :], rank.reshape(-1)[None, :], 0), axis=1)
    fast = min(2, slots_local)
    chosen = pick_slots(expert_gate_up, expert_down, my_picks[:fast])
    return chosen, (my_picks, src_dev, src_rank, load, lax.dynamic_index_in_dim(moved_slot, ex_index, 0, False))


def migrate_route(spread, plan, expert_gate_up, expert_down):
    my_picks, src_dev, src_rank, load, my_moved = plan
    ex_count = src_dev.shape[0]
    slots_local = expert_gate_up.shape[0]
    fast = spread.shape[0] // ex_count
    out_a = jnp.take(spread, src_dev * fast + jnp.minimum(src_rank, fast - 1), axis=0, mode="clip")
    if slots_local > fast:
        rest = slots_local - fast

        def extra():
            spread_b = spread_slots(pick_slots(expert_gate_up, expert_down, my_picks[fast:]), ex_count)
            out_b = jnp.take(spread_b, src_dev * rest + jnp.clip(src_rank - fast, 0, rest - 1), axis=0, mode="clip")
            return jnp.where((src_rank < fast)[:, None, None, None], out_a, out_b)

        out_a = lax.cond(load > fast, extra, lambda: out_a)
    return out_a


def deliver(outgoing):
    return lax.all_to_all(outgoing, "expert", split_axis=0, concat_axis=2, tiled=True)


def local(
    hidden,
    attn_gain,
    query_weight,
    latent_down,
    latent_up,
    out_weight,
    latent_pool,
    page_table,
    page_counts,
    ffn_gain,
    expert_ids,
    expert_gates,
    old_place,
    new_place,
    expert_gate_up,
    expert_down,
    shared_gate_up,
    shared_down,
):
    dp_count = lax.axis_size("dp")
    ex_count = lax.axis_size("expert")
    dp_index = lax.axis_index("dp")
    ex_index = lax.axis_index("expert")
    req_local = hidden.shape[0]
    group_rows = req_local * ex_count
    requests = page_counts.shape[0]
    head_local = query_weight.shape[0] // (NOPE + ROPE)
    score_scale = (NOPE + ROPE) ** (-0.5)
    group_start = dp_index * group_rows
    chosen, plan = migrate_start(expert_gate_up, expert_down, old_place, new_place, ex_index)
    by_expert = lax.all_gather(hidden, "expert", axis=0, tiled=True)
    by_expert, chosen = lax.optimization_barrier((by_expert, chosen))
    spread = spread_slots(chosen, ex_count)
    everyone = lax.all_gather(by_expert, "dp", axis=0, tiled=True)
    normed = rms_norm(everyone.astype(jnp.float32), attn_gain).astype(jnp.bfloat16)
    queries = jnp.einsum(
        "td,qd->tq", normed, query_weight, preferred_element_type=jnp.float32
    ).reshape(requests, head_local, NOPE + ROPE)
    position = (page_counts * PAGE).astype(jnp.float32)
    query_rope = rotary(queries[..., NOPE:], position[:, None]).astype(jnp.bfloat16)
    up_table = latent_up.reshape(LATENT, head_local, NOPE + VHEAD)
    query_latent = jnp.einsum(
        "thn,lhn->thl",
        queries[..., :NOPE],
        up_table[..., :NOPE].astype(jnp.float32),
        precision=HIGHEST,
    ).astype(jnp.bfloat16)
    pages_local = latent_pool.shape[0]
    pool_total = pages_local * dp_count
    flat_pages = page_table.reshape(-1)
    flat_owner = jnp.repeat(jnp.arange(requests, dtype=jnp.int32), page_table.shape[1])
    target = jnp.where(flat_pages >= 0, flat_pages, pool_total)
    owner_all = jnp.full((pool_total,), -1, jnp.int32).at[target].set(flat_owner, mode="drop")
    page_owner = lax.dynamic_slice_in_dim(owner_all, dp_index * pages_local, pages_local)
    page_used = page_owner >= 0
    owner_safe = jnp.maximum(page_owner, 0)
    page_latent = latent_pool[..., :LATENT]
    page_rope = latent_pool[..., LATENT:]
    scores = jnp.einsum(
        "phl,pkl->phk", query_latent[owner_safe], page_latent, preferred_element_type=jnp.float32
    )
    scores = (
        scores
        + jnp.einsum(
            "phr,pkr->phk", query_rope[owner_safe], page_rope, preferred_element_type=jnp.float32
        )
    ) * score_scale
    raw_max = jnp.max(scores, axis=2)
    weights = jnp.exp(scores - raw_max[..., None])
    page_total = jnp.sum(weights, axis=2)
    page_mix = jnp.einsum(
        "phk,pkl->phl",
        weights.astype(jnp.bfloat16),
        page_latent,
        preferred_element_type=jnp.float32,
    )
    page_max = jnp.where(page_used[:, None], raw_max, MASKED_SCORE)
    member = page_owner[None, :] == jnp.arange(requests, dtype=jnp.int32)[:, None]
    req_max = jnp.max(jnp.where(member[:, :, None], page_max[None], MASKED_SCORE), axis=1)
    rescale = jnp.where(page_used[:, None], jnp.exp(page_max - req_max[owner_safe]), 0.0)
    member_float = member.astype(jnp.float32)
    req_total = jnp.dot(member_float, page_total * rescale, precision=HIGHEST)
    req_mix = jnp.einsum(
        "rp,phl->rhl", member_float, page_mix * rescale[..., None], precision=HIGHEST
    )
    packed = jnp.concatenate([req_mix, req_max[..., None], req_total[..., None]], axis=-1)
    gathered = lax.all_gather(packed, "dp", axis=0, tiled=False)
    gathered = lax.dynamic_slice_in_dim(gathered, group_start, group_rows, 1)
    each_max = gathered[..., LATENT]
    part_max = jnp.max(each_max, axis=0)
    each_weight = jnp.exp(each_max - part_max[None])
    part_total = jnp.sum(gathered[..., LATENT + 1] * each_weight, axis=0)
    part_mix = jnp.sum(gathered[..., :LATENT] * each_weight[..., None], axis=0)
    own_normed = lax.dynamic_slice_in_dim(normed, group_start, group_rows, 0)
    own_position = lax.dynamic_slice_in_dim(position, group_start, group_rows, 0)
    fresh_latent = jnp.dot(own_normed, latent_down, preferred_element_type=jnp.float32)
    new_latent = rms_plain(fresh_latent[:, :LATENT]).astype(jnp.bfloat16)
    new_rope = rotary(fresh_latent[:, LATENT:], own_position).astype(jnp.bfloat16)
    own_query = lax.dynamic_slice_in_dim(query_latent, group_start, group_rows, 0)
    own_rope_query = lax.dynamic_slice_in_dim(query_rope, group_start, group_rows, 0)
    own_score = jnp.einsum("thl,tl->th", own_query, new_latent, preferred_element_type=jnp.float32)
    own_score = (
        own_score
        + jnp.einsum("thr,tr->th", own_rope_query, new_rope, preferred_element_type=jnp.float32)
    ) * score_scale
    highest = jnp.maximum(part_max, own_score)
    kept_part = jnp.exp(part_max - highest)
    own_weight = jnp.exp(own_score - highest)
    denominator = part_total * kept_part + own_weight
    numerator = (
        part_mix * kept_part[..., None]
        + own_weight[..., None] * new_latent.astype(jnp.float32)[:, None, :]
    )
    attended = (numerator / denominator[..., None]).astype(jnp.bfloat16)
    heads_out = jnp.einsum(
        "thl,lhv->thv", attended, up_table[..., NOPE:], preferred_element_type=jnp.float32
    )
    heads_out = heads_out.astype(jnp.bfloat16).reshape(group_rows, head_local * VHEAD)
    partial_value = jnp.dot(heads_out, out_weight, preferred_element_type=jnp.float32)
    partial_value, spread = lax.optimization_barrier((partial_value, spread))
    attn_group = jnp.sum(lax.all_gather(partial_value, "expert", axis=0, tiled=False), axis=0)
    group_hidden = lax.dynamic_slice_in_dim(everyone, group_start, group_rows, 0)
    group_residual = group_hidden.astype(jnp.float32) + attn_group
    residual = lax.dynamic_slice_in_dim(group_residual, ex_index * req_local, req_local, 0)
    normed_group = rms_norm(group_residual, ffn_gain).astype(jnp.bfloat16)
    slots_local = expert_gate_up.shape[0]
    ff_width = expert_gate_up.shape[2]
    col_width = expert_gate_up.shape[3]
    outgoing = migrate_route(spread, plan, expert_gate_up, expert_down)
    normed_group, outgoing = lax.optimization_barrier((normed_group, outgoing))
    every_row = lax.all_gather(normed_group, "dp", axis=0, tiled=True)
    unit = (every_row[0, 0].astype(jnp.float32) * 0.0 + 1.0).astype(expert_gate_up.dtype)
    base_gate_up = expert_gate_up * unit
    base_down = expert_down * unit
    arrived = deliver(outgoing)
    my_columns = lax.dynamic_slice_in_dim(every_row, dp_index * col_width, col_width, 1)
    by_group = my_columns.reshape(dp_count, ex_count, req_local, col_width).transpose(1, 0, 2, 3)
    ffn_rows = by_group.reshape(requests, col_width)
    column_rows = lax.dynamic_index_in_dim(by_group, ex_index, 0, keepdims=False).reshape(
        dp_count * req_local, col_width
    )
    top_count = expert_ids.shape[1]
    experts_count = EXP_DEV * ex_count
    ids_order = (
        expert_ids.reshape(dp_count, ex_count, req_local, top_count)
        .transpose(1, 0, 2, 3)
        .reshape(requests, top_count)
    )
    gates_order = (
        expert_gates.reshape(dp_count, ex_count, req_local, top_count)
        .transpose(1, 0, 2, 3)
        .reshape(requests, top_count)
    )
    old_flat = old_place.reshape(-1)
    holds_map = old_flat[None, :] == jnp.arange(experts_count, dtype=jnp.int32)[:, None]
    holder = jnp.argmax(holds_map, axis=1)
    slot_of = holder[ids_order.reshape(-1)]
    capacity = 2 * requests * top_count // experts_count
    local_slot = slot_of - ex_index * slots_local
    slot_hot = local_slot[:, None] == jnp.arange(slots_local, dtype=jnp.int32)[None, :]
    slot_rank = jnp.cumsum(slot_hot.astype(jnp.int32), axis=0) - 1
    position_in = jnp.where(slot_hot, slot_rank, capacity)
    route_hot = (
        position_in[:, :, None] == jnp.arange(capacity, dtype=jnp.int32)[None, None, :]
    ).astype(jnp.float32)
    route_hot = route_hot.reshape(requests, top_count, slots_local, capacity)
    dispatch = jnp.sum(route_hot, axis=1).astype(jnp.bfloat16)
    combine = jnp.sum(route_hot * gates_order[:, :, None, None], axis=1)
    slot_inputs = jnp.einsum(
        "tsc,td->scd", dispatch, ffn_rows, preferred_element_type=jnp.float32
    ).astype(jnp.bfloat16)
    routed_part = jnp.einsum(
        "scd,sgfd->sgcf", slot_inputs, expert_gate_up, preferred_element_type=jnp.float32
    )
    shared_part = jnp.einsum(
        "td,gfd->gtf", column_rows, shared_gate_up, preferred_element_type=jnp.float32
    )
    routed_sum, shared_sum = sum_over(routed_part, "dp"), sum_over(shared_part, "dp")
    activated = (jax.nn.silu(routed_sum[:, 0]) * routed_sum[:, 1]).astype(jnp.bfloat16)
    slot_out = jnp.einsum(
        "scf,sfd->scd", activated, expert_down, preferred_element_type=jnp.float32
    )
    routed = jnp.einsum("tsc,scd->td", combine, slot_out, precision=HIGHEST)
    shared_act = (jax.nn.silu(shared_sum[0]) * shared_sum[1]).astype(jnp.bfloat16)
    shared_term = jnp.dot(shared_act, shared_down, preferred_element_type=jnp.float32)
    routed, arrived = lax.optimization_barrier((routed, arrived))
    shared_at = ex_index * dp_count * req_local
    own_block = lax.dynamic_slice_in_dim(routed, shared_at, dp_count * req_local, 0) + shared_term
    routed = lax.dynamic_update_slice_in_dim(routed, own_block, shared_at, 0)
    by_token = routed.reshape(ex_count, dp_count, req_local, col_width).transpose(1, 0, 2, 3)
    by_token = by_token.reshape(requests, col_width)
    received = lax.all_to_all(by_token, ("dp", "expert"), split_axis=0, concat_axis=0, tiled=True)
    moe_cols = jnp.sum(received.reshape(dp_count, ex_count, req_local, col_width), axis=1)
    moe_part = moe_cols.transpose(1, 0, 2).reshape(req_local, dp_count * col_width)
    layer_out = (residual + moe_part).astype(jnp.bfloat16)
    my_moved = plan[-1]
    moved_gate_up = lax.dynamic_update_index_in_dim(base_gate_up, arrived[0, :2], my_moved, 0)
    moved_down = lax.dynamic_update_index_in_dim(base_down, arrived[0, 2], my_moved, 0)
    return (layer_out, moved_gate_up, moved_down)


def solution(mesh):
    in_specs = (
        P(("dp", "expert"), None),
        P(),
        P("expert", None),
        P(),
        P(None, "expert"),
        P("expert", None),
        P("dp", None, None),
        P(),
        P(),
        P(),
        P(),
        P(),
        P(),
        P(),
        P("expert", None, None, "dp"),
        P("expert", None, "dp"),
        P(None, None, "dp"),
        P(None, "dp"),
    )
    out_specs = (P(("dp", "expert"), None), P("expert", None, None, "dp"), P("expert", None, "dp"))
    return jax.shard_map(local, mesh=mesh, in_specs=in_specs, out_specs=out_specs, check_vma=False)
```

```python
import math

import jax
import jax.numpy as jnp
from jax import lax
from jax.sharding import PartitionSpec as P

NOPE = 128
ROPE = 64
VHEAD = 128
LATENT = 512
EXP_DEV = 3
PAGE = 32


EPSILON = 1e-06
ROPE_BASE = 50000.0
MASKED_SCORE = -1e30
HIGHEST = lax.Precision.HIGHEST


def rms_plain(values):
    mean_square = jnp.mean(values * values, axis=-1, keepdims=True)
    return values * lax.rsqrt(mean_square + EPSILON)


def rms_norm(values, norm_gain):
    return rms_plain(values) * norm_gain


def rotary(values, position):
    half_width = values.shape[-1] // 2
    exponent = jnp.arange(half_width).astype(jnp.float32) * (2.0 / values.shape[-1])
    frequency = jnp.exp(-exponent * math.log(ROPE_BASE))
    angles = position[..., None] * frequency
    cosine = jnp.cos(angles)
    sine_part = jnp.sin(angles)
    first_half = values[..., :half_width]
    second = values[..., half_width:]
    return jnp.concatenate(
        [first_half * cosine - second * sine_part, second * cosine + first_half * sine_part],
        axis=-1,
    )


def pick_rows(table, rows):
    return jnp.stack([lax.dynamic_index_in_dim(table, rows[k], 0, False) for k in range(rows.shape[0])])


def pick_slots(gate_up, down, picks):
    return jnp.concatenate([pick_rows(gate_up, picks), pick_rows(down, picks)[:, None]], axis=1)


def spread_slots(chosen, ex_count):
    count, parts, ff_width, col_width = chosen.shape
    pieces = chosen.reshape(count, parts, ex_count, ff_width // ex_count, col_width)
    pieces = pieces.transpose(2, 0, 1, 3, 4)
    spread = lax.all_to_all(pieces, "expert", split_axis=0, concat_axis=0, tiled=True)
    return spread.reshape(ex_count * count, parts, ff_width // ex_count, col_width)


def scatter_sum(values, axis):
    count = lax.axis_size(axis)
    share = values.shape[0] // count
    gathered = lax.all_gather(values, axis, axis=0, tiled=False)
    mine = lax.dynamic_slice_in_dim(gathered, lax.axis_index(axis) * share, share, 1)
    return jnp.sum(mine, axis=0)


def sum_over(values, axis):
    return jnp.sum(lax.all_gather(values, axis, axis=0, tiled=False), axis=0)


def migrate_start(expert_gate_up, expert_down, old_place, new_place, ex_index):
    rows, slots_local = old_place.shape
    slots = rows * slots_local
    ex_count = rows
    ff_width = expert_gate_up.shape[2]
    local_ids = jnp.arange(slots_local, dtype=jnp.int32)
    slot_ids = jnp.arange(slots, dtype=jnp.int32)
    changed = old_place != new_place
    moved_slot = jnp.min(jnp.where(changed, local_ids[None, :], slots_local), axis=1)
    wanted = jnp.sum(jnp.where(local_ids[None, :] == moved_slot[:, None], new_place, 0), axis=1)
    hit = old_place.reshape(-1)[None, :] == wanted[:, None]
    first = jnp.min(jnp.where(hit, slot_ids[None, :], slots), axis=1)
    last = jnp.max(jnp.where(hit, slot_ids[None, :], -1), axis=1)
    both = jnp.stack([first, last])
    needed_both = jnp.any(both[:, :, None] == slot_ids[None, None, :], axis=1)
    needed_both = needed_both.reshape(2, rows, slots_local)
    loads = jnp.max(jnp.sum(needed_both.astype(jnp.int32), axis=2), axis=1)
    use_last = loads[1] < loads[0]
    source = jnp.where(use_last, last, first)
    needed = jnp.where(use_last, needed_both[1], needed_both[0]).astype(jnp.int32)
    load = jnp.min(loads)
    before = local_ids[None, None, :] <= local_ids[None, :, None]
    rank = jnp.sum(jnp.where(before, needed[:, None, :], 0), axis=2) - 1
    my_needed = lax.dynamic_index_in_dim(needed, ex_index, 0, False) > 0
    my_rank = lax.dynamic_index_in_dim(rank, ex_index, 0, False)
    at_rank = my_needed[None, :] & (my_rank[None, :] == local_ids[:, None])
    my_picks = jnp.sum(jnp.where(at_rank, local_ids[None, :], 0), axis=1)
    src_dev = source // slots_local
    src_rank = jnp.sum(jnp.where(source[:, None] == slot_ids[None, :], rank.reshape(-1)[None, :], 0), axis=1)
    fast = min(2, slots_local)
    chosen = pick_slots(expert_gate_up, expert_down, my_picks[:fast])
    return chosen, (my_picks, src_dev, src_rank, load, lax.dynamic_index_in_dim(moved_slot, ex_index, 0, False))


def migrate_route(spread, plan, expert_gate_up, expert_down):
    my_picks, src_dev, src_rank, load, my_moved = plan
    ex_count = src_dev.shape[0]
    slots_local = expert_gate_up.shape[0]
    fast = spread.shape[0] // ex_count
    out_a = jnp.take(spread, src_dev * fast + jnp.minimum(src_rank, fast - 1), axis=0, mode="clip")
    if slots_local > fast:
        rest = slots_local - fast

        def extra():
            spread_b = spread_slots(pick_slots(expert_gate_up, expert_down, my_picks[fast:]), ex_count)
            out_b = jnp.take(spread_b, src_dev * rest + jnp.clip(src_rank - fast, 0, rest - 1), axis=0, mode="clip")
            return jnp.where((src_rank < fast)[:, None, None, None], out_a, out_b)

        out_a = lax.cond(load > fast, extra, lambda: out_a)
    return out_a


def deliver(outgoing):
    return lax.all_to_all(outgoing, "expert", split_axis=0, concat_axis=0, tiled=True)


def local(
    hidden,
    attn_gain,
    query_weight,
    latent_down,
    latent_up,
    out_weight,
    latent_pool,
    page_table,
    page_counts,
    ffn_gain,
    expert_ids,
    expert_gates,
    old_place,
    new_place,
    expert_gate_up,
    expert_down,
    shared_gate_up,
    shared_down,
):
    dp_count = lax.axis_size("dp")
    ex_count = lax.axis_size("expert")
    dp_index = lax.axis_index("dp")
    ex_index = lax.axis_index("expert")
    req_local = hidden.shape[0]
    group_rows = req_local * ex_count
    requests = page_counts.shape[0]
    head_local = query_weight.shape[0] // (NOPE + ROPE)
    score_scale = (NOPE + ROPE) ** (-0.5)
    group_start = dp_index * group_rows
    chosen, plan = migrate_start(expert_gate_up, expert_down, old_place, new_place, ex_index)
    by_expert = lax.all_gather(hidden, "expert", axis=0, tiled=True)
    by_expert, chosen = lax.optimization_barrier((by_expert, chosen))
    spread = spread_slots(chosen, ex_count)
    everyone = lax.all_gather(by_expert, "dp", axis=0, tiled=True)
    normed = rms_norm(everyone.astype(jnp.float32), attn_gain).astype(jnp.bfloat16)
    queries = jnp.einsum(
        "td,qd->tq", normed, query_weight, preferred_element_type=jnp.float32
    ).reshape(requests, head_local, NOPE + ROPE)
    position = (page_counts * PAGE).astype(jnp.float32)
    query_rope = rotary(queries[..., NOPE:], position[:, None]).astype(jnp.bfloat16)
    up_table = latent_up.reshape(LATENT, head_local, NOPE + VHEAD)
    query_latent = jnp.einsum(
        "thn,lhn->thl",
        queries[..., :NOPE],
        up_table[..., :NOPE].astype(jnp.float32),
        precision=HIGHEST,
    ).astype(jnp.bfloat16)
    pages_local = latent_pool.shape[0]
    pool_total = pages_local * dp_count
    flat_pages = page_table.reshape(-1)
    flat_owner = jnp.repeat(jnp.arange(requests, dtype=jnp.int32), page_table.shape[1])
    target = jnp.where(flat_pages >= 0, flat_pages, pool_total)
    owner_all = jnp.full((pool_total,), -1, jnp.int32).at[target].set(flat_owner, mode="drop")
    page_owner = lax.dynamic_slice_in_dim(owner_all, dp_index * pages_local, pages_local)
    page_used = page_owner >= 0
    owner_safe = jnp.maximum(page_owner, 0)
    page_latent = latent_pool[..., :LATENT]
    page_rope = latent_pool[..., LATENT:]
    scores = jnp.einsum(
        "phl,pkl->phk", query_latent[owner_safe], page_latent, preferred_element_type=jnp.float32
    )
    scores = (
        scores
        + jnp.einsum(
            "phr,pkr->phk", query_rope[owner_safe], page_rope, preferred_element_type=jnp.float32
        )
    ) * score_scale
    raw_max = jnp.max(scores, axis=2)
    weights = jnp.exp(scores - raw_max[..., None])
    page_total = jnp.sum(weights, axis=2)
    page_mix = jnp.einsum(
        "phk,pkl->phl",
        weights.astype(jnp.bfloat16),
        page_latent,
        preferred_element_type=jnp.float32,
    )
    page_max = jnp.where(page_used[:, None], raw_max, MASKED_SCORE)
    member = page_owner[None, :] == jnp.arange(requests, dtype=jnp.int32)[:, None]
    req_max = jnp.max(jnp.where(member[:, :, None], page_max[None], MASKED_SCORE), axis=1)
    rescale = jnp.where(page_used[:, None], jnp.exp(page_max - req_max[owner_safe]), 0.0)
    member_float = member.astype(jnp.float32)
    req_total = jnp.dot(member_float, page_total * rescale, precision=HIGHEST)
    req_mix = jnp.einsum(
        "rp,phl->rhl", member_float, page_mix * rescale[..., None], precision=HIGHEST
    )
    packed = jnp.concatenate([req_mix, req_max[..., None], req_total[..., None]], axis=-1)
    gathered = lax.all_gather(packed, "dp", axis=0, tiled=False)
    gathered = lax.dynamic_slice_in_dim(gathered, group_start, group_rows, 1)
    each_max = gathered[..., LATENT]
    part_max = jnp.max(each_max, axis=0)
    each_weight = jnp.exp(each_max - part_max[None])
    part_total = jnp.sum(gathered[..., LATENT + 1] * each_weight, axis=0)
    part_mix = jnp.sum(gathered[..., :LATENT] * each_weight[..., None], axis=0)
    own_normed = lax.dynamic_slice_in_dim(normed, group_start, group_rows, 0)
    own_position = lax.dynamic_slice_in_dim(position, group_start, group_rows, 0)
    fresh_latent = jnp.dot(own_normed, latent_down, preferred_element_type=jnp.float32)
    new_latent = rms_plain(fresh_latent[:, :LATENT]).astype(jnp.bfloat16)
    new_rope = rotary(fresh_latent[:, LATENT:], own_position).astype(jnp.bfloat16)
    own_query = lax.dynamic_slice_in_dim(query_latent, group_start, group_rows, 0)
    own_rope_query = lax.dynamic_slice_in_dim(query_rope, group_start, group_rows, 0)
    own_score = jnp.einsum("thl,tl->th", own_query, new_latent, preferred_element_type=jnp.float32)
    own_score = (
        own_score
        + jnp.einsum("thr,tr->th", own_rope_query, new_rope, preferred_element_type=jnp.float32)
    ) * score_scale
    highest = jnp.maximum(part_max, own_score)
    kept_part = jnp.exp(part_max - highest)
    own_weight = jnp.exp(own_score - highest)
    denominator = part_total * kept_part + own_weight
    numerator = (
        part_mix * kept_part[..., None]
        + own_weight[..., None] * new_latent.astype(jnp.float32)[:, None, :]
    )
    attended = (numerator / denominator[..., None]).astype(jnp.bfloat16)
    heads_out = jnp.einsum(
        "thl,lhv->thv", attended, up_table[..., NOPE:], preferred_element_type=jnp.float32
    )
    heads_out = heads_out.astype(jnp.bfloat16).reshape(group_rows, head_local * VHEAD)
    partial_value = jnp.dot(heads_out, out_weight, preferred_element_type=jnp.float32)
    partial_value, spread = lax.optimization_barrier((partial_value, spread))
    attn_group = jnp.sum(lax.all_gather(partial_value, "expert", axis=0, tiled=False), axis=0)
    group_hidden = lax.dynamic_slice_in_dim(everyone, group_start, group_rows, 0)
    group_residual = group_hidden.astype(jnp.float32) + attn_group
    residual = lax.dynamic_slice_in_dim(group_residual, ex_index * req_local, req_local, 0)
    normed_group = rms_norm(group_residual, ffn_gain).astype(jnp.bfloat16)
    slots_local = expert_gate_up.shape[0]
    ff_width = expert_gate_up.shape[2]
    col_width = expert_gate_up.shape[3]
    outgoing = migrate_route(spread, plan, expert_gate_up, expert_down)
    normed_group, outgoing = lax.optimization_barrier((normed_group, outgoing))
    every_row = lax.all_gather(normed_group, "dp", axis=0, tiled=True)
    unit = (every_row[0, 0].astype(jnp.float32) * 0.0 + 1.0).astype(expert_gate_up.dtype)
    base_gate_up = expert_gate_up * unit
    base_down = expert_down * unit
    arrived = deliver(outgoing)
    my_columns = lax.dynamic_slice_in_dim(every_row, dp_index * col_width, col_width, 1)
    by_group = my_columns.reshape(dp_count, ex_count, req_local, col_width).transpose(1, 0, 2, 3)
    ffn_rows = by_group.reshape(requests, col_width)
    column_rows = lax.dynamic_index_in_dim(by_group, ex_index, 0, keepdims=False).reshape(
        dp_count * req_local, col_width
    )
    top_count = expert_ids.shape[1]
    experts_count = EXP_DEV * ex_count
    ids_order = (
        expert_ids.reshape(dp_count, ex_count, req_local, top_count)
        .transpose(1, 0, 2, 3)
        .reshape(requests, top_count)
    )
    gates_order = (
        expert_gates.reshape(dp_count, ex_count, req_local, top_count)
        .transpose(1, 0, 2, 3)
        .reshape(requests, top_count)
    )
    old_flat = old_place.reshape(-1)
    holds_map = old_flat[None, :] == jnp.arange(experts_count, dtype=jnp.int32)[:, None]
    holder = jnp.argmax(holds_map, axis=1)
    slot_of = holder[ids_order.reshape(-1)]
    capacity = 2 * requests * top_count // experts_count
    local_slot = slot_of - ex_index * slots_local
    slot_hot = local_slot[:, None] == jnp.arange(slots_local, dtype=jnp.int32)[None, :]
    slot_rank = jnp.cumsum(slot_hot.astype(jnp.int32), axis=0) - 1
    position_in = jnp.where(slot_hot, slot_rank, capacity)
    route_hot = (
        position_in[:, :, None] == jnp.arange(capacity, dtype=jnp.int32)[None, None, :]
    ).astype(jnp.float32)
    route_hot = route_hot.reshape(requests, top_count, slots_local, capacity)
    dispatch = jnp.sum(route_hot, axis=1).astype(jnp.bfloat16)
    combine = jnp.sum(route_hot * gates_order[:, :, None, None], axis=1)
    slot_inputs = jnp.einsum(
        "tsc,td->scd", dispatch, ffn_rows, preferred_element_type=jnp.float32
    ).astype(jnp.bfloat16)
    routed_part = jnp.einsum(
        "scd,sgfd->sgcf", slot_inputs, expert_gate_up, preferred_element_type=jnp.float32
    )
    shared_part = jnp.einsum(
        "td,gfd->gtf", column_rows, shared_gate_up, preferred_element_type=jnp.float32
    )
    routed_sum, shared_sum = sum_over(routed_part, "dp"), sum_over(shared_part, "dp")
    activated = (jax.nn.silu(routed_sum[:, 0]) * routed_sum[:, 1]).astype(jnp.bfloat16)
    slot_out = jnp.einsum(
        "scf,sfd->scd", activated, expert_down, preferred_element_type=jnp.float32
    )
    routed = jnp.einsum("tsc,scd->td", combine, slot_out, precision=HIGHEST)
    shared_act = (jax.nn.silu(shared_sum[0]) * shared_sum[1]).astype(jnp.bfloat16)
    shared_term = jnp.dot(shared_act, shared_down, preferred_element_type=jnp.float32)
    routed, arrived = lax.optimization_barrier((routed, arrived))
    shared_at = ex_index * dp_count * req_local
    own_block = lax.dynamic_slice_in_dim(routed, shared_at, dp_count * req_local, 0) + shared_term
    routed = lax.dynamic_update_slice_in_dim(routed, own_block, shared_at, 0)
    by_token = routed.reshape(ex_count, dp_count, req_local, col_width).transpose(1, 0, 2, 3)
    by_token = by_token.reshape(requests, col_width)
    received = lax.all_to_all(by_token, ("dp", "expert"), split_axis=0, concat_axis=0, tiled=True)
    moe_cols = jnp.sum(received.reshape(dp_count, ex_count, req_local, col_width), axis=1)
    moe_part = moe_cols.transpose(1, 0, 2).reshape(req_local, dp_count * col_width)
    layer_out = (residual + moe_part).astype(jnp.bfloat16)
    my_moved = plan[-1]
    chunk_rows = arrived.shape[2]
    slot_shape = (slots_local, 2, ex_count, chunk_rows, col_width)
    new_pair = arrived[:, :2].transpose(1, 0, 2, 3)[None]
    moved_gate_up = lax.dynamic_update_slice(
        base_gate_up.reshape(slot_shape), new_pair, (my_moved, 0, 0, 0, 0)
    ).reshape(base_gate_up.shape)
    new_single = arrived[:, 2][None]
    moved_down = lax.dynamic_update_slice(
        base_down.reshape(slots_local, ex_count, chunk_rows, col_width), new_single, (my_moved, 0, 0, 0)
    ).reshape(base_down.shape)
    return (layer_out, moved_gate_up, moved_down)


def solution(mesh):
    in_specs = (
        P(("dp", "expert"), None),
        P(),
        P("expert", None),
        P(),
        P(None, "expert"),
        P("expert", None),
        P("dp", None, None),
        P(),
        P(),
        P(),
        P(),
        P(),
        P(),
        P(),
        P("expert", None, None, "dp"),
        P("expert", None, "dp"),
        P(None, None, "dp"),
        P(None, "dp"),
    )
    out_specs = (P(("dp", "expert"), None), P("expert", None, None, "dp"), P("expert", None, "dp"))
    return jax.shard_map(local, mesh=mesh, in_specs=in_specs, out_specs=out_specs, check_vma=False)
```

```python
import math

import jax
import jax.numpy as jnp
from jax import lax
from jax.sharding import PartitionSpec as P

NOPE = 128
ROPE = 64
VHEAD = 128
LATENT = 512
EXP_DEV = 3
PAGE = 32


EPSILON = 1e-06
ROPE_BASE = 50000.0
MASKED_SCORE = -1e30
HIGHEST = lax.Precision.HIGHEST


def rms_plain(values):
    mean_square = jnp.mean(values * values, axis=-1, keepdims=True)
    return values * lax.rsqrt(mean_square + EPSILON)


def rms_norm(values, norm_gain):
    return rms_plain(values) * norm_gain


def rotary(values, position):
    half_width = values.shape[-1] // 2
    exponent = jnp.arange(half_width).astype(jnp.float32) * (2.0 / values.shape[-1])
    frequency = jnp.exp(-exponent * math.log(ROPE_BASE))
    angles = position[..., None] * frequency
    cosine = jnp.cos(angles)
    sine_part = jnp.sin(angles)
    first_half = values[..., :half_width]
    second = values[..., half_width:]
    return jnp.concatenate(
        [first_half * cosine - second * sine_part, second * cosine + first_half * sine_part],
        axis=-1,
    )


def pick_rows(table, rows):
    return jnp.stack([lax.dynamic_index_in_dim(table, rows[k], 0, False) for k in range(rows.shape[0])])


def pick_slots(gate_up, down, picks):
    return jnp.concatenate([pick_rows(gate_up, picks), pick_rows(down, picks)[:, None]], axis=1)


def spread_slots(chosen, ex_count):
    count, parts, ff_width, col_width = chosen.shape
    pieces = chosen.reshape(count, parts, ex_count, ff_width // ex_count, col_width)
    pieces = pieces.transpose(2, 0, 1, 3, 4)
    spread = lax.all_to_all(pieces, "expert", split_axis=0, concat_axis=0, tiled=True)
    return spread.reshape(ex_count * count, parts, ff_width // ex_count, col_width)


def scatter_sum(values, axis):
    count = lax.axis_size(axis)
    share = values.shape[0] // count
    gathered = lax.all_gather(values, axis, axis=0, tiled=False)
    mine = lax.dynamic_slice_in_dim(gathered, lax.axis_index(axis) * share, share, 1)
    return jnp.sum(mine, axis=0)


def sum_over(values, axis):
    return jnp.sum(lax.all_gather(values, axis, axis=0, tiled=False), axis=0)


def migrate_start(expert_gate_up, expert_down, old_place, new_place, ex_index):
    rows, slots_local = old_place.shape
    slots = rows * slots_local
    ex_count = rows
    ff_width = expert_gate_up.shape[2]
    local_ids = jnp.arange(slots_local, dtype=jnp.int32)
    slot_ids = jnp.arange(slots, dtype=jnp.int32)
    changed = old_place != new_place
    moved_slot = jnp.min(jnp.where(changed, local_ids[None, :], slots_local), axis=1)
    wanted = jnp.sum(jnp.where(local_ids[None, :] == moved_slot[:, None], new_place, 0), axis=1)
    hit = old_place.reshape(-1)[None, :] == wanted[:, None]
    first = jnp.min(jnp.where(hit, slot_ids[None, :], slots), axis=1)
    last = jnp.max(jnp.where(hit, slot_ids[None, :], -1), axis=1)
    both = jnp.stack([first, last])
    needed_both = jnp.any(both[:, :, None] == slot_ids[None, None, :], axis=1)
    needed_both = needed_both.reshape(2, rows, slots_local)
    loads = jnp.max(jnp.sum(needed_both.astype(jnp.int32), axis=2), axis=1)
    use_last = loads[1] < loads[0]
    source = jnp.where(use_last, last, first)
    needed = jnp.where(use_last, needed_both[1], needed_both[0]).astype(jnp.int32)
    load = jnp.min(loads)
    before = local_ids[None, None, :] <= local_ids[None, :, None]
    rank = jnp.sum(jnp.where(before, needed[:, None, :], 0), axis=2) - 1
    my_needed = lax.dynamic_index_in_dim(needed, ex_index, 0, False) > 0
    my_rank = lax.dynamic_index_in_dim(rank, ex_index, 0, False)
    at_rank = my_needed[None, :] & (my_rank[None, :] == local_ids[:, None])
    my_picks = jnp.sum(jnp.where(at_rank, local_ids[None, :], 0), axis=1)
    src_dev = source // slots_local
    src_rank = jnp.sum(jnp.where(source[:, None] == slot_ids[None, :], rank.reshape(-1)[None, :], 0), axis=1)
    fast = min(2, slots_local)
    chosen = pick_slots(expert_gate_up, expert_down, my_picks[:fast])
    return chosen, (my_picks, src_dev, src_rank, load, lax.dynamic_index_in_dim(moved_slot, ex_index, 0, False))


def migrate_route(spread, plan, expert_gate_up, expert_down):
    my_picks, src_dev, src_rank, load, my_moved = plan
    ex_count = src_dev.shape[0]
    slots_local = expert_gate_up.shape[0]
    fast = spread.shape[0] // ex_count
    out_a = jnp.take(spread, src_dev * fast + jnp.minimum(src_rank, fast - 1), axis=0, mode="clip")
    if slots_local > fast:
        rest = slots_local - fast

        def extra():
            spread_b = spread_slots(pick_slots(expert_gate_up, expert_down, my_picks[fast:]), ex_count)
            out_b = jnp.take(spread_b, src_dev * rest + jnp.clip(src_rank - fast, 0, rest - 1), axis=0, mode="clip")
            return jnp.where((src_rank < fast)[:, None, None, None], out_a, out_b)

        out_a = lax.cond(load > fast, extra, lambda: out_a)
    return out_a


def deliver(outgoing):
    return lax.all_to_all(outgoing, "expert", split_axis=0, concat_axis=0, tiled=True)


def local(
    hidden,
    attn_gain,
    query_weight,
    latent_down,
    latent_up,
    out_weight,
    latent_pool,
    page_table,
    page_counts,
    ffn_gain,
    expert_ids,
    expert_gates,
    old_place,
    new_place,
    expert_gate_up,
    expert_down,
    shared_gate_up,
    shared_down,
):
    dp_count = lax.axis_size("dp")
    ex_count = lax.axis_size("expert")
    dp_index = lax.axis_index("dp")
    ex_index = lax.axis_index("expert")
    req_local = hidden.shape[0]
    group_rows = req_local * ex_count
    requests = page_counts.shape[0]
    head_local = query_weight.shape[0] // (NOPE + ROPE)
    score_scale = (NOPE + ROPE) ** (-0.5)
    group_start = dp_index * group_rows
    chosen, plan = migrate_start(expert_gate_up, expert_down, old_place, new_place, ex_index)
    copies = jnp.broadcast_to(hidden[None], (ex_count,) + hidden.shape)
    by_expert = lax.all_to_all(copies, "expert", split_axis=0, concat_axis=0, tiled=True)
    by_expert = by_expert.reshape(ex_count * req_local, hidden.shape[1])
    by_expert, chosen = lax.optimization_barrier((by_expert, chosen))
    spread = spread_slots(chosen, ex_count)
    everyone = lax.all_gather(by_expert, "dp", axis=0, tiled=True)
    normed = rms_norm(everyone.astype(jnp.float32), attn_gain).astype(jnp.bfloat16)
    queries = jnp.einsum(
        "td,qd->tq", normed, query_weight, preferred_element_type=jnp.float32
    ).reshape(requests, head_local, NOPE + ROPE)
    position = (page_counts * PAGE).astype(jnp.float32)
    query_rope = rotary(queries[..., NOPE:], position[:, None]).astype(jnp.bfloat16)
    up_table = latent_up.reshape(LATENT, head_local, NOPE + VHEAD)
    query_latent = jnp.einsum(
        "thn,lhn->thl",
        queries[..., :NOPE],
        up_table[..., :NOPE].astype(jnp.float32),
        precision=HIGHEST,
    ).astype(jnp.bfloat16)
    pages_local = latent_pool.shape[0]
    pool_total = pages_local * dp_count
    flat_pages = page_table.reshape(-1)
    flat_owner = jnp.repeat(jnp.arange(requests, dtype=jnp.int32), page_table.shape[1])
    target = jnp.where(flat_pages >= 0, flat_pages, pool_total)
    owner_all = jnp.full((pool_total,), -1, jnp.int32).at[target].set(flat_owner, mode="drop")
    page_owner = lax.dynamic_slice_in_dim(owner_all, dp_index * pages_local, pages_local)
    page_used = page_owner >= 0
    owner_safe = jnp.maximum(page_owner, 0)
    page_latent = latent_pool[..., :LATENT]
    page_rope = latent_pool[..., LATENT:]
    scores = jnp.einsum(
        "phl,pkl->phk", query_latent[owner_safe], page_latent, preferred_element_type=jnp.float32
    )
    scores = (
        scores
        + jnp.einsum(
            "phr,pkr->phk", query_rope[owner_safe], page_rope, preferred_element_type=jnp.float32
        )
    ) * score_scale
    raw_max = jnp.max(scores, axis=2)
    weights = jnp.exp(scores - raw_max[..., None])
    page_total = jnp.sum(weights, axis=2)
    page_mix = jnp.einsum(
        "phk,pkl->phl",
        weights.astype(jnp.bfloat16),
        page_latent,
        preferred_element_type=jnp.float32,
    )
    page_max = jnp.where(page_used[:, None], raw_max, MASKED_SCORE)
    member = page_owner[None, :] == jnp.arange(requests, dtype=jnp.int32)[:, None]
    req_max = jnp.max(jnp.where(member[:, :, None], page_max[None], MASKED_SCORE), axis=1)
    rescale = jnp.where(page_used[:, None], jnp.exp(page_max - req_max[owner_safe]), 0.0)
    member_float = member.astype(jnp.float32)
    req_total = jnp.dot(member_float, page_total * rescale, precision=HIGHEST)
    req_mix = jnp.einsum(
        "rp,phl->rhl", member_float, page_mix * rescale[..., None], precision=HIGHEST
    )
    packed = jnp.concatenate([req_mix, req_max[..., None], req_total[..., None]], axis=-1)
    gathered = lax.all_gather(packed, "dp", axis=0, tiled=False)
    gathered = lax.dynamic_slice_in_dim(gathered, group_start, group_rows, 1)
    each_max = gathered[..., LATENT]
    part_max = jnp.max(each_max, axis=0)
    each_weight = jnp.exp(each_max - part_max[None])
    part_total = jnp.sum(gathered[..., LATENT + 1] * each_weight, axis=0)
    part_mix = jnp.sum(gathered[..., :LATENT] * each_weight[..., None], axis=0)
    own_normed = lax.dynamic_slice_in_dim(normed, group_start, group_rows, 0)
    own_position = lax.dynamic_slice_in_dim(position, group_start, group_rows, 0)
    fresh_latent = jnp.dot(own_normed, latent_down, preferred_element_type=jnp.float32)
    new_latent = rms_plain(fresh_latent[:, :LATENT]).astype(jnp.bfloat16)
    new_rope = rotary(fresh_latent[:, LATENT:], own_position).astype(jnp.bfloat16)
    own_query = lax.dynamic_slice_in_dim(query_latent, group_start, group_rows, 0)
    own_rope_query = lax.dynamic_slice_in_dim(query_rope, group_start, group_rows, 0)
    own_score = jnp.einsum("thl,tl->th", own_query, new_latent, preferred_element_type=jnp.float32)
    own_score = (
        own_score
        + jnp.einsum("thr,tr->th", own_rope_query, new_rope, preferred_element_type=jnp.float32)
    ) * score_scale
    highest = jnp.maximum(part_max, own_score)
    kept_part = jnp.exp(part_max - highest)
    own_weight = jnp.exp(own_score - highest)
    denominator = part_total * kept_part + own_weight
    numerator = (
        part_mix * kept_part[..., None]
        + own_weight[..., None] * new_latent.astype(jnp.float32)[:, None, :]
    )
    attended = (numerator / denominator[..., None]).astype(jnp.bfloat16)
    heads_out = jnp.einsum(
        "thl,lhv->thv", attended, up_table[..., NOPE:], preferred_element_type=jnp.float32
    )
    heads_out = heads_out.astype(jnp.bfloat16).reshape(group_rows, head_local * VHEAD)
    partial_value = jnp.dot(heads_out, out_weight, preferred_element_type=jnp.float32)
    partial_value, spread = lax.optimization_barrier((partial_value, spread))
    attn_group = jnp.sum(lax.all_gather(partial_value, "expert", axis=0, tiled=False), axis=0)
    group_hidden = lax.dynamic_slice_in_dim(everyone, group_start, group_rows, 0)
    group_residual = group_hidden.astype(jnp.float32) + attn_group
    residual = lax.dynamic_slice_in_dim(group_residual, ex_index * req_local, req_local, 0)
    normed_group = rms_norm(group_residual, ffn_gain).astype(jnp.bfloat16)
    slots_local = expert_gate_up.shape[0]
    ff_width = expert_gate_up.shape[2]
    col_width = expert_gate_up.shape[3]
    outgoing = migrate_route(spread, plan, expert_gate_up, expert_down)
    normed_group, outgoing = lax.optimization_barrier((normed_group, outgoing))
    every_row = lax.all_gather(normed_group, "dp", axis=0, tiled=True)
    unit = (every_row[0, 0].astype(jnp.float32) * 0.0 + 1.0).astype(expert_gate_up.dtype)
    base_gate_up = expert_gate_up * unit
    base_down = expert_down * unit
    arrived = deliver(outgoing)
    my_columns = lax.dynamic_slice_in_dim(every_row, dp_index * col_width, col_width, 1)
    by_group = my_columns.reshape(dp_count, ex_count, req_local, col_width).transpose(1, 0, 2, 3)
    ffn_rows = by_group.reshape(requests, col_width)
    column_rows = lax.dynamic_index_in_dim(by_group, ex_index, 0, keepdims=False).reshape(
        dp_count * req_local, col_width
    )
    top_count = expert_ids.shape[1]
    experts_count = EXP_DEV * ex_count
    ids_order = (
        expert_ids.reshape(dp_count, ex_count, req_local, top_count)
        .transpose(1, 0, 2, 3)
        .reshape(requests, top_count)
    )
    gates_order = (
        expert_gates.reshape(dp_count, ex_count, req_local, top_count)
        .transpose(1, 0, 2, 3)
        .reshape(requests, top_count)
    )
    old_flat = old_place.reshape(-1)
    holds_map = old_flat[None, :] == jnp.arange(experts_count, dtype=jnp.int32)[:, None]
    holder = jnp.argmax(holds_map, axis=1)
    slot_of = holder[ids_order.reshape(-1)]
    capacity = 2 * requests * top_count // experts_count
    local_slot = slot_of - ex_index * slots_local
    slot_hot = local_slot[:, None] == jnp.arange(slots_local, dtype=jnp.int32)[None, :]
    slot_rank = jnp.cumsum(slot_hot.astype(jnp.int32), axis=0) - 1
    position_in = jnp.where(slot_hot, slot_rank, capacity)
    route_hot = (
        position_in[:, :, None] == jnp.arange(capacity, dtype=jnp.int32)[None, None, :]
    ).astype(jnp.float32)
    route_hot = route_hot.reshape(requests, top_count, slots_local, capacity)
    dispatch = jnp.sum(route_hot, axis=1).astype(jnp.bfloat16)
    combine = jnp.sum(route_hot * gates_order[:, :, None, None], axis=1)
    slot_inputs = jnp.einsum(
        "tsc,td->scd", dispatch, ffn_rows, preferred_element_type=jnp.float32
    ).astype(jnp.bfloat16)
    routed_part = jnp.einsum(
        "scd,sgfd->sgcf", slot_inputs, expert_gate_up, preferred_element_type=jnp.float32
    )
    shared_part = jnp.einsum(
        "td,gfd->gtf", column_rows, shared_gate_up, preferred_element_type=jnp.float32
    )
    routed_sum, shared_sum = sum_over(routed_part, "dp"), sum_over(shared_part, "dp")
    activated = (jax.nn.silu(routed_sum[:, 0]) * routed_sum[:, 1]).astype(jnp.bfloat16)
    slot_out = jnp.einsum(
        "scf,sfd->scd", activated, expert_down, preferred_element_type=jnp.float32
    )
    routed = jnp.einsum("tsc,scd->td", combine, slot_out, precision=HIGHEST)
    shared_act = (jax.nn.silu(shared_sum[0]) * shared_sum[1]).astype(jnp.bfloat16)
    shared_term = jnp.dot(shared_act, shared_down, preferred_element_type=jnp.float32)
    routed, arrived = lax.optimization_barrier((routed, arrived))
    shared_at = ex_index * dp_count * req_local
    own_block = lax.dynamic_slice_in_dim(routed, shared_at, dp_count * req_local, 0) + shared_term
    routed = lax.dynamic_update_slice_in_dim(routed, own_block, shared_at, 0)
    by_token = routed.reshape(ex_count, dp_count, req_local, col_width).transpose(1, 0, 2, 3)
    by_token = by_token.reshape(requests, col_width)
    received = lax.all_to_all(by_token, ("dp", "expert"), split_axis=0, concat_axis=0, tiled=True)
    moe_cols = jnp.sum(received.reshape(dp_count, ex_count, req_local, col_width), axis=1)
    moe_part = moe_cols.transpose(1, 0, 2).reshape(req_local, dp_count * col_width)
    layer_out = (residual + moe_part).astype(jnp.bfloat16)
    my_moved = plan[-1]
    chunk_rows = arrived.shape[2]
    slot_shape = (slots_local, 2, ex_count, chunk_rows, col_width)
    new_pair = arrived[:, :2].transpose(1, 0, 2, 3)[None]
    moved_gate_up = lax.dynamic_update_slice(
        base_gate_up.reshape(slot_shape), new_pair, (my_moved, 0, 0, 0, 0)
    ).reshape(base_gate_up.shape)
    new_single = arrived[:, 2][None]
    moved_down = lax.dynamic_update_slice(
        base_down.reshape(slots_local, ex_count, chunk_rows, col_width), new_single, (my_moved, 0, 0, 0)
    ).reshape(base_down.shape)
    return (layer_out, moved_gate_up, moved_down)


def solution(mesh):
    in_specs = (
        P(("dp", "expert"), None),
        P(),
        P("expert", None),
        P(),
        P(None, "expert"),
        P("expert", None),
        P("dp", None, None),
        P(),
        P(),
        P(),
        P(),
        P(),
        P(),
        P(),
        P("expert", None, None, "dp"),
        P("expert", None, "dp"),
        P(None, None, "dp"),
        P(None, "dp"),
    )
    out_specs = (P(("dp", "expert"), None), P("expert", None, None, "dp"), P("expert", None, "dp"))
    return jax.shard_map(local, mesh=mesh, in_specs=in_specs, out_specs=out_specs, check_vma=False)
```

```python
import math

import jax
import jax.numpy as jnp
from jax import lax
from jax.sharding import PartitionSpec as P

NOPE = 128
ROPE = 64
VHEAD = 128
LATENT = 512
EXP_DEV = 3
PAGE = 32


EPSILON = 1e-06
ROPE_BASE = 50000.0
MASKED_SCORE = -1e30
HIGHEST = lax.Precision.HIGHEST


def rms_plain(values):
    mean_square = jnp.mean(values * values, axis=-1, keepdims=True)
    return values * lax.rsqrt(mean_square + EPSILON)


def rms_norm(values, norm_gain):
    return rms_plain(values) * norm_gain


def rotary(values, position):
    half_width = values.shape[-1] // 2
    exponent = jnp.arange(half_width).astype(jnp.float32) * (2.0 / values.shape[-1])
    frequency = jnp.exp(-exponent * math.log(ROPE_BASE))
    angles = position[..., None] * frequency
    cosine = jnp.cos(angles)
    sine_part = jnp.sin(angles)
    first_half = values[..., :half_width]
    second = values[..., half_width:]
    return jnp.concatenate(
        [first_half * cosine - second * sine_part, second * cosine + first_half * sine_part],
        axis=-1,
    )


def pick_rows(table, rows):
    return jnp.stack([lax.dynamic_index_in_dim(table, rows[k], 0, False) for k in range(rows.shape[0])])


def pick_slots(gate_up, down, picks):
    return jnp.concatenate([pick_rows(gate_up, picks), pick_rows(down, picks)[:, None]], axis=1)


def spread_slots(chosen, ex_count):
    count, parts, ff_width, col_width = chosen.shape
    pieces = chosen.reshape(count, parts, ex_count, ff_width // ex_count, col_width)
    pieces = pieces.transpose(2, 0, 1, 3, 4)
    spread = lax.all_to_all(pieces, "expert", split_axis=0, concat_axis=0, tiled=True)
    return spread.reshape(ex_count * count, parts, ff_width // ex_count, col_width)


def scatter_sum(values, axis):
    count = lax.axis_size(axis)
    share = values.shape[0] // count
    gathered = lax.all_gather(values, axis, axis=0, tiled=False)
    mine = lax.dynamic_slice_in_dim(gathered, lax.axis_index(axis) * share, share, 1)
    return jnp.sum(mine, axis=0)


def sum_over(values, axis):
    return jnp.sum(lax.all_gather(values, axis, axis=0, tiled=False), axis=0)


def migrate_start(expert_gate_up, expert_down, old_place, new_place, ex_index):
    rows, slots_local = old_place.shape
    slots = rows * slots_local
    ex_count = rows
    ff_width = expert_gate_up.shape[2]
    local_ids = jnp.arange(slots_local, dtype=jnp.int32)
    slot_ids = jnp.arange(slots, dtype=jnp.int32)
    changed = old_place != new_place
    moved_slot = jnp.min(jnp.where(changed, local_ids[None, :], slots_local), axis=1)
    wanted = jnp.sum(jnp.where(local_ids[None, :] == moved_slot[:, None], new_place, 0), axis=1)
    hit = old_place.reshape(-1)[None, :] == wanted[:, None]
    first = jnp.min(jnp.where(hit, slot_ids[None, :], slots), axis=1)
    last = jnp.max(jnp.where(hit, slot_ids[None, :], -1), axis=1)
    both = jnp.stack([first, last])
    needed_both = jnp.any(both[:, :, None] == slot_ids[None, None, :], axis=1)
    needed_both = needed_both.reshape(2, rows, slots_local)
    loads = jnp.max(jnp.sum(needed_both.astype(jnp.int32), axis=2), axis=1)
    use_last = loads[1] < loads[0]
    source = jnp.where(use_last, last, first)
    needed = jnp.where(use_last, needed_both[1], needed_both[0]).astype(jnp.int32)
    load = jnp.min(loads)
    before = local_ids[None, None, :] <= local_ids[None, :, None]
    rank = jnp.sum(jnp.where(before, needed[:, None, :], 0), axis=2) - 1
    my_needed = lax.dynamic_index_in_dim(needed, ex_index, 0, False) > 0
    my_rank = lax.dynamic_index_in_dim(rank, ex_index, 0, False)
    at_rank = my_needed[None, :] & (my_rank[None, :] == local_ids[:, None])
    my_picks = jnp.sum(jnp.where(at_rank, local_ids[None, :], 0), axis=1)
    src_dev = source // slots_local
    src_rank = jnp.sum(jnp.where(source[:, None] == slot_ids[None, :], rank.reshape(-1)[None, :], 0), axis=1)
    fast = min(2, slots_local)
    chosen = pick_slots(expert_gate_up, expert_down, my_picks[:fast])
    return chosen, (my_picks, src_dev, src_rank, load, lax.dynamic_index_in_dim(moved_slot, ex_index, 0, False))


def migrate_route(spread, plan, expert_gate_up, expert_down):
    my_picks, src_dev, src_rank, load, my_moved = plan
    ex_count = src_dev.shape[0]
    slots_local = expert_gate_up.shape[0]
    fast = spread.shape[0] // ex_count
    out_a = jnp.take(spread, src_dev * fast + jnp.minimum(src_rank, fast - 1), axis=0, mode="clip")
    if slots_local > fast:
        rest = slots_local - fast

        def extra():
            spread_b = spread_slots(pick_slots(expert_gate_up, expert_down, my_picks[fast:]), ex_count)
            out_b = jnp.take(spread_b, src_dev * rest + jnp.clip(src_rank - fast, 0, rest - 1), axis=0, mode="clip")
            return jnp.where((src_rank < fast)[:, None, None, None], out_a, out_b)

        out_a = lax.cond(load > fast, extra, lambda: out_a)
    return out_a


def deliver(outgoing):
    return lax.all_to_all(outgoing, "expert", split_axis=0, concat_axis=0, tiled=True)


def local(
    hidden,
    attn_gain,
    query_weight,
    latent_down,
    latent_up,
    out_weight,
    latent_pool,
    page_table,
    page_counts,
    ffn_gain,
    expert_ids,
    expert_gates,
    old_place,
    new_place,
    expert_gate_up,
    expert_down,
    shared_gate_up,
    shared_down,
):
    dp_count = lax.axis_size("dp")
    ex_count = lax.axis_size("expert")
    dp_index = lax.axis_index("dp")
    ex_index = lax.axis_index("expert")
    req_local = hidden.shape[0]
    group_rows = req_local * ex_count
    requests = page_counts.shape[0]
    head_local = query_weight.shape[0] // (NOPE + ROPE)
    score_scale = (NOPE + ROPE) ** (-0.5)
    group_start = dp_index * group_rows
    chosen, plan = migrate_start(expert_gate_up, expert_down, old_place, new_place, ex_index)
    copies = jnp.broadcast_to(hidden[None], (ex_count,) + hidden.shape)
    by_expert = lax.all_to_all(copies, "expert", split_axis=0, concat_axis=0, tiled=True)
    by_expert = by_expert.reshape(ex_count * req_local, hidden.shape[1])
    by_expert, chosen = lax.optimization_barrier((by_expert, chosen))
    spread = spread_slots(chosen, ex_count)
    everyone = lax.all_gather(by_expert, "dp", axis=0, tiled=True)
    normed = rms_norm(everyone.astype(jnp.float32), attn_gain).astype(jnp.bfloat16)
    queries = jnp.einsum(
        "td,qd->tq", normed, query_weight, preferred_element_type=jnp.float32
    ).reshape(requests, head_local, NOPE + ROPE)
    position = (page_counts * PAGE).astype(jnp.float32)
    query_rope = rotary(queries[..., NOPE:], position[:, None]).astype(jnp.bfloat16)
    up_table = latent_up.reshape(LATENT, head_local, NOPE + VHEAD)
    query_latent = jnp.einsum(
        "thn,lhn->thl",
        queries[..., :NOPE],
        up_table[..., :NOPE].astype(jnp.float32),
        precision=HIGHEST,
    ).astype(jnp.bfloat16)
    pages_local = latent_pool.shape[0]
    pool_total = pages_local * dp_count
    flat_pages = page_table.reshape(-1)
    flat_owner = jnp.repeat(jnp.arange(requests, dtype=jnp.int32), page_table.shape[1])
    target = jnp.where(flat_pages >= 0, flat_pages, pool_total)
    owner_all = jnp.full((pool_total,), -1, jnp.int32).at[target].set(flat_owner, mode="drop")
    page_owner = lax.dynamic_slice_in_dim(owner_all, dp_index * pages_local, pages_local)
    page_used = page_owner >= 0
    owner_safe = jnp.maximum(page_owner, 0)
    page_latent = latent_pool[..., :LATENT]
    page_rope = latent_pool[..., LATENT:]
    scores = jnp.einsum(
        "phl,pkl->phk", query_latent[owner_safe], page_latent, preferred_element_type=jnp.float32
    )
    scores = (
        scores
        + jnp.einsum(
            "phr,pkr->phk", query_rope[owner_safe], page_rope, preferred_element_type=jnp.float32
        )
    ) * score_scale
    raw_max = jnp.max(scores, axis=2)
    weights = jnp.exp(scores - raw_max[..., None])
    page_total = jnp.sum(weights, axis=2)
    page_mix = jnp.einsum(
        "phk,pkl->phl",
        weights.astype(jnp.bfloat16),
        page_latent,
        preferred_element_type=jnp.float32,
    )
    page_max = jnp.where(page_used[:, None], raw_max, MASKED_SCORE)
    member = page_owner[None, :] == jnp.arange(requests, dtype=jnp.int32)[:, None]
    req_max = jnp.max(jnp.where(member[:, :, None], page_max[None], MASKED_SCORE), axis=1)
    rescale = jnp.where(page_used[:, None], jnp.exp(page_max - req_max[owner_safe]), 0.0)
    member_float = member.astype(jnp.float32)
    req_total = jnp.dot(member_float, page_total * rescale, precision=HIGHEST)
    req_mix = jnp.einsum(
        "rp,phl->rhl", member_float, page_mix * rescale[..., None], precision=HIGHEST
    )
    packed = jnp.concatenate([req_mix, req_max[..., None], req_total[..., None]], axis=-1)
    gathered = lax.all_gather(packed, "dp", axis=0, tiled=False)
    gathered = lax.dynamic_slice_in_dim(gathered, group_start, group_rows, 1)
    each_max = gathered[..., LATENT]
    part_max = jnp.max(each_max, axis=0)
    each_weight = jnp.exp(each_max - part_max[None])
    part_total = jnp.sum(gathered[..., LATENT + 1] * each_weight, axis=0)
    part_mix = jnp.sum(gathered[..., :LATENT] * each_weight[..., None], axis=0)
    own_normed = lax.dynamic_slice_in_dim(normed, group_start, group_rows, 0)
    own_position = lax.dynamic_slice_in_dim(position, group_start, group_rows, 0)
    fresh_latent = jnp.dot(own_normed, latent_down, preferred_element_type=jnp.float32)
    new_latent = rms_plain(fresh_latent[:, :LATENT]).astype(jnp.bfloat16)
    new_rope = rotary(fresh_latent[:, LATENT:], own_position).astype(jnp.bfloat16)
    own_query = lax.dynamic_slice_in_dim(query_latent, group_start, group_rows, 0)
    own_rope_query = lax.dynamic_slice_in_dim(query_rope, group_start, group_rows, 0)
    own_score = jnp.einsum("thl,tl->th", own_query, new_latent, preferred_element_type=jnp.float32)
    own_score = (
        own_score
        + jnp.einsum("thr,tr->th", own_rope_query, new_rope, preferred_element_type=jnp.float32)
    ) * score_scale
    highest = jnp.maximum(part_max, own_score)
    kept_part = jnp.exp(part_max - highest)
    own_weight = jnp.exp(own_score - highest)
    denominator = part_total * kept_part + own_weight
    numerator = (
        part_mix * kept_part[..., None]
        + own_weight[..., None] * new_latent.astype(jnp.float32)[:, None, :]
    )
    attended = (numerator / denominator[..., None]).astype(jnp.bfloat16)
    heads_out = jnp.einsum(
        "thl,lhv->thv", attended, up_table[..., NOPE:], preferred_element_type=jnp.float32
    )
    heads_out = heads_out.astype(jnp.bfloat16).reshape(group_rows, head_local * VHEAD)
    partial_value = jnp.dot(heads_out, out_weight, preferred_element_type=jnp.float32)
    partial_value, spread = lax.optimization_barrier((partial_value, spread))
    attn_group = jnp.sum(lax.all_gather(partial_value, "expert", axis=0, tiled=False), axis=0)
    group_hidden = lax.dynamic_slice_in_dim(everyone, group_start, group_rows, 0)
    group_residual = group_hidden.astype(jnp.float32) + attn_group
    residual = lax.dynamic_slice_in_dim(group_residual, ex_index * req_local, req_local, 0)
    normed_group = rms_norm(group_residual, ffn_gain).astype(jnp.bfloat16)
    slots_local = expert_gate_up.shape[0]
    ff_width = expert_gate_up.shape[2]
    col_width = expert_gate_up.shape[3]
    outgoing = migrate_route(spread, plan, expert_gate_up, expert_down)
    normed_group, outgoing = lax.optimization_barrier((normed_group, outgoing))
    every_row = lax.all_gather(normed_group, "dp", axis=0, tiled=True)
    unit = (every_row[0, 0].astype(jnp.float32) * 0.0 + 1.0).astype(expert_gate_up.dtype)
    base_gate_up = expert_gate_up * unit
    base_down = expert_down * unit
    arrived = deliver(outgoing)
    my_columns = lax.dynamic_slice_in_dim(every_row, dp_index * col_width, col_width, 1)
    by_group = my_columns.reshape(dp_count, ex_count, req_local, col_width).transpose(1, 0, 2, 3)
    ffn_rows = by_group.reshape(requests, col_width)
    column_rows = lax.dynamic_index_in_dim(by_group, ex_index, 0, keepdims=False).reshape(
        dp_count * req_local, col_width
    )
    top_count = expert_ids.shape[1]
    experts_count = EXP_DEV * ex_count
    ids_order = (
        expert_ids.reshape(dp_count, ex_count, req_local, top_count)
        .transpose(1, 0, 2, 3)
        .reshape(requests, top_count)
    )
    gates_order = (
        expert_gates.reshape(dp_count, ex_count, req_local, top_count)
        .transpose(1, 0, 2, 3)
        .reshape(requests, top_count)
    )
    old_flat = old_place.reshape(-1)
    holds_map = old_flat[None, :] == jnp.arange(experts_count, dtype=jnp.int32)[:, None]
    holder = jnp.argmax(holds_map, axis=1)
    slot_of = holder[ids_order.reshape(-1)]
    capacity = 2 * requests * top_count // experts_count
    local_slot = slot_of - ex_index * slots_local
    slot_hot = local_slot[:, None] == jnp.arange(slots_local, dtype=jnp.int32)[None, :]
    slot_rank = jnp.cumsum(slot_hot.astype(jnp.int32), axis=0) - 1
    position_in = jnp.where(slot_hot, slot_rank, capacity)
    route_hot = (
        position_in[:, :, None] == jnp.arange(capacity, dtype=jnp.int32)[None, None, :]
    ).astype(jnp.float32)
    route_hot = route_hot.reshape(requests, top_count, slots_local, capacity)
    dispatch = jnp.sum(route_hot, axis=1).astype(jnp.bfloat16)
    combine = jnp.sum(route_hot * gates_order[:, :, None, None], axis=1)
    slot_inputs = jnp.einsum(
        "tsc,td->scd", dispatch, ffn_rows, preferred_element_type=jnp.float32
    ).astype(jnp.bfloat16)
    routed_part = jnp.einsum(
        "scd,sgfd->sgcf", slot_inputs, expert_gate_up, preferred_element_type=jnp.float32
    )
    shared_part = jnp.einsum(
        "td,gfd->gtf", column_rows, shared_gate_up, preferred_element_type=jnp.float32
    )
    routed_sum, shared_sum = sum_over(routed_part, "dp"), sum_over(shared_part, "dp")
    activated = (jax.nn.silu(routed_sum[:, 0]) * routed_sum[:, 1]).astype(jnp.bfloat16)
    slot_out = jnp.einsum(
        "scf,sfd->scd", activated, expert_down, preferred_element_type=jnp.float32
    )
    combine_tok = combine.reshape((ex_count, dp_count, req_local) + combine.shape[1:])
    combine_tok = combine_tok.transpose(1, 0, 2, 3, 4).reshape(combine.shape)
    routed = jnp.einsum("tsc,scd->td", combine_tok, slot_out, precision=HIGHEST)
    shared_act = (jax.nn.silu(shared_sum[0]) * shared_sum[1]).astype(jnp.bfloat16)
    shared_term = jnp.dot(shared_act, shared_down, preferred_element_type=jnp.float32)
    routed, arrived = lax.optimization_barrier((routed, arrived))
    token_ids = jnp.arange(requests, dtype=jnp.int32)
    token_ex = (token_ids // req_local) % ex_count
    token_slot = (token_ids // (req_local * ex_count)) * req_local + token_ids % req_local
    owns = (token_ex == ex_index)[:, None] & (
        token_slot[:, None] == jnp.arange(dp_count * req_local, dtype=jnp.int32)[None, :]
    )
    by_token = routed + jnp.dot(owns.astype(jnp.float32), shared_term, precision=HIGHEST)
    received = lax.all_to_all(by_token, ("dp", "expert"), split_axis=0, concat_axis=0, tiled=True)
    moe_cols = jnp.sum(received.reshape(dp_count, ex_count, req_local, col_width), axis=1)
    moe_part = moe_cols.transpose(1, 0, 2).reshape(req_local, dp_count * col_width)
    layer_out = (residual + moe_part).astype(jnp.bfloat16)
    my_moved = plan[-1]
    chunk_rows = arrived.shape[2]
    slot_shape = (slots_local, 2, ex_count, chunk_rows, col_width)
    new_pair = arrived[:, :2].transpose(1, 0, 2, 3)[None]
    moved_gate_up = lax.dynamic_update_slice(
        base_gate_up.reshape(slot_shape), new_pair, (my_moved, 0, 0, 0, 0)
    ).reshape(base_gate_up.shape)
    new_single = arrived[:, 2][None]
    moved_down = lax.dynamic_update_slice(
        base_down.reshape(slots_local, ex_count, chunk_rows, col_width), new_single, (my_moved, 0, 0, 0)
    ).reshape(base_down.shape)
    return (layer_out, moved_gate_up, moved_down)


def solution(mesh):
    in_specs = (
        P(("dp", "expert"), None),
        P(),
        P("expert", None),
        P(),
        P(None, "expert"),
        P("expert", None),
        P("dp", None, None),
        P(),
        P(),
        P(),
        P(),
        P(),
        P(),
        P(),
        P("expert", None, None, "dp"),
        P("expert", None, "dp"),
        P(None, None, "dp"),
        P(None, "dp"),
    )
    out_specs = (P(("dp", "expert"), None), P("expert", None, None, "dp"), P("expert", None, "dp"))
    return jax.shard_map(local, mesh=mesh, in_specs=in_specs, out_specs=out_specs, check_vma=False)
```
